32 devices in a mesh: dp: 2 (over x), ctx: 16 (over z, y, core).
Axes of the slice: x: 2, y: 2, z: 4, core: 2. Of those that a mesh axis runs over, the one named last changes fastest.
Arguments:
- token_values: bfloat16 [2, 2048, 2560], P('dp', 'ctx'), may hold values from -0.3125 to 0.3125
- cotangent: bfloat16 [2, 2048, 2560], P('dp', 'ctx'), may hold values from -0.5 to 0.5
- write_coeffs: bfloat16 [2, 2048, 128], P('dp', 'ctx'), may hold values from -1.5 to 1.5
- read_coeffs: bfloat16 [2, 2048, 128], P('dp', 'ctx'), may hold values from -1.5 to 1.5
- decay_codes: int32 [2, 2048, 40], P('dp', 'ctx'), may hold values from 0 to 3276, as said below
- skip_gain: float32 [40], replicated, may hold values from 0.5 to 2
Outputs:
- grad_values: bfloat16 [2, 2048, 2560], P('dp', 'ctx')
- grad_write: bfloat16 [2, 2048, 128], P('dp', 'ctx')
- grad_read: bfloat16 [2, 2048, 128], P('dp', 'ctx')
- grad_skip: float32 [40], replicated
The draws below stay inside these ranges and needn't reach their ends.
Inputs may be any that keep to these rules, and one draw needn't show every extreme that they name: `decay_codes`: one code per sequence, token and head; larger codes mean faster forgetting.
All inputs are finite; a program needn't handle non-finite values.
Results may differ from the reference program's by a relative error of at most 0.0059.
Values sent between devices are 32-bit elements; how exact they have to be, the bound alone decides.
No kernel may reach another device: no remote copies, remote signals or barrier semaphores. Data moves between devices by JAX's collectives and lax.ppermute only.
A program may use at most 128 MiB of HBM per device.

```python
import jax
import jax.numpy as jnp
from jax import lax

HEAD_TOTAL = 40
P_SIZE = 64
N = 128
SPAN = 128
SEQUENCE_COUNT = 2
SEQUENCE_TOKENS = 2048


def draw_decay_codes(key, part):
    random_keys = jax.random.split(jax.random.fold_in(key, 17), 5)
    block_count = SEQUENCE_TOKENS // SPAN
    fast_heads = jax.random.randint(random_keys[0], (SEQUENCE_COUNT, 1, HEAD_TOTAL), 0, 2)
    levels = jax.random.randint(random_keys[1], (SEQUENCE_COUNT, block_count, 1, HEAD_TOTAL), 0, 3)
    levels = jnp.broadcast_to(levels, (SEQUENCE_COUNT, block_count, SPAN, HEAD_TOTAL)).reshape(SEQUENCE_COUNT, SEQUENCE_TOKENS, HEAD_TOTAL)
    slow_codes = jax.random.randint(random_keys[2], (SEQUENCE_COUNT, SEQUENCE_TOKENS, HEAD_TOTAL), 0, 1 + 2 * levels)
    fast_codes = jax.random.randint(random_keys[3], (SEQUENCE_COUNT, SEQUENCE_TOKENS, HEAD_TOTAL), 0, (1 + levels) * (SEQUENCE_TOKENS // 10))
    codes = jnp.where(fast_heads == 1, fast_codes, slow_codes)
    release_position = jax.random.randint(random_keys[4], (SEQUENCE_COUNT, 1, 3, HEAD_TOTAL), 0, SEQUENCE_TOKENS)
    token_positions = jnp.arange(SEQUENCE_TOKENS, dtype=jnp.int32)[None, :, None, None]
    selected_flags = jnp.any(token_positions == release_position, axis=2)
    codes = jnp.where(selected_flags, 8 * SEQUENCE_TOKENS // 5, codes)
    return codes.astype(jnp.int32)


def shard_levels(rng, shape, cuts, least, top_value):
    def one(axis_at, shards_of):
        draws = jax.random.uniform(jax.random.fold_in(jax.random.fold_in(rng, 6), axis_at), (shards_of,), jnp.float32, least / len(cuts), top_value / len(cuts))
        return jnp.repeat(jnp.exp(draws), shape[axis_at] // shards_of).reshape((-1,) + (1,) * (len(shape) - axis_at - 1))

    gain = one(*cuts[0])
    for cut in cuts[1:]:
        gain = gain * one(*cut)
    return gain


def noise(own_key, dims, scale, limit, shards=(), held_as=jnp.bfloat16):
    level = shard_levels(own_key, dims, shards, -0.22, 0.18) if shards else 1.0
    result = jax.random.normal(own_key, dims, jnp.float32) * scale * level
    return jnp.minimum(jnp.maximum(result, -limit), limit).astype(held_as)


def setup_inputs(seed: int = 0) -> dict:
    key_list = jax.random.split(jax.random.key(seed), 7)
    return {
        "token_values": noise(key_list[0], (SEQUENCE_COUNT, SEQUENCE_TOKENS, HEAD_TOTAL * P_SIZE), 0.055, 0.3125, ((0, 2), (1, 16))),
        "cotangent": noise(key_list[1], (SEQUENCE_COUNT, SEQUENCE_TOKENS, HEAD_TOTAL * P_SIZE), 0.09, 0.5, ((0, 2), (1, 16))),
        "write_coeffs": noise(key_list[2], (SEQUENCE_COUNT, SEQUENCE_TOKENS, N), 0.25, 1.5, ((0, 2), (1, 16))),
        "read_coeffs": noise(key_list[3], (SEQUENCE_COUNT, SEQUENCE_TOKENS, N), 0.25, 1.5, ((0, 2), (1, 16))),
        "decay_codes": draw_decay_codes(jax.random.fold_in(key_list[6], 71), 0),
        "skip_gain": jnp.clip(jax.random.uniform(key_list[5], (HEAD_TOTAL,), jnp.float32, 0.5, 2.0), 0.5, 2.0),
    }


def kept_bf16(array):
    return lax.optimization_barrier(array.astype(jnp.bfloat16)).astype(jnp.float32)


def block_states(values, cotan, write_map, read_map, codes, factor):
    token_count = values.shape[0]
    head_count = codes.shape[1]
    head_width = values.shape[1] // head_count
    log_decay = -codes.astype(jnp.float32) * factor
    within = jnp.cumsum(log_decay, axis=0)
    totals = within[-1]
    vals_three = values.reshape(token_count, head_count, head_width).astype(jnp.float32)
    cot_three = cotan.reshape(token_count, head_count, head_width).astype(jnp.float32)
    decayed_vals = kept_bf16(vals_three * jnp.exp(totals - within)[:, :, None])
    decayed_cot = kept_bf16(cot_three * jnp.exp(within)[:, :, None])
    fwd_state = jnp.einsum("jn,jhp->hnp", write_map.astype(jnp.float32), decayed_vals, precision=lax.Precision.HIGHEST)
    adj_state = jnp.einsum("in,ihp->hnp", read_map.astype(jnp.float32), decayed_cot, precision=lax.Precision.HIGHEST)
    return within, totals, decayed_vals, decayed_cot, fwd_state, adj_state


def block_grads(values, cotan, write_map, read_map, within, totals, decayed_vals, decayed_cot, carried_state, carried_adjoint, skip_gain):
    token_count = values.shape[0]
    head_count = skip_gain.shape[0]
    head_width = values.shape[1] // head_count
    highest = lax.Precision.HIGHEST
    vals_three = values.reshape(token_count, head_count, head_width).astype(jnp.float32)
    cot_three = cotan.reshape(token_count, head_count, head_width).astype(jnp.float32)
    write_f = write_map.astype(jnp.float32)
    read_f = read_map.astype(jnp.float32)
    rows = jnp.arange(token_count)
    causal = (rows[:, None] >= rows[None, :])[None]
    lead = within.T
    spread = lead[:, :, None] - lead[:, None, :]
    decay_matrix = jnp.where(causal, jnp.exp(jnp.where(causal, spread, 0.0)), 0.0)
    products = jnp.einsum("ihp,jhp->hij", cot_three, vals_three, precision=highest)
    read_weights = kept_bf16(products * decay_matrix)
    gram = jnp.dot(read_map, write_map.T, preferred_element_type=jnp.float32)
    value_weights = kept_bf16(gram[None] * decay_matrix)
    state_rounded = kept_bf16(carried_state)
    adjoint_rounded = kept_bf16(carried_adjoint)
    grad_read = jnp.einsum("hij,jn->in", read_weights, write_f, precision=highest) + jnp.einsum("ihp,hnp->in", decayed_cot, state_rounded, precision=highest)
    grad_write = jnp.einsum("hij,in->jn", read_weights, read_f, precision=highest) + jnp.einsum("jhp,hnp->jn", decayed_vals, adjoint_rounded, precision=highest)
    carried_term = jnp.einsum("jn,hnp->jhp", write_f, adjoint_rounded, precision=highest)
    grad_values = jnp.einsum("hij,ihp->jhp", value_weights, cot_three, precision=highest) + jnp.exp(totals - within)[:, :, None] * carried_term + skip_gain[None, :, None] * cot_three
    skip_part = jnp.einsum("ihp,ihp->h", cot_three, vals_three, precision=highest)
    return (grad_values.reshape(token_count, head_count * head_width).astype(jnp.bfloat16), grad_write.astype(jnp.bfloat16), grad_read.astype(jnp.bfloat16), skip_part)


def reference(token_values, cotangent, write_coeffs, read_coeffs, decay_codes, skip_gain):
    factor = 0.25 / SEQUENCE_TOKENS
    block_count = SEQUENCE_TOKENS // SPAN

    def carry_step(carry, item):
        gains, state = item
        return jnp.exp(gains)[:, None, None] * carry + state, carry

    def one_sequence(seq_args):
        values, cotan, write_map, read_map, codes = seq_args
        shaped = (values.reshape(block_count, SPAN, -1), cotan.reshape(block_count, SPAN, -1), write_map.reshape(block_count, SPAN, -1), read_map.reshape(block_count, SPAN, -1), codes.reshape(block_count, SPAN, -1))
        within, totals, decayed_vals, decayed_cot, fwd_state, adj_state = lax.map(lambda blk: block_states(blk[0], blk[1], blk[2], blk[3], blk[4], factor), shaped)
        empty = jnp.zeros(fwd_state.shape[1:], jnp.float32)
        final_state, carried_state = lax.scan(carry_step, empty, (totals, fwd_state))
        final_adjoint, carried_adjoint = lax.scan(carry_step, empty, (totals, adj_state), reverse=True)
        pieces = (shaped[0], shaped[1], shaped[2], shaped[3], within, totals, decayed_vals, decayed_cot, carried_state, carried_adjoint)
        grad_vals, grad_wr, grad_rd, skip_parts = lax.map(lambda blk: block_grads(blk[0], blk[1], blk[2], blk[3], blk[4], blk[5], blk[6], blk[7], blk[8], blk[9], skip_gain), pieces)
        return (grad_vals.reshape(SEQUENCE_TOKENS, -1), grad_wr.reshape(SEQUENCE_TOKENS, -1), grad_rd.reshape(SEQUENCE_TOKENS, -1), jnp.sum(skip_parts, axis=0))

    results = lax.map(one_sequence, (token_values, cotangent, write_coeffs, read_coeffs, decay_codes))
    return (results[0], results[1], results[2], jnp.sum(results[3], axis=0))
```

```python
import functools

import jax
import jax.numpy as jnp
from jax import lax
from jax.sharding import PartitionSpec as P


def block_states(values, cotan, write_map, read_map, codes, factor):
    token_count = values.shape[0]
    head_count = codes.shape[1]
    head_width = values.shape[1] // head_count
    log_decay = -codes.astype(jnp.float32) * factor
    within = jnp.cumsum(log_decay, axis=0)
    totals = within[-1]
    vals_three = values.reshape(token_count, head_count, head_width)
    cot_three = cotan.reshape(token_count, head_count, head_width)
    decayed_vals = (vals_three * jnp.exp(totals - within)[:, :, None]).astype(jnp.bfloat16)
    decayed_cot = (cot_three * jnp.exp(within)[:, :, None]).astype(jnp.bfloat16)
    fwd_state = jnp.einsum(
        "jn,jhp->hnp", write_map, decayed_vals, preferred_element_type=jnp.float32
    )
    adj_state = jnp.einsum("in,ihp->hnp", read_map, decayed_cot, preferred_element_type=jnp.float32)
    return (within, totals, decayed_vals, decayed_cot, fwd_state, adj_state)


def block_grads(
    values,
    cotan,
    write_map,
    read_map,
    within,
    totals,
    decayed_vals,
    decayed_cot,
    carried_state,
    carried_adjoint,
    skip_gain,
):
    token_count = values.shape[0]
    head_count = skip_gain.shape[0]
    head_width = values.shape[1] // head_count
    vals_three = values.reshape(token_count, head_count, head_width)
    cot_three = cotan.reshape(token_count, head_count, head_width)
    rows = jnp.arange(token_count)
    causal = (rows[:, None] >= rows[None, :])[None]
    lead = within.T
    spread = lead[:, :, None] - lead[:, None, :]
    decay_matrix = jnp.where(causal, jnp.exp(jnp.where(causal, spread, 0.0)), 0.0)
    products = jnp.einsum("ihp,jhp->hij", cot_three, vals_three, preferred_element_type=jnp.float32)
    read_weights = (products * decay_matrix).astype(jnp.bfloat16)
    gram = jnp.einsum("in,jn->ij", read_map, write_map, preferred_element_type=jnp.float32)
    value_weights = (gram[None] * decay_matrix).astype(jnp.bfloat16)
    state_rounded = carried_state.astype(jnp.bfloat16)
    adjoint_rounded = carried_adjoint.astype(jnp.bfloat16)
    grad_read = jnp.einsum(
        "hij,jn->in", read_weights, write_map, preferred_element_type=jnp.float32
    ) + jnp.einsum("ihp,hnp->in", decayed_cot, state_rounded, preferred_element_type=jnp.float32)
    grad_write = jnp.einsum(
        "hij,in->jn", read_weights, read_map, preferred_element_type=jnp.float32
    ) + jnp.einsum("jhp,hnp->jn", decayed_vals, adjoint_rounded, preferred_element_type=jnp.float32)
    carried_term = jnp.einsum(
        "jn,hnp->jhp", write_map, adjoint_rounded, preferred_element_type=jnp.float32
    )
    grad_values = (
        jnp.einsum("hij,ihp->jhp", value_weights, cot_three, preferred_element_type=jnp.float32)
        + jnp.exp(totals - within)[:, :, None] * carried_term
        + skip_gain[None, :, None] * cot_three
    )
    skip_part = jnp.einsum("ihp,ihp->h", cot_three, vals_three, preferred_element_type=jnp.float32)
    return (
        grad_values.reshape(token_count, head_count * head_width).astype(jnp.bfloat16),
        grad_write.astype(jnp.bfloat16),
        grad_read.astype(jnp.bfloat16),
        skip_part,
    )


def chain_pair(earlier, later):
    return (earlier[0] * later[0], later[0][..., None, None] * earlier[1] + later[1])


def pick_tree(flag, first_tree, second_tree):
    return jax.tree.map(
        lambda first_leaf, other_leaf: jnp.where(flag, first_leaf, other_leaf),
        first_tree,
        second_tree,
    )


def sweep_scan(gains, state, position, count, reverse):
    level_count = count.bit_length() - 1
    index = count - 1 - position if reverse else position

    def mapped(pairs):
        if reverse:
            return [(count - 1 - a, count - 1 - b) for a, b in pairs]
        return pairs

    total = (gains, state)
    lowers = []
    for level in range(level_count):
        span = 1 << level
        pairs = [(i, i + span) for i in range(count) if i % (2 * span) == span - 1]
        lower = lax.ppermute(total, "ctx", mapped(pairs))
        lowers.append(lower)
        if level < level_count - 1:
            receives = index % (2 * span) == 2 * span - 1
            total = pick_tree(receives, chain_pair(lower, total), total)
    prefix = jnp.zeros_like(state)
    for level in reversed(range(level_count)):
        span = 1 << level
        if level < level_count - 1:
            pairs = [(i, i - span) for i in range(count) if i % (2 * span) == 2 * span - 1]
            sent = lax.ppermute(prefix, "ctx", mapped(pairs))
            prefix = jnp.where(index % (2 * span) == span - 1, sent, prefix)
        lower_gain, lower_state = lowers[level]
        grown = lower_gain[..., None, None] * prefix + lower_state
        prefix = jnp.where(index % (2 * span) == 2 * span - 1, grown, prefix)
    return prefix


def local(token_values, cotangent, write_coeffs, read_coeffs, decay_codes, skip_gain):
    seq_len = token_values.shape[1] * lax.axis_size("ctx")
    factor = 0.25 / seq_len
    prepare = jax.vmap(functools.partial(block_states, factor=factor))
    within, totals, decayed_vals, decayed_cot, fwd_state, adj_state = prepare(
        token_values, cotangent, write_coeffs, read_coeffs, decay_codes
    )
    block_gains = jnp.exp(totals)
    position = lax.axis_index("ctx")
    count = lax.axis_size("ctx")
    carried_state = sweep_scan(block_gains, fwd_state, position, count, False)
    carried_adjoint = sweep_scan(block_gains, adj_state, position, count, True)
    finish = jax.vmap(block_grads, (0, 0, 0, 0, 0, 0, 0, 0, 0, 0, None))
    grad_values, grad_write, grad_read, skip_parts = finish(
        token_values,
        cotangent,
        write_coeffs,
        read_coeffs,
        within,
        totals,
        decayed_vals,
        decayed_cot,
        carried_state,
        carried_adjoint,
        skip_gain,
    )
    grad_skip = lax.psum(jnp.sum(skip_parts, axis=0), ("dp", "ctx"))
    return (grad_values, grad_write, grad_read, grad_skip)


def solution(mesh):
    in_specs = (
        P("dp", "ctx", None),
        P("dp", "ctx", None),
        P("dp", "ctx", None),
        P("dp", "ctx", None),
        P("dp", "ctx", None),
        P(),
    )
    out_specs = (P("dp", "ctx", None), P("dp", "ctx", None), P("dp", "ctx", None), P())
    return jax.shard_map(local, mesh=mesh, in_specs=in_specs, out_specs=out_specs, check_vma=False)
```

```python
import functools

import jax
import jax.numpy as jnp
from jax import lax
from jax.sharding import PartitionSpec as P


def spread_heads(per_head, width):
    return jnp.repeat(per_head, width, axis=-1)


def block_states(values, cotan, write_map, read_map, codes, factor):
    head_count = codes.shape[1]
    head_width = values.shape[1] // head_count
    log_decay = -codes.astype(jnp.float32) * factor
    within = jnp.cumsum(log_decay, axis=0)
    totals = within[-1]
    value_scale = spread_heads(jnp.exp(totals - within), head_width)
    cot_scale = spread_heads(jnp.exp(within), head_width)
    decayed_vals = (values.astype(jnp.float32) * value_scale).astype(jnp.bfloat16)
    decayed_cot = (cotan.astype(jnp.float32) * cot_scale).astype(jnp.bfloat16)
    fwd_state = jnp.einsum("jn,jq->nq", write_map, decayed_vals, preferred_element_type=jnp.float32)
    adj_state = jnp.einsum("in,iq->nq", read_map, decayed_cot, preferred_element_type=jnp.float32)
    skip_part = jnp.sum(
        (values.astype(jnp.float32) * cotan.astype(jnp.float32)).reshape(
            values.shape[0], head_count, head_width
        ),
        axis=(0, 2),
    )
    return within, totals, value_scale, decayed_vals, decayed_cot, fwd_state, adj_state, skip_part


def block_local_grads(values, cotan, write_map, read_map, within, skip_gain):
    token_count = values.shape[0]
    head_count = skip_gain.shape[0]
    head_width = values.shape[1] // head_count
    vals_three = values.reshape(token_count, head_count, head_width)
    cot_three = cotan.reshape(token_count, head_count, head_width)
    rows = jnp.arange(token_count)
    causal = (rows[:, None] >= rows[None, :])[None]
    lead = within.T
    spread = lead[:, :, None] - lead[:, None, :]
    decay_matrix = jnp.where(causal, jnp.exp(jnp.where(causal, spread, 0.0)), 0.0)
    products = jnp.einsum("ihp,jhp->hij", cot_three, vals_three, preferred_element_type=jnp.float32)
    read_weights = (products * decay_matrix).astype(jnp.bfloat16)
    gram = jnp.einsum("in,jn->ij", read_map, write_map, preferred_element_type=jnp.float32)
    value_weights = (gram[None] * decay_matrix).astype(jnp.bfloat16)
    grad_read = jnp.einsum("hij,jn->in", read_weights, write_map, preferred_element_type=jnp.float32)
    grad_write = jnp.einsum("hij,in->jn", read_weights, read_map, preferred_element_type=jnp.float32)
    grad_values = jnp.einsum(
        "hij,ihp->jhp", value_weights, cot_three, preferred_element_type=jnp.float32
    ) + skip_gain[None, :, None] * cot_three.astype(jnp.float32)
    return grad_values.reshape(token_count, head_count * head_width), grad_write, grad_read


def block_carried_grads(
    write_map, value_scale, decayed_vals, decayed_cot, carried_state, carried_adjoint, local_grads
):
    local_values, local_write, local_read = local_grads
    state_rounded = carried_state.astype(jnp.bfloat16)
    adjoint_rounded = carried_adjoint.astype(jnp.bfloat16)
    grad_read = local_read + jnp.einsum(
        "iq,nq->in", decayed_cot, state_rounded, preferred_element_type=jnp.float32
    )
    grad_write = local_write + jnp.einsum(
        "jq,nq->jn", decayed_vals, adjoint_rounded, preferred_element_type=jnp.float32
    )
    carried_term = jnp.einsum("jn,nq->jq", write_map, adjoint_rounded, preferred_element_type=jnp.float32)
    grad_values = local_values + value_scale * carried_term
    return (
        grad_values.astype(jnp.bfloat16),
        grad_write.astype(jnp.bfloat16),
        grad_read.astype(jnp.bfloat16),
    )


def sweep_scan(gains, state, position, count, reverse):
    head_width = state.shape[-1] // gains.shape[-1]
    level_count = count.bit_length() - 1
    index = count - 1 - position if reverse else position

    def mapped(pairs):
        if reverse:
            return [(count - 1 - a, count - 1 - b) for a, b in pairs]
        return pairs

    def grow(gain, earlier, later):
        return spread_heads(gain, head_width)[..., None, :] * earlier + later

    total_gain, total_state = gains, state
    lowers = []
    for level in range(level_count):
        span = 1 << level
        pairs = [(i, i + span) for i in range(count) if i % (2 * span) == span - 1]
        lower = lax.ppermute((total_gain, total_state), "ctx", mapped(pairs))
        lowers.append(lower)
        if level < level_count - 1:
            receives = index % (2 * span) == 2 * span - 1
            total_state = jnp.where(receives, grow(total_gain, lower[1], total_state), total_state)
            total_gain = jnp.where(receives, lower[0] * total_gain, total_gain)
    prefix = jnp.zeros_like(state)
    for level in reversed(range(level_count)):
        span = 1 << level
        if level < level_count - 1:
            pairs = [(i, i - span) for i in range(count) if i % (2 * span) == 2 * span - 1]
            sent = lax.ppermute(prefix, "ctx", mapped(pairs))
            prefix = jnp.where(index % (2 * span) == span - 1, sent, prefix)
        lower_gain, lower_state = lowers[level]
        prefix = jnp.where(
            index % (2 * span) == 2 * span - 1, grow(lower_gain, prefix, lower_state), prefix
        )
    return prefix


def local(token_values, cotangent, write_coeffs, read_coeffs, decay_codes, skip_gain):
    seq_len = token_values.shape[1] * lax.axis_size("ctx")
    factor = 0.25 / seq_len
    prepare = jax.vmap(functools.partial(block_states, factor=factor))
    within, totals, value_scale, decayed_vals, decayed_cot, fwd_state, adj_state, skip_parts = prepare(
        token_values, cotangent, write_coeffs, read_coeffs, decay_codes
    )
    grad_skip = lax.psum(jnp.sum(skip_parts, axis=0), ("dp", "ctx"))
    grad_skip, fwd_state, adj_state = lax.optimization_barrier((grad_skip, fwd_state, adj_state))
    block_gains = jnp.exp(totals)
    position = lax.axis_index("ctx")
    count = lax.axis_size("ctx")
    carried_state = sweep_scan(block_gains, fwd_state, position, count, False)
    carried_adjoint = sweep_scan(block_gains, adj_state, position, count, True)
    local_grads = jax.vmap(block_local_grads, (0, 0, 0, 0, 0, None))(
        token_values, cotangent, write_coeffs, read_coeffs, within, skip_gain
    )
    grad_values, grad_write, grad_read = jax.vmap(block_carried_grads)(
        write_coeffs, value_scale, decayed_vals, decayed_cot, carried_state, carried_adjoint, local_grads
    )
    return (grad_values, grad_write, grad_read, grad_skip)


def solution(mesh):
    in_specs = (
        P("dp", "ctx", None),
        P("dp", "ctx", None),
        P("dp", "ctx", None),
        P("dp", "ctx", None),
        P("dp", "ctx", None),
        P(),
    )
    out_specs = (P("dp", "ctx", None), P("dp", "ctx", None), P("dp", "ctx", None), P())
    return jax.shard_map(local, mesh=mesh, in_specs=in_specs, out_specs=out_specs, check_vma=False)
```

```python
import functools

import jax
import jax.numpy as jnp
from jax import lax
from jax.sharding import PartitionSpec as P


def spread_heads(per_head, width):
    return jnp.repeat(per_head, width, axis=-1)


def block_states(values, cotan, write_map, read_map, codes, factor):
    head_count = codes.shape[1]
    head_width = values.shape[1] // head_count
    log_decay = -codes.astype(jnp.float32) * factor
    within = jnp.cumsum(log_decay, axis=0)
    totals = within[-1]
    value_scale = spread_heads(jnp.exp(totals - within), head_width)
    cot_scale = spread_heads(jnp.exp(within), head_width)
    decayed_vals = (values.astype(jnp.float32) * value_scale).astype(jnp.bfloat16)
    decayed_cot = (cotan.astype(jnp.float32) * cot_scale).astype(jnp.bfloat16)
    fwd_state = jnp.einsum("jn,jq->nq", write_map, decayed_vals, preferred_element_type=jnp.float32)
    adj_state = jnp.einsum("in,iq->nq", read_map, decayed_cot, preferred_element_type=jnp.float32)
    skip_part = jnp.sum(
        (values.astype(jnp.float32) * cotan.astype(jnp.float32)).reshape(
            values.shape[0], head_count, head_width
        ),
        axis=(0, 2),
    )
    return within, totals, value_scale, decayed_vals, decayed_cot, fwd_state, adj_state, skip_part


def block_local_grads(values, cotan, write_map, read_map, within, skip_gain):
    token_count = values.shape[0]
    head_count = skip_gain.shape[0]
    head_width = values.shape[1] // head_count
    vals_three = values.reshape(token_count, head_count, head_width)
    cot_three = cotan.reshape(token_count, head_count, head_width)
    rows = jnp.arange(token_count)
    causal = (rows[:, None] >= rows[None, :])[None]
    lead = within.T
    spread = lead[:, :, None] - lead[:, None, :]
    decay_matrix = jnp.where(causal, jnp.exp(jnp.where(causal, spread, 0.0)), 0.0)
    products = jnp.einsum("ihp,jhp->hij", cot_three, vals_three, preferred_element_type=jnp.float32)
    read_weights = (products * decay_matrix).astype(jnp.bfloat16)
    gram = jnp.einsum("in,jn->ij", read_map, write_map, preferred_element_type=jnp.float32)
    value_weights = (gram[None] * decay_matrix).astype(jnp.bfloat16)
    grad_read = jnp.einsum("hij,jn->in", read_weights, write_map, preferred_element_type=jnp.float32)
    grad_write = jnp.einsum("hij,in->jn", read_weights, read_map, preferred_element_type=jnp.float32)
    grad_values = jnp.einsum(
        "hij,ihp->jhp", value_weights, cot_three, preferred_element_type=jnp.float32
    ) + skip_gain[None, :, None] * cot_three.astype(jnp.float32)
    return grad_values.reshape(token_count, head_count * head_width), grad_write, grad_read


def block_carried_grads(
    write_map, value_scale, decayed_vals, decayed_cot, carried_state, carried_adjoint, local_grads
):
    local_values, local_write, local_read = local_grads
    state_rounded = carried_state.astype(jnp.bfloat16)
    adjoint_rounded = carried_adjoint.astype(jnp.bfloat16)
    grad_read = local_read + jnp.einsum(
        "iq,nq->in", decayed_cot, state_rounded, preferred_element_type=jnp.float32
    )
    grad_write = local_write + jnp.einsum(
        "jq,nq->jn", decayed_vals, adjoint_rounded, preferred_element_type=jnp.float32
    )
    carried_term = jnp.einsum("jn,nq->jq", write_map, adjoint_rounded, preferred_element_type=jnp.float32)
    grad_values = local_values + value_scale * carried_term
    return (
        grad_values.astype(jnp.bfloat16),
        grad_write.astype(jnp.bfloat16),
        grad_read.astype(jnp.bfloat16),
    )


def xor_pairs(count, bit):
    return [(i, i ^ (1 << bit)) for i in range(count)]


def gather_totals(totals, skip_part, position, count):
    rows = jnp.arange(count)[:, None]
    table = jnp.concatenate([jnp.where(rows == position, totals[None, :], 0.0), skip_part[None, :]], 0)
    tables = [table]
    for bit in range(count.bit_length() - 1):
        table = table + lax.ppermute(table, "ctx", xor_pairs(count, bit))
        tables.append(table)
    return tables


def range_gain(table, count, low, high, reverse):
    rows = jnp.arange(count)
    virtual = count - 1 - rows if reverse else rows
    inside = (virtual >= low) & (virtual <= high)
    return jnp.exp(jnp.sum(jnp.where(inside[:, None], table[:count], 0.0), axis=0))


def sweep_scan(tables, state, position, count, reverse):
    head_width = state.shape[-1] // tables[0].shape[-1]
    level_count = count.bit_length() - 1
    index = count - 1 - position if reverse else position

    def mapped(pairs):
        if reverse:
            return [(count - 1 - a, count - 1 - b) for a, b in pairs]
        return pairs

    def spread(gain):
        return spread_heads(gain, head_width)[..., None, :]

    total = state
    lowers = []
    for level in range(level_count):
        span = 1 << level
        pairs = [(i, i + span) for i in range(count) if i % (2 * span) == span - 1]
        lower = lax.ppermute(total, "ctx", mapped(pairs))
        lowers.append(lower)
        if level < level_count - 1:
            upper_gain = range_gain(tables[level], count, index - span + 1, index, reverse)
            total = spread(upper_gain) * lower + total
    prefix = jnp.zeros_like(state)
    for level in reversed(range(level_count)):
        span = 1 << level
        if level < level_count - 1:
            pairs = [(i, i - span) for i in range(count) if i % (2 * span) == 2 * span - 1]
            prefix = prefix + lax.ppermute(prefix, "ctx", mapped(pairs))
        lower_gain = range_gain(tables[-1], count, index - 2 * span + 1, index - span, reverse)
        lower_gain = jnp.where(index % (2 * span) == 2 * span - 1, lower_gain, 1.0)
        prefix = spread(lower_gain) * prefix + lowers[level]
    return prefix


def local(token_values, cotangent, write_coeffs, read_coeffs, decay_codes, skip_gain):
    seq_len = token_values.shape[1] * lax.axis_size("ctx")
    factor = 0.25 / seq_len
    prepare = jax.vmap(functools.partial(block_states, factor=factor))
    within, totals, value_scale, decayed_vals, decayed_cot, fwd_state, adj_state, skip_parts = prepare(
        token_values, cotangent, write_coeffs, read_coeffs, decay_codes
    )
    position = lax.axis_index("ctx")
    count = lax.axis_size("ctx")
    tables = jax.vmap(gather_totals, (0, 0, None, None))(totals, skip_parts, position, count)
    grad_skip = jnp.sum(tables[-1][:, count], axis=0)
    for bit in range(lax.axis_size("dp").bit_length() - 1):
        grad_skip = grad_skip + lax.ppermute(grad_skip, "dp", xor_pairs(lax.axis_size("dp"), bit))
    scan = jax.vmap(sweep_scan, (0, 0, None, None, None))
    carried_state = scan(tables, fwd_state, position, count, False)
    carried_adjoint = scan(tables, adj_state, position, count, True)
    local_grads = jax.vmap(block_local_grads, (0, 0, 0, 0, 0, None))(
        token_values, cotangent, write_coeffs, read_coeffs, within, skip_gain
    )
    grad_values, grad_write, grad_read = jax.vmap(block_carried_grads)(
        write_coeffs, value_scale, decayed_vals, decayed_cot, carried_state, carried_adjoint, local_grads
    )
    return (grad_values, grad_write, grad_read, grad_skip)


def solution(mesh):
    in_specs = (
        P("dp", "ctx", None),
        P("dp", "ctx", None),
        P("dp", "ctx", None),
        P("dp", "ctx", None),
        P("dp", "ctx", None),
        P(),
    )
    out_specs = (P("dp", "ctx", None), P("dp", "ctx", None), P("dp", "ctx", None), P())
    return jax.shard_map(local, mesh=mesh, in_specs=in_specs, out_specs=out_specs, check_vma=False)
```

```python
import functools

import jax
import jax.numpy as jnp
from jax import lax
from jax.sharding import PartitionSpec as P


def spread_heads(per_head, width):
    return jnp.repeat(per_head, width, axis=-1)


def block_states(values, cotan, write_map, read_map, codes, factor):
    head_count = codes.shape[1]
    head_width = values.shape[1] // head_count
    log_decay = -codes.astype(jnp.float32) * factor
    within = jnp.cumsum(log_decay, axis=0)
    totals = within[-1]
    value_scale = spread_heads(jnp.exp(totals - within), head_width)
    cot_scale = spread_heads(jnp.exp(within), head_width)
    decayed_vals = (values.astype(jnp.float32) * value_scale).astype(jnp.bfloat16)
    decayed_cot = (cotan.astype(jnp.float32) * cot_scale).astype(jnp.bfloat16)
    fwd_state = jnp.einsum("jn,jq->nq", write_map, decayed_vals, preferred_element_type=jnp.float32)
    adj_state = jnp.einsum("in,iq->nq", read_map, decayed_cot, preferred_element_type=jnp.float32)
    skip_part = jnp.sum(
        (values.astype(jnp.float32) * cotan.astype(jnp.float32)).reshape(
            values.shape[0], head_count, head_width
        ),
        axis=(0, 2),
    )
    return within, totals, value_scale, decayed_vals, decayed_cot, fwd_state, adj_state, skip_part


def block_local_grads(values, cotan, write_map, read_map, within, skip_gain):
    token_count = values.shape[0]
    head_count = skip_gain.shape[0]
    head_width = values.shape[1] // head_count
    vals_three = values.reshape(token_count, head_count, head_width)
    cot_three = cotan.reshape(token_count, head_count, head_width)
    rows = jnp.arange(token_count)
    causal = (rows[:, None] >= rows[None, :])[None]
    lead = within.T
    spread = lead[:, :, None] - lead[:, None, :]
    decay_matrix = jnp.where(causal, jnp.exp(jnp.where(causal, spread, 0.0)), 0.0)
    products = jnp.einsum("ihp,jhp->hij", cot_three, vals_three, preferred_element_type=jnp.float32)
    read_weights = (products * decay_matrix).astype(jnp.bfloat16)
    gram = jnp.einsum("in,jn->ij", read_map, write_map, preferred_element_type=jnp.float32)
    value_weights = (gram[None] * decay_matrix).astype(jnp.bfloat16)
    grad_read = jnp.einsum("hij,jn->in", read_weights, write_map, preferred_element_type=jnp.float32)
    grad_write = jnp.einsum("hij,in->jn", read_weights, read_map, preferred_element_type=jnp.float32)
    grad_values = jnp.einsum(
        "hij,ihp->jhp", value_weights, cot_three, preferred_element_type=jnp.float32
    ) + skip_gain[None, :, None] * cot_three.astype(jnp.float32)
    return grad_values.reshape(token_count, head_count * head_width), grad_write, grad_read


def block_carried_grads(
    write_map, value_scale, decayed_vals, decayed_cot, carried_state, carried_adjoint, local_grads
):
    local_values, local_write, local_read = local_grads
    state_rounded = carried_state.astype(jnp.bfloat16)
    adjoint_rounded = carried_adjoint.astype(jnp.bfloat16)
    grad_read = local_read + jnp.einsum(
        "iq,nq->in", decayed_cot, state_rounded, preferred_element_type=jnp.float32
    )
    grad_write = local_write + jnp.einsum(
        "jq,nq->jn", decayed_vals, adjoint_rounded, preferred_element_type=jnp.float32
    )
    carried_term = jnp.einsum("jn,nq->jq", write_map, adjoint_rounded, preferred_element_type=jnp.float32)
    grad_values = local_values + value_scale * carried_term
    return (
        grad_values.astype(jnp.bfloat16),
        grad_write.astype(jnp.bfloat16),
        grad_read.astype(jnp.bfloat16),
    )


def xor_pairs(count, bit):
    return [(i, i ^ (1 << bit)) for i in range(count)]


def gather_totals(totals, skip_part, position, count):
    rows = jnp.arange(count)[:, None]
    table = jnp.concatenate([jnp.where(rows == position, totals[None, :], 0.0), skip_part[None, :]], 0)
    tables = [table]
    for bit in range(count.bit_length() - 1):
        table = table + lax.ppermute(table, "ctx", xor_pairs(count, bit))
        tables.append(table)
    return tables


def range_gain(table, count, low, high, reverse):
    rows = jnp.arange(count)
    virtual = count - 1 - rows if reverse else rows
    inside = (virtual >= low) & (virtual <= high)
    return jnp.exp(jnp.sum(jnp.where(inside[:, None], table[:count], 0.0), axis=0))


def take_half(array, upper):
    half = array.shape[-1] // 2
    return jnp.where(upper, array[..., half:], array[..., :half])


def join_halves(mine, other, upper):
    return jnp.where(upper, jnp.concatenate([other, mine], -1), jnp.concatenate([mine, other], -1))


class Direction:
    def __init__(self, tables, position, count, reverse, head_width):
        self.tables = tables
        self.count = count
        self.reverse = reverse
        self.head_width = head_width
        self.index = count - 1 - position if reverse else position
        self.upper = self.index % 2 == 1
        self.pair = self.index // 2

    def actual(self, pairs):
        if self.reverse:
            return [(self.count - 1 - a, self.count - 1 - b) for a, b in pairs]
        return pairs

    def pair_pairs(self, pairs):
        return self.actual([(2 * a + j, 2 * b + j) for a, b in pairs for j in (0, 1)])

    def gain(self, table_index, low_block, high_block):
        full = range_gain(self.tables[table_index], self.count, low_block, high_block, self.reverse)
        return spread_heads(take_half(full, self.upper), self.head_width)[..., None, :]


def pair_scan(way, pair_total):
    pair_count = way.count // 2
    level_count = pair_count.bit_length() - 1
    low_tables = lambda level: min(level + 1, len(way.tables) - 1)
    total = pair_total
    lowers = []
    for level in range(level_count):
        span = 1 << level
        pairs = [(a, a + span) for a in range(pair_count) if a % (2 * span) == span - 1]
        lower = lax.ppermute(total, "ctx", way.pair_pairs(pairs))
        lowers.append(lower)
        if level < level_count - 1:
            first = 2 * (way.pair - span + 1)
            total = way.gain(low_tables(level), first, 2 * way.pair + 1) * lower + total
    prefix = jnp.zeros_like(pair_total)
    for level in reversed(range(level_count)):
        span = 1 << level
        if level < level_count - 1:
            pairs = [(a, a - span) for a in range(pair_count) if a % (2 * span) == 2 * span - 1]
            prefix = prefix + lax.ppermute(prefix, "ctx", way.pair_pairs(pairs))
        first = 2 * (way.pair - 2 * span + 1)
        lower_gain = way.gain(-1, first, 2 * (way.pair - span) + 1)
        lower_gain = jnp.where(way.pair % (2 * span) == 2 * span - 1, lower_gain, 1.0)
        prefix = lower_gain * prefix + lowers[level]
    return prefix


def carried_pair(tables, fwd_state, adj_state, position, count, head_width):
    ways = [Direction(tables, position, count, reverse, head_width) for reverse in (False, True)]
    states = [fwd_state, adj_state]
    sent = jnp.concatenate([take_half(s, ~w.upper) for s, w in zip(states, ways)], -1)
    got = lax.ppermute(sent, "ctx", [(i, i ^ 1) for i in range(count)])
    got = [got[..., : got.shape[-1] // 2], got[..., got.shape[-1] // 2 :]]
    lifted_parts = []
    keep_parts = []
    for way, state, other in zip(ways, states, got):
        own = take_half(state, way.upper)
        low_block = jnp.where(way.upper, other, own)
        high_block = jnp.where(way.upper, own, other)
        pair_total = way.gain(1, 2 * way.pair + 1, 2 * way.pair + 1) * low_block + high_block
        pair_prefix = pair_scan(way, pair_total)
        lifted = way.gain(1, 2 * way.pair, 2 * way.pair) * pair_prefix + low_block
        lifted_parts.append(jnp.where(way.upper, pair_prefix, lifted))
        keep_parts.append(jnp.where(way.upper, lifted, pair_prefix))
    got = lax.ppermute(jnp.concatenate(lifted_parts, -1), "ctx", [(i, i ^ 1) for i in range(count)])
    unit = jnp.exp(jnp.min(tables[-1]) * 0.0)
    got = got * unit
    half = got.shape[-1] // 2
    results = []
    for way, mine, other in zip(ways, keep_parts, [got[..., :half], got[..., half:]]):
        results.append(join_halves(mine, other, way.upper))
    return results


def local(token_values, cotangent, write_coeffs, read_coeffs, decay_codes, skip_gain):
    seq_len = token_values.shape[1] * lax.axis_size("ctx")
    factor = 0.25 / seq_len
    prepare = jax.vmap(functools.partial(block_states, factor=factor))
    within, totals, value_scale, decayed_vals, decayed_cot, fwd_state, adj_state, skip_parts = prepare(
        token_values, cotangent, write_coeffs, read_coeffs, decay_codes
    )
    position = lax.axis_index("ctx")
    count = lax.axis_size("ctx")
    tables = jax.vmap(gather_totals, (0, 0, None, None))(totals, skip_parts, position, count)
    grad_skip = jnp.sum(tables[-1][:, count], axis=0)
    for bit in range(lax.axis_size("dp").bit_length() - 1):
        grad_skip = grad_skip + lax.ppermute(grad_skip, "dp", xor_pairs(lax.axis_size("dp"), bit))
    head_width = token_values.shape[2] // decay_codes.shape[2]
    carried_state, carried_adjoint = jax.vmap(carried_pair, (0, 0, 0, None, None, None))(
        tables, fwd_state, adj_state, position, count, head_width
    )
    local_grads = jax.vmap(block_local_grads, (0, 0, 0, 0, 0, None))(
        token_values, cotangent, write_coeffs, read_coeffs, within, skip_gain
    )
    grad_values, grad_write, grad_read = jax.vmap(block_carried_grads)(
        write_coeffs, value_scale, decayed_vals, decayed_cot, carried_state, carried_adjoint, local_grads
    )
    return (grad_values, grad_write, grad_read, grad_skip)


def solution(mesh):
    in_specs = (
        P("dp", "ctx", None),
        P("dp", "ctx", None),
        P("dp", "ctx", None),
        P("dp", "ctx", None),
        P("dp", "ctx", None),
        P(),
    )
    out_specs = (P("dp", "ctx", None), P("dp", "ctx", None), P("dp", "ctx", None), P())
    return jax.shard_map(local, mesh=mesh, in_specs=in_specs, out_specs=out_specs, check_vma=False)
```

```python
import functools

import jax
import jax.numpy as jnp
from jax import lax
from jax.sharding import PartitionSpec as P


def spread_heads(per_head, width):
    return jnp.repeat(per_head, width, axis=-1)


def block_states(values, cotan, write_map, read_map, codes, factor):
    head_count = codes.shape[1]
    head_width = values.shape[1] // head_count
    log_decay = -codes.astype(jnp.float32) * factor
    within = jnp.cumsum(log_decay, axis=0)
    totals = within[-1]
    value_scale = spread_heads(jnp.exp(totals - within), head_width)
    cot_scale = spread_heads(jnp.exp(within), head_width)
    decayed_vals = (values.astype(jnp.float32) * value_scale).astype(jnp.bfloat16)
    decayed_cot = (cotan.astype(jnp.float32) * cot_scale).astype(jnp.bfloat16)
    fwd_state = jnp.einsum("jn,jq->nq", write_map, decayed_vals, preferred_element_type=jnp.float32)
    adj_state = jnp.einsum("in,iq->nq", read_map, decayed_cot, preferred_element_type=jnp.float32)
    skip_part = jnp.sum(
        (values.astype(jnp.float32) * cotan.astype(jnp.float32)).reshape(
            values.shape[0], head_count, head_width
        ),
        axis=(0, 2),
    )
    return within, totals, value_scale, decayed_vals, decayed_cot, fwd_state, adj_state, skip_part


def block_local_grads(values, cotan, write_map, read_map, within, skip_gain):
    token_count = values.shape[0]
    head_count = skip_gain.shape[0]
    head_width = values.shape[1] // head_count
    vals_three = values.reshape(token_count, head_count, head_width)
    cot_three = cotan.reshape(token_count, head_count, head_width)
    rows = jnp.arange(token_count)
    causal = (rows[:, None] >= rows[None, :])[None]
    lead = within.T
    spread = lead[:, :, None] - lead[:, None, :]
    decay_matrix = jnp.where(causal, jnp.exp(jnp.where(causal, spread, 0.0)), 0.0)
    products = jnp.einsum("ihp,jhp->hij", cot_three, vals_three, preferred_element_type=jnp.float32)
    read_weights = (products * decay_matrix).astype(jnp.bfloat16)
    gram = jnp.einsum("in,jn->ij", read_map, write_map, preferred_element_type=jnp.float32)
    value_weights = (gram[None] * decay_matrix).astype(jnp.bfloat16)
    grad_read = jnp.einsum("hij,jn->in", read_weights, write_map, preferred_element_type=jnp.float32)
    grad_write = jnp.einsum("hij,in->jn", read_weights, read_map, preferred_element_type=jnp.float32)
    grad_values = jnp.einsum(
        "hij,ihp->jhp", value_weights, cot_three, preferred_element_type=jnp.float32
    ) + skip_gain[None, :, None] * cot_three.astype(jnp.float32)
    return grad_values.reshape(token_count, head_count * head_width), grad_write, grad_read


def block_carried_grads(
    write_map, value_scale, decayed_vals, decayed_cot, carried_state, carried_adjoint, local_grads
):
    local_values, local_write, local_read = local_grads
    state_rounded = carried_state.astype(jnp.bfloat16)
    adjoint_rounded = carried_adjoint.astype(jnp.bfloat16)
    grad_read = local_read + jnp.einsum(
        "iq,nq->in", decayed_cot, state_rounded, preferred_element_type=jnp.float32
    )
    grad_write = local_write + jnp.einsum(
        "jq,nq->jn", decayed_vals, adjoint_rounded, preferred_element_type=jnp.float32
    )
    carried_term = jnp.einsum("jn,nq->jq", write_map, adjoint_rounded, preferred_element_type=jnp.float32)
    grad_values = local_values + value_scale * carried_term
    return (
        grad_values.astype(jnp.bfloat16),
        grad_write.astype(jnp.bfloat16),
        grad_read.astype(jnp.bfloat16),
    )


def xor_pairs(count, bit):
    return [(i, i ^ (1 << bit)) for i in range(count)]


def gather_totals(totals, skip_part, position, count):
    rows = jnp.arange(count)[:, None]
    table = jnp.concatenate([jnp.where(rows == position, totals[None, :], 0.0), skip_part[None, :]], 0)
    tables = [table]
    for bit in range(count.bit_length() - 1):
        table = table + lax.ppermute(table, "ctx", xor_pairs(count, bit))
        tables.append(table)
    return tables


def range_gain(table, count, low, high, reverse):
    rows = jnp.arange(count)
    virtual = count - 1 - rows if reverse else rows
    inside = (virtual >= low) & (virtual <= high)
    return jnp.exp(jnp.sum(jnp.where(inside[:, None], table[:count], 0.0), axis=0))


def take_half(array, upper):
    half = array.shape[-1] // 2
    return jnp.where(upper, array[..., half:], array[..., :half])


def join_halves(mine, other, upper):
    return jnp.where(upper, jnp.concatenate([other, mine], -1), jnp.concatenate([mine, other], -1))


class Direction:
    def __init__(self, tables, position, count, reverse, head_width):
        self.tables = tables
        self.count = count
        self.reverse = reverse
        self.head_width = head_width
        self.index = count - 1 - position if reverse else position
        self.upper = self.index % 2 == 1
        self.pair = self.index // 2

    def actual(self, pairs):
        if self.reverse:
            return [(self.count - 1 - a, self.count - 1 - b) for a, b in pairs]
        return pairs

    def pair_pairs(self, pairs):
        return self.actual([(2 * a + j, 2 * b + j) for a, b in pairs for j in (0, 1)])

    def gain(self, table_index, low_block, high_block):
        full = range_gain(self.tables[table_index], self.count, low_block, high_block, self.reverse)
        return spread_heads(take_half(full, self.upper), self.head_width)[..., None, :]


def pair_scan(way, pair_total):
    pair_count = way.count // 2
    level_count = pair_count.bit_length() - 1
    flip = level_count >= 2
    last_table = len(way.tables) - 1
    table_at = lambda level: min(level + 2, last_table)
    pair = way.pair
    role = jnp.where(way.upper, pair ^ 1, pair) if flip else pair

    def device_pairs(pairs, first_level):
        lower = [(2 * a, 2 * b) for a, b in pairs]
        if flip and first_level:
            upper = [(2 * b + 1, 2 * a + 1) for a, b in pairs]
        elif flip:
            upper = [(2 * (a ^ 1) + 1, 2 * (b ^ 1) + 1) for a, b in pairs]
        else:
            upper = [(2 * a + 1, 2 * b + 1) for a, b in pairs]
        return way.actual(lower + upper)

    def pair_gain(level, low_pair, high_pair):
        return way.gain(table_at(level), 2 * low_pair, 2 * high_pair + 1)

    total = pair_total
    lowers = []
    for level in range(level_count):
        span = 1 << level
        pairs = [(a, a + span) for a in range(pair_count) if a % (2 * span) == span - 1]
        lower = lax.ppermute(total, "ctx", device_pairs(pairs, level == 0))
        lowers.append(lower)
        if level < level_count - 1:
            if flip and level == 0:
                kept_upper = pair_gain(0, pair ^ 1, pair ^ 1) * total + lower
                kept_lower = pair_gain(0, pair, pair) * lower + total
                total = jnp.where(way.upper, kept_upper, kept_lower)
            else:
                total = pair_gain(level, role - span + 1, role) * lower + total
    prefix = jnp.zeros_like(pair_total)
    for level in reversed(range(level_count)):
        span = 1 << level
        if flip and level == 0:
            sent = jnp.where(way.upper, pair_gain(0, pair, pair) * prefix + pair_total, prefix)
            pairs = [(2 * (a + 1), 2 * a) for a in range(0, pair_count, 2)]
            pairs += [(2 * a + 1, 2 * (a + 1) + 1) for a in range(0, pair_count, 2)]
            got = lax.ppermute(sent, "ctx", way.actual(pairs))
            grown = pair_gain(level_count, pair - 1, pair - 1) * prefix + lowers[0]
            odd = pair % 2 == 1
            prefix = jnp.where(way.upper, jnp.where(odd, got, prefix), jnp.where(odd, grown, got))
            continue
        if level < level_count - 1:
            pairs = [(a, a - span) for a in range(pair_count) if a % (2 * span) == 2 * span - 1]
            prefix = prefix + lax.ppermute(prefix, "ctx", device_pairs(pairs, False))
        lower_gain = pair_gain(level_count, role - 2 * span + 1, role - span)
        lower_gain = jnp.where(role % (2 * span) == 2 * span - 1, lower_gain, 1.0)
        prefix = lower_gain * prefix + lowers[level]
    return prefix


def carried_pair(tables, fwd_state, adj_state, position, count, head_width):
    ways = [Direction(tables, position, count, reverse, head_width) for reverse in (False, True)]
    states = [fwd_state, adj_state]
    sent = jnp.concatenate([take_half(s, ~w.upper) for s, w in zip(states, ways)], -1)
    got = lax.ppermute(sent, "ctx", [(i, i ^ 1) for i in range(count)])
    got = [got[..., : got.shape[-1] // 2], got[..., got.shape[-1] // 2 :]]
    lifted_parts = []
    keep_parts = []
    for way, state, other in zip(ways, states, got):
        own = take_half(state, way.upper)
        low_block = jnp.where(way.upper, other, own)
        high_block = jnp.where(way.upper, own, other)
        pair_total = way.gain(1, 2 * way.pair + 1, 2 * way.pair + 1) * low_block + high_block
        pair_prefix = pair_scan(way, pair_total)
        lifted = way.gain(1, 2 * way.pair, 2 * way.pair) * pair_prefix + low_block
        lifted_parts.append(jnp.where(way.upper, pair_prefix, lifted))
        keep_parts.append(jnp.where(way.upper, lifted, pair_prefix))
    got = lax.ppermute(jnp.concatenate(lifted_parts, -1), "ctx", [(i, i ^ 1) for i in range(count)])
    unit = jnp.exp(jnp.min(tables[-1]) * 0.0)
    got = got * unit
    half = got.shape[-1] // 2
    results = []
    for way, mine, other in zip(ways, keep_parts, [got[..., :half], got[..., half:]]):
        results.append(join_halves(mine, other, way.upper))
    return results


def local(token_values, cotangent, write_coeffs, read_coeffs, decay_codes, skip_gain):
    seq_len = token_values.shape[1] * lax.axis_size("ctx")
    factor = 0.25 / seq_len
    prepare = jax.vmap(functools.partial(block_states, factor=factor))
    within, totals, value_scale, decayed_vals, decayed_cot, fwd_state, adj_state, skip_parts = prepare(
        token_values, cotangent, write_coeffs, read_coeffs, decay_codes
    )
    position = lax.axis_index("ctx")
    count = lax.axis_size("ctx")
    tables = jax.vmap(gather_totals, (0, 0, None, None))(totals, skip_parts, position, count)
    grad_skip = jnp.sum(tables[-1][:, count], axis=0)
    for bit in range(lax.axis_size("dp").bit_length() - 1):
        grad_skip = grad_skip + lax.ppermute(grad_skip, "dp", xor_pairs(lax.axis_size("dp"), bit))
    head_width = token_values.shape[2] // decay_codes.shape[2]
    carried_state, carried_adjoint = jax.vmap(carried_pair, (0, 0, 0, None, None, None))(
        tables, fwd_state, adj_state, position, count, head_width
    )
    local_grads = jax.vmap(block_local_grads, (0, 0, 0, 0, 0, None))(
        token_values, cotangent, write_coeffs, read_coeffs, within, skip_gain
    )
    grad_values, grad_write, grad_read = jax.vmap(block_carried_grads)(
        write_coeffs, value_scale, decayed_vals, decayed_cot, carried_state, carried_adjoint, local_grads
    )
    return (grad_values, grad_write, grad_read, grad_skip)


def solution(mesh):
    in_specs = (
        P("dp", "ctx", None),
        P("dp", "ctx", None),
        P("dp", "ctx", None),
        P("dp", "ctx", None),
        P("dp", "ctx", None),
        P(),
    )
    out_specs = (P("dp", "ctx", None), P("dp", "ctx", None), P("dp", "ctx", None), P())
    return jax.shard_map(local, mesh=mesh, in_specs=in_specs, out_specs=out_specs, check_vma=False)
```

```python
import functools

import jax
import jax.numpy as jnp
from jax import lax
from jax.sharding import PartitionSpec as P


def spread_heads(per_head, width):
    return jnp.repeat(per_head, width, axis=-1)


def block_states(values, cotan, write_map, read_map, codes, factor):
    head_count = codes.shape[1]
    head_width = values.shape[1] // head_count
    log_decay = -codes.astype(jnp.float32) * factor
    within = jnp.cumsum(log_decay, axis=0)
    totals = within[-1]
    value_scale = spread_heads(jnp.exp(totals - within), head_width)
    cot_scale = spread_heads(jnp.exp(within), head_width)
    decayed_vals = (values.astype(jnp.float32) * value_scale).astype(jnp.bfloat16)
    decayed_cot = (cotan.astype(jnp.float32) * cot_scale).astype(jnp.bfloat16)
    fwd_state = jnp.einsum("jn,jq->nq", write_map, decayed_vals, preferred_element_type=jnp.float32)
    adj_state = jnp.einsum("in,iq->nq", read_map, decayed_cot, preferred_element_type=jnp.float32)
    skip_part = jnp.sum(
        (values.astype(jnp.float32) * cotan.astype(jnp.float32)).reshape(
            values.shape[0], head_count, head_width
        ),
        axis=(0, 2),
    )
    return within, totals, value_scale, decayed_vals, decayed_cot, fwd_state, adj_state, skip_part


def block_local_grads(values, cotan, write_map, read_map, within, skip_gain):
    token_count = values.shape[0]
    head_count = skip_gain.shape[0]
    head_width = values.shape[1] // head_count
    vals_three = values.reshape(token_count, head_count, head_width)
    cot_three = cotan.reshape(token_count, head_count, head_width)
    rows = jnp.arange(token_count)
    causal = (rows[:, None] >= rows[None, :])[None]
    lead = within.T
    spread = lead[:, :, None] - lead[:, None, :]
    decay_matrix = jnp.where(causal, jnp.exp(jnp.where(causal, spread, 0.0)), 0.0)
    products = jnp.einsum("ihp,jhp->hij", cot_three, vals_three, preferred_element_type=jnp.float32)
    read_weights = (products * decay_matrix).astype(jnp.bfloat16)
    gram = jnp.einsum("in,jn->ij", read_map, write_map, preferred_element_type=jnp.float32)
    value_weights = (gram[None] * decay_matrix).astype(jnp.bfloat16)
    grad_read = jnp.einsum("hij,jn->in", read_weights, write_map, preferred_element_type=jnp.float32)
    grad_write = jnp.einsum("hij,in->jn", read_weights, read_map, preferred_element_type=jnp.float32)
    grad_values = jnp.einsum(
        "hij,ihp->jhp", value_weights, cot_three, preferred_element_type=jnp.float32
    ) + skip_gain[None, :, None] * cot_three.astype(jnp.float32)
    return grad_values.reshape(token_count, head_count * head_width), grad_write, grad_read


def xor_pairs(count, bit):
    return [(i, i ^ (1 << bit)) for i in range(count)]


def gather_totals(totals, skip_part, position, count):
    rows = jnp.arange(count)[:, None]
    table = jnp.concatenate([jnp.where(rows == position, totals[None, :], 0.0), skip_part[None, :]], 0)
    tables = [table]
    for bit in range(count.bit_length() - 1):
        table = table + lax.ppermute(table, "ctx", xor_pairs(count, bit))
        tables.append(table)
    return tables


def range_gain(table, count, low, high, reverse):
    rows = jnp.arange(count)
    virtual = count - 1 - rows if reverse else rows
    inside = (virtual >= low) & (virtual <= high)
    return jnp.exp(jnp.sum(jnp.where(inside[:, None], table[:count], 0.0), axis=0))


def take_half(array, upper):
    half = array.shape[-1] // 2
    return jnp.where(upper, array[..., half:], array[..., :half])


def join_halves(mine, other, upper):
    return jnp.where(upper, jnp.concatenate([other, mine], -1), jnp.concatenate([mine, other], -1))


class Direction:
    def __init__(self, tables, position, count, reverse, head_width):
        self.tables = tables
        self.count = count
        self.reverse = reverse
        self.head_width = head_width
        self.index = count - 1 - position if reverse else position
        self.upper = self.index % 2 == 1
        self.pair = self.index // 2

    def actual(self, pairs):
        if self.reverse:
            return [(self.count - 1 - a, self.count - 1 - b) for a, b in pairs]
        return pairs

    def pair_pairs(self, pairs):
        return self.actual([(2 * a + j, 2 * b + j) for a, b in pairs for j in (0, 1)])

    def gain(self, table_index, low_block, high_block):
        full = range_gain(self.tables[table_index], self.count, low_block, high_block, self.reverse)
        return spread_heads(take_half(full, self.upper), self.head_width)[..., None, :]


def exchange(payloads, pair_lists):
    results = [None] * len(payloads)
    done = set()
    for first in range(len(payloads)):
        if first in done:
            continue
        group = [k for k in range(len(payloads)) if set(pair_lists[k]) == set(pair_lists[first])]
        done.update(group)
        widths = [payloads[k].shape[-1] for k in group]
        moved = lax.ppermute(jnp.concatenate([payloads[k] for k in group], -1), "ctx", pair_lists[first])
        offset = 0
        for k, width in zip(group, widths):
            results[k] = moved[..., offset : offset + width]
            offset += width
    return results


class PairScan:
    def __init__(self, way):
        self.way = way
        self.pair_count = way.count // 2
        self.level_count = self.pair_count.bit_length() - 1
        self.flip = self.level_count >= 2
        pair = way.pair
        self.role = jnp.where(way.upper, pair ^ 1, pair) if self.flip else pair

    def device_pairs(self, pairs, first_level):
        lower = [(2 * a, 2 * b) for a, b in pairs]
        if self.flip and first_level:
            upper = [(2 * b + 1, 2 * a + 1) for a, b in pairs]
        elif self.flip:
            upper = [(2 * (a ^ 1) + 1, 2 * (b ^ 1) + 1) for a, b in pairs]
        else:
            upper = [(2 * a + 1, 2 * b + 1) for a, b in pairs]
        return self.way.actual(lower + upper)

    def pair_gain(self, level, low_pair, high_pair):
        table = min(level + 2, len(self.way.tables) - 1)
        return self.way.gain(table, 2 * low_pair, 2 * high_pair + 1)

    def up_send(self, level):
        span = 1 << level
        pairs = [(a, a + span) for a in range(self.pair_count) if a % (2 * span) == span - 1]
        return self.device_pairs(pairs, level == 0)

    def up_combine(self, level, total, lower):
        span = 1 << level
        if self.flip and level == 0:
            pair = self.way.pair
            kept_upper = self.pair_gain(0, pair ^ 1, pair ^ 1) * total + lower
            kept_lower = self.pair_gain(0, pair, pair) * lower + total
            return jnp.where(self.way.upper, kept_upper, kept_lower)
        return self.pair_gain(level, self.role - span + 1, self.role) * lower + total

    def down_send(self, level, prefix, pair_total):
        span = 1 << level
        if self.flip and level == 0:
            pair = self.way.pair
            sent = jnp.where(self.way.upper, self.pair_gain(0, pair, pair) * prefix + pair_total, prefix)
            pairs = [(2 * (a + 1), 2 * a) for a in range(0, self.pair_count, 2)]
            pairs += [(2 * a + 1, 2 * (a + 1) + 1) for a in range(0, self.pair_count, 2)]
            return sent, self.way.actual(pairs)
        pairs = [(a, a - span) for a in range(self.pair_count) if a % (2 * span) == 2 * span - 1]
        return prefix, self.device_pairs(pairs, False)

    def down_combine(self, level, prefix, got, lowers):
        span = 1 << level
        if self.flip and level == 0:
            pair = self.way.pair
            grown = self.pair_gain(self.level_count, pair - 1, pair - 1) * prefix + lowers[0]
            odd = pair % 2 == 1
            return jnp.where(self.way.upper, jnp.where(odd, got, prefix), jnp.where(odd, grown, got))
        if got is not None:
            prefix = prefix + got
        lower_gain = self.pair_gain(self.level_count, self.role - 2 * span + 1, self.role - span)
        lower_gain = jnp.where(self.role % (2 * span) == 2 * span - 1, lower_gain, 1.0)
        return lower_gain * prefix + lowers[level]


def pair_scans(ways, pair_totals):
    scans = [PairScan(way) for way in ways]
    level_count = scans[0].level_count
    totals = list(pair_totals)
    lowers = [[] for _ in scans]
    for level in range(level_count):
        got = exchange(totals, [scan.up_send(level) for scan in scans])
        for k, scan in enumerate(scans):
            lowers[k].append(got[k])
            if level < level_count - 1:
                totals[k] = scan.up_combine(level, totals[k], got[k])
    prefixes = [jnp.zeros_like(total) for total in pair_totals]
    for level in reversed(range(level_count)):
        if level < level_count - 1 or (scans[0].flip and level == 0):
            sends = [scan.down_send(level, p, t) for scan, p, t in zip(scans, prefixes, pair_totals)]
            got = exchange([s[0] for s in sends], [s[1] for s in sends])
        else:
            got = [None] * len(scans)
        prefixes = [
            scan.down_combine(level, p, g, low) for scan, p, g, low in zip(scans, prefixes, got, lowers)
        ]
    return prefixes


def carried_pair(tables, fwd_state, adj_state, position, count, head_width):
    ways = [Direction(tables, position, count, reverse, head_width) for reverse in (False, True)]
    states = [fwd_state, adj_state]
    sent = jnp.concatenate([take_half(s, ~w.upper) for s, w in zip(states, ways)], -1)
    got = lax.ppermute(sent, "ctx", [(i, i ^ 1) for i in range(count)])
    got = [got[..., : got.shape[-1] // 2], got[..., got.shape[-1] // 2 :]]
    lows = []
    totals = []
    for way, state, other in zip(ways, states, got):
        own = take_half(state, way.upper)
        low_block = jnp.where(way.upper, other, own)
        high_block = jnp.where(way.upper, own, other)
        lows.append(low_block)
        totals.append(way.gain(1, 2 * way.pair + 1, 2 * way.pair + 1) * low_block + high_block)
    pair_prefixes = pair_scans(ways, totals)
    lifted_parts = []
    keep_parts = []
    for way, pair_prefix, low_block in zip(ways, pair_prefixes, lows):
        lifted = way.gain(1, 2 * way.pair, 2 * way.pair) * pair_prefix + low_block
        lifted_parts.append(jnp.where(way.upper, pair_prefix, lifted))
        keep_parts.append(jnp.where(way.upper, lifted, pair_prefix))
    got = lax.ppermute(jnp.concatenate(lifted_parts, -1), "ctx", [(i, i ^ 1) for i in range(count)])
    unit = jnp.exp(jnp.min(tables[-1]) * 0.0)
    got = got * unit
    half = got.shape[-1] // 2
    others = [got[..., :half], got[..., half:]]
    return keep_parts, others, [way.upper for way in ways]


def block_carried_grads(write_map, value_scale, decayed_vals, decayed_cot, carried, local_grads):
    local_values, local_write, local_read = local_grads
    (state_mine, adjoint_mine), (state_other, adjoint_other), (state_upper, adjoint_upper) = carried

    def rows_times(coeffs, mine, other, upper):
        return jnp.einsum(
            "iq,nq->in", take_half(coeffs, upper), mine.astype(jnp.bfloat16), preferred_element_type=jnp.float32
        ) + jnp.einsum(
            "iq,nq->in", take_half(coeffs, ~upper), other.astype(jnp.bfloat16), preferred_element_type=jnp.float32
        )

    grad_read = local_read + rows_times(decayed_cot, state_mine, state_other, state_upper)
    grad_write = local_write + rows_times(decayed_vals, adjoint_mine, adjoint_other, adjoint_upper)
    term_mine = jnp.einsum(
        "jn,nq->jq", write_map, adjoint_mine.astype(jnp.bfloat16), preferred_element_type=jnp.float32
    )
    term_other = jnp.einsum(
        "jn,nq->jq", write_map, adjoint_other.astype(jnp.bfloat16), preferred_element_type=jnp.float32
    )
    carried_term = join_halves(term_mine, term_other, adjoint_upper)
    grad_values = local_values + value_scale * carried_term
    return (
        grad_values.astype(jnp.bfloat16),
        grad_write.astype(jnp.bfloat16),
        grad_read.astype(jnp.bfloat16),
    )


def local(token_values, cotangent, write_coeffs, read_coeffs, decay_codes, skip_gain):
    seq_len = token_values.shape[1] * lax.axis_size("ctx")
    factor = 0.25 / seq_len
    prepare = jax.vmap(functools.partial(block_states, factor=factor))
    within, totals, value_scale, decayed_vals, decayed_cot, fwd_state, adj_state, skip_parts = prepare(
        token_values, cotangent, write_coeffs, read_coeffs, decay_codes
    )
    position = lax.axis_index("ctx")
    count = lax.axis_size("ctx")
    tables = jax.vmap(gather_totals, (0, 0, None, None))(totals, skip_parts, position, count)
    grad_skip = jnp.sum(tables[-1][:, count], axis=0)
    for bit in range(lax.axis_size("dp").bit_length() - 1):
        grad_skip = grad_skip + lax.ppermute(grad_skip, "dp", xor_pairs(lax.axis_size("dp"), bit))
    head_width = token_values.shape[2] // decay_codes.shape[2]
    carried = jax.vmap(carried_pair, (0, 0, 0, None, None, None))(
        tables, fwd_state, adj_state, position, count, head_width
    )
    local_grads = jax.vmap(block_local_grads, (0, 0, 0, 0, 0, None))(
        token_values, cotangent, write_coeffs, read_coeffs, within, skip_gain
    )
    grad_values, grad_write, grad_read = jax.vmap(block_carried_grads)(
        write_coeffs, value_scale, decayed_vals, decayed_cot, carried, local_grads
    )
    return (grad_values, grad_write, grad_read, grad_skip)


def solution(mesh):
    in_specs = (
        P("dp", "ctx", None),
        P("dp", "ctx", None),
        P("dp", "ctx", None),
        P("dp", "ctx", None),
        P("dp", "ctx", None),
        P(),
    )
    out_specs = (P("dp", "ctx", None), P("dp", "ctx", None), P("dp", "ctx", None), P())
    return jax.shard_map(local, mesh=mesh, in_specs=in_specs, out_specs=out_specs, check_vma=False)
```

```python
import functools

import jax
import jax.numpy as jnp
from jax import lax
from jax.sharding import PartitionSpec as P


def spread_heads(per_head, width):
    return jnp.repeat(per_head, width, axis=-1)


def block_states(values, cotan, write_map, read_map, codes, factor):
    head_count = codes.shape[1]
    head_width = values.shape[1] // head_count
    log_decay = -codes.astype(jnp.float32) * factor
    within = jnp.cumsum(log_decay, axis=0)
    totals = within[-1]
    value_scale = spread_heads(jnp.exp(totals - within), head_width)
    cot_scale = spread_heads(jnp.exp(within), head_width)
    decayed_vals = (values.astype(jnp.float32) * value_scale).astype(jnp.bfloat16)
    decayed_cot = (cotan.astype(jnp.float32) * cot_scale).astype(jnp.bfloat16)
    fwd_state = jnp.einsum("jn,jq->nq", write_map, decayed_vals, preferred_element_type=jnp.float32)
    adj_state = jnp.einsum("in,iq->nq", read_map, decayed_cot, preferred_element_type=jnp.float32)
    skip_part = jnp.sum(
        (values.astype(jnp.float32) * cotan.astype(jnp.float32)).reshape(
            values.shape[0], head_count, head_width
        ),
        axis=(0, 2),
    )
    return within, totals, value_scale, decayed_vals, decayed_cot, fwd_state, adj_state, skip_part


def block_local_grads(values, cotan, write_map, read_map, within, skip_gain):
    token_count = values.shape[0]
    head_count = skip_gain.shape[0]
    head_width = values.shape[1] // head_count
    vals_three = values.reshape(token_count, head_count, head_width)
    cot_three = cotan.reshape(token_count, head_count, head_width)
    rows = jnp.arange(token_count)
    causal = (rows[:, None] >= rows[None, :])[None]
    lead = within.T
    spread = lead[:, :, None] - lead[:, None, :]
    decay_matrix = jnp.where(causal, jnp.exp(jnp.where(causal, spread, 0.0)), 0.0)
    products = jnp.einsum("ihp,jhp->hij", cot_three, vals_three, preferred_element_type=jnp.float32)
    read_weights = (products * decay_matrix).astype(jnp.bfloat16)
    gram = jnp.einsum("in,jn->ij", read_map, write_map, preferred_element_type=jnp.float32)
    value_weights = (gram[None] * decay_matrix).astype(jnp.bfloat16)
    grad_read = jnp.einsum("hij,jn->in", read_weights, write_map, preferred_element_type=jnp.float32)
    grad_write = jnp.einsum("hij,in->jn", read_weights, read_map, preferred_element_type=jnp.float32)
    grad_values = jnp.einsum(
        "hij,ihp->jhp", value_weights, cot_three, preferred_element_type=jnp.float32
    ) + skip_gain[None, :, None] * cot_three.astype(jnp.float32)
    return grad_values.reshape(token_count, head_count * head_width), grad_write, grad_read


def xor_pairs(count, bit):
    return [(i, i ^ (1 << bit)) for i in range(count)]


def gather_totals(totals, skip_part, position, count):
    rows = jnp.arange(count)[:, None]
    table = jnp.concatenate([jnp.where(rows == position, totals[None, :], 0.0), skip_part[None, :]], 0)
    tables = [table]
    for bit in range(count.bit_length() - 1):
        table = table + lax.ppermute(table, "ctx", xor_pairs(count, bit))
        tables.append(table)
    return tables


def range_gain(table, count, low, high, reverse):
    rows = jnp.arange(count)
    virtual = count - 1 - rows if reverse else rows
    inside = (virtual >= low) & (virtual <= high)
    return jnp.exp(jnp.sum(jnp.where(inside[:, None], table[:count], 0.0), axis=0))


def take_half(array, upper):
    half = array.shape[-1] // 2
    return jnp.where(upper, array[..., half:], array[..., :half])


def join_halves(mine, other, upper):
    return jnp.where(upper, jnp.concatenate([other, mine], -1), jnp.concatenate([mine, other], -1))


class Direction:
    def __init__(self, tables, position, count, reverse, head_width):
        self.tables = tables
        self.count = count
        self.reverse = reverse
        self.head_width = head_width
        self.index = count - 1 - position if reverse else position
        self.upper = self.index % 2 == 1
        self.pair = self.index // 2

    def actual(self, pairs):
        if self.reverse:
            return [(self.count - 1 - a, self.count - 1 - b) for a, b in pairs]
        return pairs

    def pair_pairs(self, pairs):
        return self.actual([(2 * a + j, 2 * b + j) for a, b in pairs for j in (0, 1)])

    def gain(self, table_index, low_block, high_block):
        full = range_gain(self.tables[table_index], self.count, low_block, high_block, self.reverse)
        return spread_heads(take_half(full, self.upper), self.head_width)[..., None, :]


def exchange(payloads, pair_lists):
    return [lax.ppermute(p, "ctx", pairs) for p, pairs in zip(payloads, pair_lists)]


class PairScan:
    def __init__(self, way):
        self.way = way
        self.pair_count = way.count // 2
        self.level_count = self.pair_count.bit_length() - 1
        self.flip = self.level_count >= 2
        pair = way.pair
        self.role = jnp.where(way.upper, pair ^ 1, pair) if self.flip else pair

    def device_pairs(self, pairs, first_level):
        lower = [(2 * a, 2 * b) for a, b in pairs]
        if self.flip and first_level:
            upper = [(2 * b + 1, 2 * a + 1) for a, b in pairs]
        elif self.flip:
            upper = [(2 * (a ^ 1) + 1, 2 * (b ^ 1) + 1) for a, b in pairs]
        else:
            upper = [(2 * a + 1, 2 * b + 1) for a, b in pairs]
        return self.way.actual(lower + upper)

    def pair_gain(self, level, low_pair, high_pair):
        table = min(level + 2, len(self.way.tables) - 1)
        return self.way.gain(table, 2 * low_pair, 2 * high_pair + 1)

    def up_send(self, level):
        span = 1 << level
        pairs = [(a, a + span) for a in range(self.pair_count) if a % (2 * span) == span - 1]
        return self.device_pairs(pairs, level == 0)

    def up_combine(self, level, total, lower):
        span = 1 << level
        if self.flip and level == 0:
            pair = self.way.pair
            kept_upper = self.pair_gain(0, pair ^ 1, pair ^ 1) * total + lower
            kept_lower = self.pair_gain(0, pair, pair) * lower + total
            return jnp.where(self.way.upper, kept_upper, kept_lower)
        return self.pair_gain(level, self.role - span + 1, self.role) * lower + total

    def down_send(self, level, prefix, pair_total):
        span = 1 << level
        if self.flip and level == 0:
            pair = self.way.pair
            sent = jnp.where(self.way.upper, self.pair_gain(0, pair, pair) * prefix + pair_total, prefix)
            pairs = [(2 * (a + 1), 2 * a) for a in range(0, self.pair_count, 2)]
            pairs += [(2 * a + 1, 2 * (a + 1) + 1) for a in range(0, self.pair_count, 2)]
            return sent, self.way.actual(pairs)
        pairs = [(a, a - span) for a in range(self.pair_count) if a % (2 * span) == 2 * span - 1]
        return prefix, self.device_pairs(pairs, False)

    def down_combine(self, level, prefix, got, lowers):
        span = 1 << level
        if self.flip and level == 0:
            pair = self.way.pair
            grown = self.pair_gain(self.level_count, pair - 1, pair - 1) * prefix + lowers[0]
            odd = pair % 2 == 1
            return jnp.where(self.way.upper, jnp.where(odd, got, prefix), jnp.where(odd, grown, got))
        if got is not None:
            prefix = prefix + got
        lower_gain = self.pair_gain(self.level_count, self.role - 2 * span + 1, self.role - span)
        lower_gain = jnp.where(self.role % (2 * span) == 2 * span - 1, lower_gain, 1.0)
        return lower_gain * prefix + lowers[level]


def pair_scans(ways, pair_totals):
    scans = [PairScan(way) for way in ways]
    level_count = scans[0].level_count
    totals = list(pair_totals)
    lowers = [[] for _ in scans]
    for level in range(level_count):
        got = exchange(totals, [scan.up_send(level) for scan in scans])
        for k, scan in enumerate(scans):
            lowers[k].append(got[k])
            if level < level_count - 1:
                totals[k] = scan.up_combine(level, totals[k], got[k])
    prefixes = [jnp.zeros_like(total) for total in pair_totals]
    for level in reversed(range(level_count)):
        if level < level_count - 1 or (scans[0].flip and level == 0):
            sends = [scan.down_send(level, p, t) for scan, p, t in zip(scans, prefixes, pair_totals)]
            got = exchange([s[0] for s in sends], [s[1] for s in sends])
        else:
            got = [None] * len(scans)
        prefixes = [
            scan.down_combine(level, p, g, low) for scan, p, g, low in zip(scans, prefixes, got, lowers)
        ]
    return prefixes


def carried_pair(tables, fwd_state, adj_state, position, count, head_width):
    ways = [Direction(tables, position, count, reverse, head_width) for reverse in (False, True)]
    states = [fwd_state, adj_state]
    sent = jnp.concatenate([take_half(s, ~w.upper) for s, w in zip(states, ways)], -1)
    got = lax.ppermute(sent, "ctx", [(i, i ^ 1) for i in range(count)])
    got = [got[..., : got.shape[-1] // 2], got[..., got.shape[-1] // 2 :]]
    lows = []
    totals = []
    for way, state, other in zip(ways, states, got):
        own = take_half(state, way.upper)
        low_block = jnp.where(way.upper, other, own)
        high_block = jnp.where(way.upper, own, other)
        lows.append(low_block)
        totals.append(way.gain(1, 2 * way.pair + 1, 2 * way.pair + 1) * low_block + high_block)
    pair_prefixes = pair_scans(ways, totals)
    lifted_parts = []
    keep_parts = []
    for way, pair_prefix, low_block in zip(ways, pair_prefixes, lows):
        lifted = way.gain(1, 2 * way.pair, 2 * way.pair) * pair_prefix + low_block
        lifted_parts.append(jnp.where(way.upper, pair_prefix, lifted))
        keep_parts.append(jnp.where(way.upper, lifted, pair_prefix))
    got = lax.ppermute(jnp.concatenate(lifted_parts, -1), "ctx", [(i, i ^ 1) for i in range(count)])
    unit = jnp.exp(jnp.min(tables[-1]) * 0.0)
    got = got * unit
    half = got.shape[-1] // 2
    others = [got[..., :half], got[..., half:]]
    return keep_parts, others, [way.upper for way in ways]


def block_carried_grads(write_map, value_scale, decayed_vals, decayed_cot, carried, local_grads):
    local_values, local_write, local_read = local_grads
    (state_mine, adjoint_mine), (state_other, adjoint_other), (state_upper, adjoint_upper) = carried

    def rows_times(coeffs, mine, other, upper):
        return jnp.einsum(
            "iq,nq->in", take_half(coeffs, upper), mine.astype(jnp.bfloat16), preferred_element_type=jnp.float32
        ) + jnp.einsum(
            "iq,nq->in", take_half(coeffs, ~upper), other.astype(jnp.bfloat16), preferred_element_type=jnp.float32
        )

    grad_read = local_read + rows_times(decayed_cot, state_mine, state_other, state_upper)
    grad_write = local_write + rows_times(decayed_vals, adjoint_mine, adjoint_other, adjoint_upper)
    term_mine = jnp.einsum(
        "jn,nq->jq", write_map, adjoint_mine.astype(jnp.bfloat16), preferred_element_type=jnp.float32
    )
    term_other = jnp.einsum(
        "jn,nq->jq", write_map, adjoint_other.astype(jnp.bfloat16), preferred_element_type=jnp.float32
    )
    carried_term = join_halves(term_mine, term_other, adjoint_upper)
    grad_values = local_values + value_scale * carried_term
    return (
        grad_values.astype(jnp.bfloat16),
        grad_write.astype(jnp.bfloat16),
        grad_read.astype(jnp.bfloat16),
    )


def local(token_values, cotangent, write_coeffs, read_coeffs, decay_codes, skip_gain):
    seq_len = token_values.shape[1] * lax.axis_size("ctx")
    factor = 0.25 / seq_len
    prepare = jax.vmap(functools.partial(block_states, factor=factor))
    within, totals, value_scale, decayed_vals, decayed_cot, fwd_state, adj_state, skip_parts = prepare(
        token_values, cotangent, write_coeffs, read_coeffs, decay_codes
    )
    position = lax.axis_index("ctx")
    count = lax.axis_size("ctx")
    tables = jax.vmap(gather_totals, (0, 0, None, None))(totals, skip_parts, position, count)
    grad_skip = jnp.sum(tables[-1][:, count], axis=0)
    for bit in range(lax.axis_size("dp").bit_length() - 1):
        grad_skip = grad_skip + lax.ppermute(grad_skip, "dp", xor_pairs(lax.axis_size("dp"), bit))
    head_width = token_values.shape[2] // decay_codes.shape[2]
    carried = jax.vmap(carried_pair, (0, 0, 0, None, None, None))(
        tables, fwd_state, adj_state, position, count, head_width
    )
    local_grads = jax.vmap(block_local_grads, (0, 0, 0, 0, 0, None))(
        token_values, cotangent, write_coeffs, read_coeffs, within, skip_gain
    )
    grad_values, grad_write, grad_read = jax.vmap(block_carried_grads)(
        write_coeffs, value_scale, decayed_vals, decayed_cot, carried, local_grads
    )
    return (grad_values, grad_write, grad_read, grad_skip)


def solution(mesh):
    in_specs = (
        P("dp", "ctx", None),
        P("dp", "ctx", None),
        P("dp", "ctx", None),
        P("dp", "ctx", None),
        P("dp", "ctx", None),
        P(),
    )
    out_specs = (P("dp", "ctx", None), P("dp", "ctx", None), P("dp", "ctx", None), P())
    return jax.shard_map(local, mesh=mesh, in_specs=in_specs, out_specs=out_specs, check_vma=False)
```

```python
import functools

import jax
import jax.numpy as jnp
from jax import lax
from jax.sharding import PartitionSpec as P


def spread_heads(per_head, width):
    return jnp.repeat(per_head, width, axis=-1)


def block_states(values, cotan, write_map, read_map, codes, factor):
    head_count = codes.shape[1]
    head_width = values.shape[1] // head_count
    log_decay = -codes.astype(jnp.float32) * factor
    within = jnp.cumsum(log_decay, axis=0)
    totals = within[-1]
    value_scale = spread_heads(jnp.exp(totals - within), head_width)
    cot_scale = spread_heads(jnp.exp(within), head_width)
    decayed_vals = (values.astype(jnp.float32) * value_scale).astype(jnp.bfloat16)
    decayed_cot = (cotan.astype(jnp.float32) * cot_scale).astype(jnp.bfloat16)
    fwd_state = jnp.einsum("jn,jq->nq", write_map, decayed_vals, preferred_element_type=jnp.float32)
    adj_state = jnp.einsum("in,iq->nq", read_map, decayed_cot, preferred_element_type=jnp.float32)
    skip_part = jnp.sum(
        (values.astype(jnp.float32) * cotan.astype(jnp.float32)).reshape(
            values.shape[0], head_count, head_width
        ),
        axis=(0, 2),
    )
    return within, totals, value_scale, decayed_vals, decayed_cot, fwd_state, adj_state, skip_part


def block_local_grads(values, cotan, write_map, read_map, within, skip_gain):
    token_count = values.shape[0]
    head_count = skip_gain.shape[0]
    head_width = values.shape[1] // head_count
    vals_three = values.reshape(token_count, head_count, head_width)
    cot_three = cotan.reshape(token_count, head_count, head_width)
    rows = jnp.arange(token_count)
    causal = (rows[:, None] >= rows[None, :])[None]
    lead = within.T
    spread = lead[:, :, None] - lead[:, None, :]
    decay_matrix = jnp.where(causal, jnp.exp(jnp.where(causal, spread, 0.0)), 0.0)
    products = jnp.einsum("ihp,jhp->hij", cot_three, vals_three, preferred_element_type=jnp.float32)
    read_weights = (products * decay_matrix).astype(jnp.bfloat16)
    gram = jnp.einsum("in,jn->ij", read_map, write_map, preferred_element_type=jnp.float32)
    value_weights = (gram[None] * decay_matrix).astype(jnp.bfloat16)
    grad_read = jnp.einsum("hij,jn->in", read_weights, write_map, preferred_element_type=jnp.float32)
    grad_write = jnp.einsum("hij,in->jn", read_weights, read_map, preferred_element_type=jnp.float32)
    grad_values = jnp.einsum(
        "hij,ihp->jhp", value_weights, cot_three, preferred_element_type=jnp.float32
    ) + skip_gain[None, :, None] * cot_three.astype(jnp.float32)
    return grad_values.reshape(token_count, head_count * head_width), grad_write, grad_read


def xor_pairs(count, bit):
    return [(i, i ^ (1 << bit)) for i in range(count)]


def gather_totals(totals, skip_part, position, count):
    rows = jnp.arange(count)[:, None]
    table = jnp.concatenate([jnp.where(rows == position, totals[None, :], 0.0), skip_part[None, :]], 0)
    tables = [table]
    for bit in range(count.bit_length() - 1):
        table = table + lax.ppermute(table, "ctx", xor_pairs(count, bit))
        tables.append(table)
    return tables


def take_half(array, upper):
    half = array.shape[-1] // 2
    return jnp.where(upper, array[..., half:], array[..., :half])


def join_halves(mine, other, upper):
    return jnp.where(upper, jnp.concatenate([other, mine], -1), jnp.concatenate([mine, other], -1))


class Direction:
    def __init__(self, tables, position, count, reverse, head_width):
        self.tables = tables
        self.count = count
        self.reverse = reverse
        self.head_width = head_width
        self.index = count - 1 - position if reverse else position
        self.upper = self.index % 2 == 1
        self.pair = self.index // 2
        self.pyramids = {}

    def actual(self, pairs):
        if self.reverse:
            return [(self.count - 1 - a, self.count - 1 - b) for a, b in pairs]
        return pairs

    def pair_pairs(self, pairs):
        return self.actual([(2 * a + j, 2 * b + j) for a, b in pairs for j in (0, 1)])

    def gain(self, table_index, low_block, size):
        key = (table_index % len(self.tables), size)
        if key not in self.pyramids:
            rows = self.tables[key[0]][: self.count]
            if self.reverse:
                rows = rows[::-1]
            grouped = rows.reshape(self.count // size, size, rows.shape[-1]).sum(axis=1)
            self.pyramids[key] = jnp.exp(grouped)
        full = lax.dynamic_index_in_dim(self.pyramids[key], low_block // size, keepdims=False)
        return spread_heads(take_half(full, self.upper), self.head_width)[..., None, :]


def exchange(payloads, pair_lists):
    return [lax.ppermute(p, "ctx", pairs) for p, pairs in zip(payloads, pair_lists)]


class PairScan:
    def __init__(self, way):
        self.way = way
        self.pair_count = way.count // 2
        self.level_count = self.pair_count.bit_length() - 1
        self.flip = self.level_count >= 2
        pair = way.pair
        self.role = jnp.where(way.upper, pair ^ 1, pair) if self.flip else pair

    def device_pairs(self, pairs, first_level):
        lower = [(2 * a, 2 * b) for a, b in pairs]
        if self.flip and first_level:
            upper = [(2 * b + 1, 2 * a + 1) for a, b in pairs]
        elif self.flip:
            upper = [(2 * (a ^ 1) + 1, 2 * (b ^ 1) + 1) for a, b in pairs]
        else:
            upper = [(2 * a + 1, 2 * b + 1) for a, b in pairs]
        return self.way.actual(lower + upper)

    def pair_gain(self, level, low_pair, pair_span):
        table = min(level + 2, len(self.way.tables) - 1)
        return self.way.gain(table, 2 * low_pair, 2 * pair_span)

    def up_send(self, level):
        span = 1 << level
        pairs = [(a, a + span) for a in range(self.pair_count) if a % (2 * span) == span - 1]
        return self.device_pairs(pairs, level == 0)

    def up_combine(self, level, total, lower):
        span = 1 << level
        if self.flip and level == 0:
            pair = self.way.pair
            kept_upper = self.pair_gain(0, pair ^ 1, 1) * total + lower
            kept_lower = self.pair_gain(0, pair, 1) * lower + total
            return jnp.where(self.way.upper, kept_upper, kept_lower)
        return self.pair_gain(level, self.role - span + 1, span) * lower + total

    def down_send(self, level, prefix, pair_total):
        span = 1 << level
        if self.flip and level == 0:
            pair = self.way.pair
            sent = jnp.where(self.way.upper, self.pair_gain(0, pair, 1) * prefix + pair_total, prefix)
            pairs = [(2 * (a + 1), 2 * a) for a in range(0, self.pair_count, 2)]
            pairs += [(2 * a + 1, 2 * (a + 1) + 1) for a in range(0, self.pair_count, 2)]
            return sent, self.way.actual(pairs)
        pairs = [(a, a - span) for a in range(self.pair_count) if a % (2 * span) == 2 * span - 1]
        return prefix, self.device_pairs(pairs, False)

    def down_combine(self, level, prefix, got, lowers):
        span = 1 << level
        if self.flip and level == 0:
            pair = self.way.pair
            grown = self.pair_gain(self.level_count, pair - 1, 1) * prefix + lowers[0]
            odd = pair % 2 == 1
            return jnp.where(self.way.upper, jnp.where(odd, got, prefix), jnp.where(odd, grown, got))
        if got is not None:
            prefix = prefix + got
        lower_gain = self.pair_gain(self.level_count, self.role - 2 * span + 1, span)
        lower_gain = jnp.where(self.role % (2 * span) == 2 * span - 1, lower_gain, 1.0)
        return lower_gain * prefix + lowers[level]


def pair_scans(ways, pair_totals):
    scans = [PairScan(way) for way in ways]
    level_count = scans[0].level_count
    totals = list(pair_totals)
    lowers = [[] for _ in scans]
    for level in range(level_count):
        got = exchange(totals, [scan.up_send(level) for scan in scans])
        for k, scan in enumerate(scans):
            lowers[k].append(got[k])
            if level < level_count - 1:
                totals[k] = scan.up_combine(level, totals[k], got[k])
    prefixes = [jnp.zeros_like(total) for total in pair_totals]
    for level in reversed(range(level_count)):
        if level < level_count - 1 or (scans[0].flip and level == 0):
            sends = [scan.down_send(level, p, t) for scan, p, t in zip(scans, prefixes, pair_totals)]
            got = exchange([s[0] for s in sends], [s[1] for s in sends])
        else:
            got = [None] * len(scans)
        prefixes = [
            scan.down_combine(level, p, g, low) for scan, p, g, low in zip(scans, prefixes, got, lowers)
        ]
    return prefixes


def carried_pair(tables, fwd_state, adj_state, position, count, head_width):
    ways = [Direction(tables, position, count, reverse, head_width) for reverse in (False, True)]
    states = [fwd_state, adj_state]
    sent = jnp.concatenate([take_half(s, ~w.upper) for s, w in zip(states, ways)], -1)
    got = lax.ppermute(sent, "ctx", [(i, i ^ 1) for i in range(count)])
    got = [got[..., : got.shape[-1] // 2], got[..., got.shape[-1] // 2 :]]
    lows = []
    totals = []
    for way, state, other in zip(ways, states, got):
        own = take_half(state, way.upper)
        low_block = jnp.where(way.upper, other, own)
        high_block = jnp.where(way.upper, own, other)
        lows.append(low_block)
        totals.append(way.gain(1, 2 * way.pair + 1, 1) * low_block + high_block)
    pair_prefixes = pair_scans(ways, totals)
    lifted_parts = []
    keep_parts = []
    for way, pair_prefix, low_block in zip(ways, pair_prefixes, lows):
        lifted = way.gain(1, 2 * way.pair, 1) * pair_prefix + low_block
        lifted_parts.append(jnp.where(way.upper, pair_prefix, lifted))
        keep_parts.append(jnp.where(way.upper, lifted, pair_prefix))
    got = lax.ppermute(jnp.concatenate(lifted_parts, -1), "ctx", [(i, i ^ 1) for i in range(count)])
    unit = jnp.exp(jnp.min(tables[-1]) * 0.0)
    got = got * unit
    half = got.shape[-1] // 2
    others = [got[..., :half], got[..., half:]]
    return keep_parts, others, [way.upper for way in ways]


def block_carried_grads(write_map, value_scale, decayed_vals, decayed_cot, carried, local_grads):
    local_values, local_write, local_read = local_grads
    (state_mine, adjoint_mine), (state_other, adjoint_other), (state_upper, adjoint_upper) = carried

    def rows_times(coeffs, mine, other, upper):
        return jnp.einsum(
            "iq,nq->in", take_half(coeffs, upper), mine.astype(jnp.bfloat16), preferred_element_type=jnp.float32
        ) + jnp.einsum(
            "iq,nq->in", take_half(coeffs, ~upper), other.astype(jnp.bfloat16), preferred_element_type=jnp.float32
        )

    grad_read = local_read + rows_times(decayed_cot, state_mine, state_other, state_upper)
    grad_write = local_write + rows_times(decayed_vals, adjoint_mine, adjoint_other, adjoint_upper)
    term_mine = jnp.einsum(
        "jn,nq->jq", write_map, adjoint_mine.astype(jnp.bfloat16), preferred_element_type=jnp.float32
    )
    term_other = jnp.einsum(
        "jn,nq->jq", write_map, adjoint_other.astype(jnp.bfloat16), preferred_element_type=jnp.float32
    )
    carried_term = join_halves(term_mine, term_other, adjoint_upper)
    grad_values = local_values + value_scale * carried_term
    return (
        grad_values.astype(jnp.bfloat16),
        grad_write.astype(jnp.bfloat16),
        grad_read.astype(jnp.bfloat16),
    )


def local(token_values, cotangent, write_coeffs, read_coeffs, decay_codes, skip_gain):
    seq_len = token_values.shape[1] * lax.axis_size("ctx")
    factor = 0.25 / seq_len
    prepare = jax.vmap(functools.partial(block_states, factor=factor))
    within, totals, value_scale, decayed_vals, decayed_cot, fwd_state, adj_state, skip_parts = prepare(
        token_values, cotangent, write_coeffs, read_coeffs, decay_codes
    )
    position = lax.axis_index("ctx")
    count = lax.axis_size("ctx")
    tables = jax.vmap(gather_totals, (0, 0, None, None))(totals, skip_parts, position, count)
    grad_skip = jnp.sum(tables[-1][:, count], axis=0)
    for bit in range(lax.axis_size("dp").bit_length() - 1):
        grad_skip = grad_skip + lax.ppermute(grad_skip, "dp", xor_pairs(lax.axis_size("dp"), bit))
    head_width = token_values.shape[2] // decay_codes.shape[2]
    carried = jax.vmap(carried_pair, (0, 0, 0, None, None, None))(
        tables, fwd_state, adj_state, position, count, head_width
    )
    local_grads = jax.vmap(block_local_grads, (0, 0, 0, 0, 0, None))(
        token_values, cotangent, write_coeffs, read_coeffs, within, skip_gain
    )
    grad_values, grad_write, grad_read = jax.vmap(block_carried_grads)(
        write_coeffs, value_scale, decayed_vals, decayed_cot, carried, local_grads
    )
    return (grad_values, grad_write, grad_read, grad_skip)


def solution(mesh):
    in_specs = (
        P("dp", "ctx", None),
        P("dp", "ctx", None),
        P("dp", "ctx", None),
        P("dp", "ctx", None),
        P("dp", "ctx", None),
        P(),
    )
    out_specs = (P("dp", "ctx", None), P("dp", "ctx", None), P("dp", "ctx", None), P())
    return jax.shard_map(local, mesh=mesh, in_specs=in_specs, out_specs=out_specs, check_vma=False)
```

```python
import functools

import jax
import jax.numpy as jnp
from jax import lax
from jax.sharding import PartitionSpec as P


def spread_heads(per_head, width):
    return jnp.repeat(per_head, width, axis=-1)


def block_states(values, cotan, write_map, read_map, codes, factor):
    head_count = codes.shape[1]
    head_width = values.shape[1] // head_count
    log_decay = -codes.astype(jnp.float32) * factor
    within = jnp.cumsum(log_decay, axis=0)
    totals = within[-1]
    value_scale = spread_heads(jnp.exp(totals - within), head_width)
    cot_scale = spread_heads(jnp.exp(within), head_width)
    decayed_vals = (values.astype(jnp.float32) * value_scale).astype(jnp.bfloat16)
    decayed_cot = (cotan.astype(jnp.float32) * cot_scale).astype(jnp.bfloat16)
    fwd_state = jnp.einsum("jn,jq->nq", write_map, decayed_vals, preferred_element_type=jnp.float32)
    adj_state = jnp.einsum("in,iq->nq", read_map, decayed_cot, preferred_element_type=jnp.float32)
    skip_part = jnp.sum(
        (values.astype(jnp.float32) * cotan.astype(jnp.float32)).reshape(
            values.shape[0], head_count, head_width
        ),
        axis=(0, 2),
    )
    return within, totals, value_scale, decayed_vals, decayed_cot, fwd_state, adj_state, skip_part


def block_local_grads(values, cotan, write_map, read_map, within, skip_gain):
    token_count = values.shape[0]
    head_count = skip_gain.shape[0]
    head_width = values.shape[1] // head_count
    vals_three = values.reshape(token_count, head_count, head_width)
    cot_three = cotan.reshape(token_count, head_count, head_width)
    rows = jnp.arange(token_count)
    causal = (rows[:, None] >= rows[None, :])[None]
    lead = within.T
    spread = lead[:, :, None] - lead[:, None, :]
    decay_matrix = jnp.where(causal, jnp.exp(jnp.where(causal, spread, 0.0)), 0.0)
    products = jnp.einsum("ihp,jhp->hij", cot_three, vals_three, preferred_element_type=jnp.float32)
    read_weights = (products * decay_matrix).astype(jnp.bfloat16)
    gram = jnp.einsum("in,jn->ij", read_map, write_map, preferred_element_type=jnp.float32)
    value_weights = (gram[None] * decay_matrix).astype(jnp.bfloat16)
    grad_read = jnp.einsum("hij,jn->in", read_weights, write_map, preferred_element_type=jnp.float32)
    grad_write = jnp.einsum("hij,in->jn", read_weights, read_map, preferred_element_type=jnp.float32)
    grad_values = jnp.einsum(
        "hij,ihp->jhp", value_weights, cot_three, preferred_element_type=jnp.float32
    ) + skip_gain[None, :, None] * cot_three.astype(jnp.float32)
    return grad_values.reshape(token_count, head_count * head_width), grad_write, grad_read


def xor_pairs(count, bit):
    return [(i, i ^ (1 << bit)) for i in range(count)]


def gather_totals(totals, skip_part, position, count):
    rows = jnp.arange(count)[:, None]
    table = jnp.concatenate([jnp.where(rows == position, totals[None, :], 0.0), skip_part[None, :]], 0)
    tables = [table]
    for bit in range(count.bit_length() - 1):
        table = table + lax.ppermute(table, "ctx", xor_pairs(count, bit))
        tables.append(table)
    return tables


def take_half(array, upper):
    half = array.shape[-1] // 2
    return jnp.where(upper, array[..., half:], array[..., :half])


def join_halves(mine, other, upper):
    return jnp.where(upper, jnp.concatenate([other, mine], -1), jnp.concatenate([mine, other], -1))


class Direction:
    def __init__(self, tables, position, count, reverse, head_width):
        self.tables = tables
        self.count = count
        self.reverse = reverse
        self.head_width = head_width
        self.index = count - 1 - position if reverse else position
        self.upper = self.index % 2 == 1
        self.pair = self.index // 2
        self.pyramids = {}

    def actual(self, pairs):
        if self.reverse:
            return [(self.count - 1 - a, self.count - 1 - b) for a, b in pairs]
        return pairs

    def pair_pairs(self, pairs):
        return self.actual([(2 * a + j, 2 * b + j) for a, b in pairs for j in (0, 1)])

    def gain(self, table_index, low_block, size):
        key = (table_index % len(self.tables), size)
        if key not in self.pyramids:
            rows = self.tables[key[0]][: self.count]
            if self.reverse:
                rows = rows[::-1]
            grouped = rows.reshape(self.count // size, size, rows.shape[-1]).sum(axis=1)
            self.pyramids[key] = jnp.exp(grouped)
        full = lax.dynamic_index_in_dim(self.pyramids[key], low_block // size, keepdims=False)
        return spread_heads(take_half(full, self.upper), self.head_width)[..., None, :]


def exchange(payloads, pair_lists):
    return [lax.ppermute(p, "ctx", pairs) for p, pairs in zip(payloads, pair_lists)]


class PairScan:
    def __init__(self, way):
        self.way = way
        self.pair_count = way.count // 2
        self.level_count = self.pair_count.bit_length() - 1
        self.flip = self.level_count >= 2
        pair = way.pair
        self.role = jnp.where(way.upper, pair ^ 1, pair) if self.flip else pair

    def device_pairs(self, pairs, first_level):
        lower = [(2 * a, 2 * b) for a, b in pairs]
        if self.flip and first_level:
            upper = [(2 * b + 1, 2 * a + 1) for a, b in pairs]
        elif self.flip:
            upper = [(2 * (a ^ 1) + 1, 2 * (b ^ 1) + 1) for a, b in pairs]
        else:
            upper = [(2 * a + 1, 2 * b + 1) for a, b in pairs]
        return self.way.actual(lower + upper)

    def pair_gain(self, level, low_pair, pair_span):
        table = min(level + 2, len(self.way.tables) - 1)
        return self.way.gain(table, 2 * low_pair, 2 * pair_span)

    def up_send(self, level):
        span = 1 << level
        pairs = [(a, a + span) for a in range(self.pair_count) if a % (2 * span) == span - 1]
        return self.device_pairs(pairs, level == 0)

    def up_combine(self, level, total, lower):
        span = 1 << level
        if self.flip and level == 0:
            pair = self.way.pair
            kept_upper = self.pair_gain(0, pair ^ 1, 1) * total + lower
            kept_lower = self.pair_gain(0, pair, 1) * lower + total
            return jnp.where(self.way.upper, kept_upper, kept_lower)
        return self.pair_gain(level, self.role - span + 1, span) * lower + total

    def down_send(self, level, prefix, pair_total):
        span = 1 << level
        if self.flip and level == 0:
            pair = self.way.pair
            sent = jnp.where(self.way.upper, self.pair_gain(0, pair, 1) * prefix + pair_total, prefix)
            pairs = [(2 * (a + 1), 2 * a) for a in range(0, self.pair_count, 2)]
            pairs += [(2 * a + 1, 2 * (a + 1) + 1) for a in range(0, self.pair_count, 2)]
            return sent, self.way.actual(pairs)
        pairs = [(a, a - span) for a in range(self.pair_count) if a % (2 * span) == 2 * span - 1]
        return prefix, self.device_pairs(pairs, False)

    def down_combine(self, level, prefix, got, lowers):
        span = 1 << level
        if self.flip and level == 0:
            pair = self.way.pair
            grown = self.pair_gain(self.level_count, pair - 1, 1) * prefix + lowers[0]
            odd = pair % 2 == 1
            return jnp.where(self.way.upper, jnp.where(odd, got, prefix), jnp.where(odd, grown, got))
        if got is not None:
            prefix = prefix + got
        lower_gain = self.pair_gain(self.level_count, self.role - 2 * span + 1, span)
        lower_gain = jnp.where(self.role % (2 * span) == 2 * span - 1, lower_gain, 1.0)
        return lower_gain * prefix + lowers[level]


def pair_scans(ways, pair_totals):
    scans = [PairScan(way) for way in ways]
    level_count = scans[0].level_count
    totals = list(pair_totals)
    lowers = [[] for _ in scans]
    for level in range(level_count):
        got = exchange(totals, [scan.up_send(level) for scan in scans])
        for k, scan in enumerate(scans):
            lowers[k].append(got[k])
            if level < level_count - 1:
                totals[k] = scan.up_combine(level, totals[k], got[k])
    prefixes = [jnp.zeros_like(total) for total in pair_totals]
    for level in reversed(range(level_count)):
        if level < level_count - 1 or (scans[0].flip and level == 0):
            sends = [scan.down_send(level, p, t) for scan, p, t in zip(scans, prefixes, pair_totals)]
            got = exchange([s[0] for s in sends], [s[1] for s in sends])
        else:
            got = [None] * len(scans)
        prefixes = [
            scan.down_combine(level, p, g, low) for scan, p, g, low in zip(scans, prefixes, got, lowers)
        ]
    anchor = lowers[0][0] if level_count else pair_totals[0]
    return prefixes, anchor


def carried_pair(tables, fwd_state, adj_state, position, count, head_width):
    ways = [Direction(tables, position, count, reverse, head_width) for reverse in (False, True)]
    states = [fwd_state, adj_state]
    sent = jnp.concatenate([take_half(s, ~w.upper) for s, w in zip(states, ways)], -1)
    got = lax.ppermute(sent, "ctx", [(i, i ^ 1) for i in range(count)])
    got = [got[..., : got.shape[-1] // 2], got[..., got.shape[-1] // 2 :]]
    lows = []
    totals = []
    for way, state, other in zip(ways, states, got):
        own = take_half(state, way.upper)
        low_block = jnp.where(way.upper, other, own)
        high_block = jnp.where(way.upper, own, other)
        lows.append(low_block)
        totals.append(way.gain(1, 2 * way.pair + 1, 1) * low_block + high_block)
    pair_prefixes, anchor = pair_scans(ways, totals)
    lifted_parts = []
    keep_parts = []
    for way, pair_prefix, low_block in zip(ways, pair_prefixes, lows):
        lifted = way.gain(1, 2 * way.pair, 1) * pair_prefix + low_block
        lifted_parts.append(jnp.where(way.upper, pair_prefix, lifted))
        keep_parts.append(jnp.where(way.upper, lifted, pair_prefix))
    got = lax.ppermute(jnp.concatenate(lifted_parts, -1), "ctx", [(i, i ^ 1) for i in range(count)])
    unit = jnp.exp(jnp.min(tables[-1]) * 0.0)
    got = got * unit
    half = got.shape[-1] // 2
    others = [got[..., :half], got[..., half:]]
    return (keep_parts, others, [way.upper for way in ways]), anchor


def block_carried_grads(write_map, value_scale, decayed_vals, decayed_cot, carried, local_grads):
    local_values, local_write, local_read = local_grads
    (state_mine, adjoint_mine), (state_other, adjoint_other), (state_upper, adjoint_upper) = carried

    def rows_times(coeffs, mine, other, upper):
        return jnp.einsum(
            "iq,nq->in", take_half(coeffs, upper), mine.astype(jnp.bfloat16), preferred_element_type=jnp.float32
        ) + jnp.einsum(
            "iq,nq->in", take_half(coeffs, ~upper), other.astype(jnp.bfloat16), preferred_element_type=jnp.float32
        )

    grad_read = local_read + rows_times(decayed_cot, state_mine, state_other, state_upper)
    grad_write = local_write + rows_times(decayed_vals, adjoint_mine, adjoint_other, adjoint_upper)
    term_mine = jnp.einsum(
        "jn,nq->jq", write_map, adjoint_mine.astype(jnp.bfloat16), preferred_element_type=jnp.float32
    )
    term_other = jnp.einsum(
        "jn,nq->jq", write_map, adjoint_other.astype(jnp.bfloat16), preferred_element_type=jnp.float32
    )
    carried_term = join_halves(term_mine, term_other, adjoint_upper)
    grad_values = local_values + value_scale * carried_term
    return (
        grad_values.astype(jnp.bfloat16),
        grad_write.astype(jnp.bfloat16),
        grad_read.astype(jnp.bfloat16),
    )


def local(token_values, cotangent, write_coeffs, read_coeffs, decay_codes, skip_gain):
    seq_len = token_values.shape[1] * lax.axis_size("ctx")
    factor = 0.25 / seq_len
    prepare = jax.vmap(functools.partial(block_states, factor=factor))
    within, totals, value_scale, decayed_vals, decayed_cot, fwd_state, adj_state, skip_parts = prepare(
        token_values, cotangent, write_coeffs, read_coeffs, decay_codes
    )
    position = lax.axis_index("ctx")
    count = lax.axis_size("ctx")
    tables = jax.vmap(gather_totals, (0, 0, None, None))(totals, skip_parts, position, count)
    grad_skip = jnp.sum(tables[-1][:, count], axis=0)
    for bit in range(lax.axis_size("dp").bit_length() - 1):
        grad_skip = grad_skip + lax.ppermute(grad_skip, "dp", xor_pairs(lax.axis_size("dp"), bit))
    head_width = token_values.shape[2] // decay_codes.shape[2]
    carried, anchor = jax.vmap(carried_pair, (0, 0, 0, None, None, None))(
        tables, fwd_state, adj_state, position, count, head_width
    )
    local_inputs, _ = lax.optimization_barrier(
        ((token_values, cotangent, write_coeffs, read_coeffs, within), anchor)
    )
    local_grads = jax.vmap(block_local_grads, (0, 0, 0, 0, 0, None))(*local_inputs, skip_gain)
    grad_values, grad_write, grad_read = jax.vmap(block_carried_grads)(
        write_coeffs, value_scale, decayed_vals, decayed_cot, carried, local_grads
    )
    return (grad_values, grad_write, grad_read, grad_skip)


def solution(mesh):
    in_specs = (
        P("dp", "ctx", None),
        P("dp", "ctx", None),
        P("dp", "ctx", None),
        P("dp", "ctx", None),
        P("dp", "ctx", None),
        P(),
    )
    out_specs = (P("dp", "ctx", None), P("dp", "ctx", None), P("dp", "ctx", None), P())
    return jax.shard_map(local, mesh=mesh, in_specs=in_specs, out_specs=out_specs, check_vma=False)
```

```python
import functools

import jax
import jax.numpy as jnp
from jax import lax
from jax.sharding import PartitionSpec as P


def spread_heads(per_head, width):
    return jnp.repeat(per_head, width, axis=-1)


def block_states(values, cotan, write_map, read_map, codes, factor):
    head_count = codes.shape[1]
    head_width = values.shape[1] // head_count
    log_decay = -codes.astype(jnp.float32) * factor
    within = jnp.cumsum(log_decay, axis=0)
    totals = within[-1]
    value_scale = spread_heads(jnp.exp(totals - within), head_width)
    cot_scale = spread_heads(jnp.exp(within), head_width)
    decayed_vals = (values.astype(jnp.float32) * value_scale).astype(jnp.bfloat16)
    decayed_cot = (cotan.astype(jnp.float32) * cot_scale).astype(jnp.bfloat16)
    fwd_state = jnp.einsum("jn,jq->nq", write_map, decayed_vals, preferred_element_type=jnp.float32)
    adj_state = jnp.einsum("in,iq->nq", read_map, decayed_cot, preferred_element_type=jnp.float32)
    skip_part = jnp.sum(
        (values.astype(jnp.float32) * cotan.astype(jnp.float32)).reshape(
            values.shape[0], head_count, head_width
        ),
        axis=(0, 2),
    )
    return within, totals, value_scale, decayed_vals, decayed_cot, fwd_state, adj_state, skip_part


def block_local_grads(values, cotan, write_map, read_map, within, skip_gain):
    token_count = values.shape[0]
    head_count = skip_gain.shape[0]
    head_width = values.shape[1] // head_count
    vals_three = values.reshape(token_count, head_count, head_width)
    cot_three = cotan.reshape(token_count, head_count, head_width)
    rows = jnp.arange(token_count)
    causal = (rows[:, None] >= rows[None, :])[None]
    lead = within.T
    spread = lead[:, :, None] - lead[:, None, :]
    decay_matrix = jnp.where(causal, jnp.exp(jnp.where(causal, spread, 0.0)), 0.0)
    products = jnp.einsum("ihp,jhp->hij", cot_three, vals_three, preferred_element_type=jnp.float32)
    read_weights = (products * decay_matrix).astype(jnp.bfloat16)
    gram = jnp.einsum("in,jn->ij", read_map, write_map, preferred_element_type=jnp.float32)
    value_weights = (gram[None] * decay_matrix).astype(jnp.bfloat16)
    grad_read = jnp.einsum("hij,jn->in", read_weights, write_map, preferred_element_type=jnp.float32)
    grad_write = jnp.einsum("hij,in->jn", read_weights, read_map, preferred_element_type=jnp.float32)
    grad_values = jnp.einsum(
        "hij,ihp->jhp", value_weights, cot_three, preferred_element_type=jnp.float32
    ) + skip_gain[None, :, None] * cot_three.astype(jnp.float32)
    return grad_values.reshape(token_count, head_count * head_width), grad_write, grad_read


def xor_pairs(count, bit):
    return [(i, i ^ (1 << bit)) for i in range(count)]


def all_sum(value, axis):
    size = lax.axis_size(axis)
    for bit in range(size.bit_length() - 1):
        value = value + lax.ppermute(value, axis, xor_pairs(size, bit))
    return value


def take_half(array, upper):
    half = array.shape[-1] // 2
    return jnp.where(upper, array[..., half:], array[..., :half])


def join_halves(mine, other, upper):
    return jnp.where(upper, jnp.concatenate([other, mine], -1), jnp.concatenate([mine, other], -1))


class Direction:
    def __init__(self, position, count, reverse):
        self.count = count
        self.reverse = reverse
        self.index = count - 1 - position if reverse else position
        self.upper = self.index % 2 == 1
        self.pair = self.index // 2

    def actual(self, pairs):
        if self.reverse:
            return [(self.count - 1 - a, self.count - 1 - b) for a, b in pairs]
        return pairs


def exchange(payloads, pair_lists):
    return [lax.ppermute(p, "ctx", pairs) for p, pairs in zip(payloads, pair_lists)]


def chain(earlier, later):
    rows = lax.broadcasted_iota(jnp.int32, earlier.shape, earlier.ndim - 2)
    gain = jnp.exp(later[..., -1:, :])
    return jnp.where(rows < earlier.shape[-2] - 1, gain * earlier + later, earlier + later)


def lift(summary, prefix):
    return jnp.exp(summary[..., -1:, :]) * prefix + summary[..., :-1, :]


class PairScan:
    def __init__(self, way):
        self.way = way
        self.pair_count = way.count // 2
        self.level_count = self.pair_count.bit_length() - 1
        self.flip = self.level_count >= 2

    def device_pairs(self, pairs, first_level):
        lower = [(2 * a, 2 * b) for a, b in pairs]
        if self.flip and first_level:
            upper = [(2 * b + 1, 2 * a + 1) for a, b in pairs]
        elif self.flip:
            upper = [(2 * (a ^ 1) + 1, 2 * (b ^ 1) + 1) for a, b in pairs]
        else:
            upper = [(2 * a + 1, 2 * b + 1) for a, b in pairs]
        return self.way.actual(lower + upper)

    def up_send(self, level):
        span = 1 << level
        pairs = [(a, a + span) for a in range(self.pair_count) if a % (2 * span) == span - 1]
        return self.device_pairs(pairs, level == 0)

    def up_combine(self, level, total, lower):
        if self.flip and level == 0:
            return jnp.where(self.way.upper, chain(total, lower), chain(lower, total))
        return chain(lower, total)

    def down_send(self, level, prefix, pair_total):
        span = 1 << level
        if self.flip and level == 0:
            sent = jnp.where(self.way.upper, lift(pair_total, prefix), prefix)
            pairs = [(2 * (a + 1), 2 * a) for a in range(0, self.pair_count, 2)]
            pairs += [(2 * a + 1, 2 * (a + 1) + 1) for a in range(0, self.pair_count, 2)]
            return sent, self.way.actual(pairs)
        pairs = [(a, a - span) for a in range(self.pair_count) if a % (2 * span) == 2 * span - 1]
        return prefix, self.device_pairs(pairs, False)

    def down_combine(self, level, prefix, got, lowers):
        if self.flip and level == 0:
            odd = self.way.pair % 2 == 1
            grown = lift(lowers[0], prefix)
            return jnp.where(self.way.upper, jnp.where(odd, got, prefix), jnp.where(odd, grown, got))
        if got is not None:
            prefix = prefix + got
        return lift(lowers[level], prefix)


def pair_scans(ways, pair_totals):
    scans = [PairScan(way) for way in ways]
    level_count = scans[0].level_count
    totals = list(pair_totals)
    lowers = [[] for _ in scans]
    for level in range(level_count):
        got = exchange(totals, [scan.up_send(level) for scan in scans])
        for k, scan in enumerate(scans):
            lowers[k].append(got[k])
            if level < level_count - 1:
                totals[k] = scan.up_combine(level, totals[k], got[k])
    prefixes = [jnp.zeros_like(total[..., :-1, :]) for total in pair_totals]
    for level in reversed(range(level_count)):
        if level < level_count - 1 or (scans[0].flip and level == 0):
            sends = [scan.down_send(level, p, t) for scan, p, t in zip(scans, prefixes, pair_totals)]
            got = exchange([s[0] for s in sends], [s[1] for s in sends])
        else:
            got = [None] * len(scans)
        prefixes = [
            scan.down_combine(level, p, g, low) for scan, p, g, low in zip(scans, prefixes, got, lowers)
        ]
    anchor = lowers[0][0] if level_count else pair_totals[0]
    return prefixes, anchor


def carried_pair(log_totals, fwd_state, adj_state, position, count):
    ways = [Direction(position, count, reverse) for reverse in (False, True)]
    summaries = [jnp.concatenate([s, log_totals[None, :]], 0) for s in (fwd_state, adj_state)]
    sent = jnp.concatenate([take_half(s, ~w.upper) for s, w in zip(summaries, ways)], -1)
    got = lax.ppermute(sent, "ctx", [(i, i ^ 1) for i in range(count)])
    got = [got[..., : got.shape[-1] // 2], got[..., got.shape[-1] // 2 :]]
    lows = []
    totals = []
    for way, summary, other in zip(ways, summaries, got):
        own = take_half(summary, way.upper)
        low_block = jnp.where(way.upper, other, own)
        high_block = jnp.where(way.upper, own, other)
        lows.append(low_block)
        totals.append(chain(low_block, high_block))
    pair_prefixes, anchor = pair_scans(ways, totals)
    lifted_parts = []
    keep_parts = []
    for way, pair_prefix, low_block in zip(ways, pair_prefixes, lows):
        lifted = lift(low_block, pair_prefix)
        lifted_parts.append(jnp.where(way.upper, pair_prefix, lifted))
        keep_parts.append(jnp.where(way.upper, lifted, pair_prefix))
    got = lax.ppermute(jnp.concatenate(lifted_parts, -1), "ctx", [(i, i ^ 1) for i in range(count)])
    unit = jnp.exp(jnp.min(log_totals) * 0.0)
    got = got * unit
    half = got.shape[-1] // 2
    others = [got[..., :half], got[..., half:]]
    return (keep_parts, others, [way.upper for way in ways]), anchor


def block_carried_grads(write_map, value_scale, decayed_vals, decayed_cot, carried, local_grads):
    local_values, local_write, local_read = local_grads
    (state_mine, adjoint_mine), (state_other, adjoint_other), (state_upper, adjoint_upper) = carried

    def rows_times(coeffs, mine, other, upper):
        return jnp.einsum(
            "iq,nq->in", take_half(coeffs, upper), mine.astype(jnp.bfloat16), preferred_element_type=jnp.float32
        ) + jnp.einsum(
            "iq,nq->in", take_half(coeffs, ~upper), other.astype(jnp.bfloat16), preferred_element_type=jnp.float32
        )

    grad_read = local_read + rows_times(decayed_cot, state_mine, state_other, state_upper)
    grad_write = local_write + rows_times(decayed_vals, adjoint_mine, adjoint_other, adjoint_upper)
    term_mine = jnp.einsum(
        "jn,nq->jq", write_map, adjoint_mine.astype(jnp.bfloat16), preferred_element_type=jnp.float32
    )
    term_other = jnp.einsum(
        "jn,nq->jq", write_map, adjoint_other.astype(jnp.bfloat16), preferred_element_type=jnp.float32
    )
    carried_term = join_halves(term_mine, term_other, adjoint_upper)
    grad_values = local_values + value_scale * carried_term
    return (
        grad_values.astype(jnp.bfloat16),
        grad_write.astype(jnp.bfloat16),
        grad_read.astype(jnp.bfloat16),
    )


def local(token_values, cotangent, write_coeffs, read_coeffs, decay_codes, skip_gain):
    seq_len = token_values.shape[1] * lax.axis_size("ctx")
    factor = 0.25 / seq_len
    prepare = jax.vmap(functools.partial(block_states, factor=factor))
    within, totals, value_scale, decayed_vals, decayed_cot, fwd_state, adj_state, skip_parts = prepare(
        token_values, cotangent, write_coeffs, read_coeffs, decay_codes
    )
    position = lax.axis_index("ctx")
    count = lax.axis_size("ctx")
    grad_skip = all_sum(all_sum(jnp.sum(skip_parts, axis=0), "ctx"), "dp")
    head_width = token_values.shape[2] // decay_codes.shape[2]
    carried, anchor = jax.vmap(carried_pair, (0, 0, 0, None, None))(
        spread_heads(totals, head_width), fwd_state, adj_state, position, count
    )
    local_inputs, _ = lax.optimization_barrier(
        ((token_values, cotangent, write_coeffs, read_coeffs, within), anchor)
    )
    local_grads = jax.vmap(block_local_grads, (0, 0, 0, 0, 0, None))(*local_inputs, skip_gain)
    grad_values, grad_write, grad_read = jax.vmap(block_carried_grads)(
        write_coeffs, value_scale, decayed_vals, decayed_cot, carried, local_grads
    )
    return (grad_values, grad_write, grad_read, grad_skip)


def solution(mesh):
    in_specs = (
        P("dp", "ctx", None),
        P("dp", "ctx", None),
        P("dp", "ctx", None),
        P("dp", "ctx", None),
        P("dp", "ctx", None),
        P(),
    )
    out_specs = (P("dp", "ctx", None), P("dp", "ctx", None), P("dp", "ctx", None), P())
    return jax.shard_map(local, mesh=mesh, in_specs=in_specs, out_specs=out_specs, check_vma=False)
```

```python
import functools

import jax
import jax.numpy as jnp
from jax import lax
from jax.sharding import PartitionSpec as P


def spread_heads(per_head, width):
    return jnp.repeat(per_head, width, axis=-1)


def block_states(values, cotan, write_map, read_map, codes, factor):
    head_count = codes.shape[1]
    head_width = values.shape[1] // head_count
    log_decay = -codes.astype(jnp.float32) * factor
    within = jnp.cumsum(log_decay, axis=0)
    totals = within[-1]
    value_scale = spread_heads(jnp.exp(totals - within), head_width)
    cot_scale = spread_heads(jnp.exp(within), head_width)
    decayed_vals = (values.astype(jnp.float32) * value_scale).astype(jnp.bfloat16)
    decayed_cot = (cotan.astype(jnp.float32) * cot_scale).astype(jnp.bfloat16)
    fwd_state = jnp.einsum("jn,jq->nq", write_map, decayed_vals, preferred_element_type=jnp.float32)
    adj_state = jnp.einsum("in,iq->nq", read_map, decayed_cot, preferred_element_type=jnp.float32)
    skip_part = jnp.sum(
        (values.astype(jnp.float32) * cotan.astype(jnp.float32)).reshape(
            values.shape[0], head_count, head_width
        ),
        axis=(0, 2),
    )
    return within, totals, value_scale, decayed_vals, decayed_cot, fwd_state, adj_state, skip_part


def block_local_grads(values, cotan, write_map, read_map, within, skip_gain):
    token_count = values.shape[0]
    head_count = skip_gain.shape[0]
    head_width = values.shape[1] // head_count
    vals_three = values.reshape(token_count, head_count, head_width)
    cot_three = cotan.reshape(token_count, head_count, head_width)
    rows = jnp.arange(token_count)
    causal = (rows[:, None] >= rows[None, :])[None]
    lead = within.T
    spread = lead[:, :, None] - lead[:, None, :]
    decay_matrix = jnp.where(causal, jnp.exp(jnp.where(causal, spread, 0.0)), 0.0)
    products = jnp.einsum("ihp,jhp->hij", cot_three, vals_three, preferred_element_type=jnp.float32)
    read_weights = (products * decay_matrix).astype(jnp.bfloat16)
    gram = jnp.einsum("in,jn->ij", read_map, write_map, preferred_element_type=jnp.float32)
    value_weights = (gram[None] * decay_matrix).astype(jnp.bfloat16)
    grad_read = jnp.einsum("hij,jn->in", read_weights, write_map, preferred_element_type=jnp.float32)
    grad_write = jnp.einsum("hij,in->jn", read_weights, read_map, preferred_element_type=jnp.float32)
    grad_values = jnp.einsum(
        "hij,ihp->jhp", value_weights, cot_three, preferred_element_type=jnp.float32
    ) + skip_gain[None, :, None] * cot_three.astype(jnp.float32)
    return grad_values.reshape(token_count, head_count * head_width), grad_write, grad_read


def xor_pairs(count, bit):
    return [(i, i ^ (1 << bit)) for i in range(count)]


def gather_totals(totals, skip_part, position, count):
    rows = jnp.arange(count)[:, None]
    table = jnp.concatenate([jnp.where(rows == position, totals[None, :], 0.0), skip_part[None, :]], 0)
    return [table]


def extend_totals(tables, count, start_bit, stop_bit):
    for bit in range(start_bit, min(stop_bit, count.bit_length() - 1)):
        tables.append(tables[-1] + lax.ppermute(tables[-1], "ctx", xor_pairs(count, bit)))


def take_half(array, upper):
    half = array.shape[-1] // 2
    return jnp.where(upper, array[..., half:], array[..., :half])


def join_halves(mine, other, upper):
    return jnp.where(upper, jnp.concatenate([other, mine], -1), jnp.concatenate([mine, other], -1))


class Direction:
    def __init__(self, tables, position, count, reverse, head_width):
        self.tables = tables
        self.count = count
        self.reverse = reverse
        self.head_width = head_width
        self.index = count - 1 - position if reverse else position
        self.upper = self.index % 2 == 1
        self.pair = self.index // 2
        self.pyramids = {}

    def actual(self, pairs):
        if self.reverse:
            return [(self.count - 1 - a, self.count - 1 - b) for a, b in pairs]
        return pairs

    def pair_pairs(self, pairs):
        return self.actual([(2 * a + j, 2 * b + j) for a, b in pairs for j in (0, 1)])

    def gain(self, table_index, low_block, size):
        key = (table_index % len(self.tables), size)
        if key not in self.pyramids:
            rows = self.tables[key[0]][: self.count]
            if self.reverse:
                rows = rows[::-1]
            grouped = rows.reshape(self.count // size, size, rows.shape[-1]).sum(axis=1)
            self.pyramids[key] = jnp.exp(grouped)
        full = lax.dynamic_index_in_dim(self.pyramids[key], low_block // size, keepdims=False)
        return spread_heads(take_half(full, self.upper), self.head_width)[..., None, :]


def exchange(payloads, pair_lists):
    return [lax.ppermute(p, "ctx", pairs) for p, pairs in zip(payloads, pair_lists)]


class PairScan:
    def __init__(self, way):
        self.way = way
        self.pair_count = way.count // 2
        self.level_count = self.pair_count.bit_length() - 1
        self.flip = self.level_count >= 2
        pair = way.pair
        self.role = jnp.where(way.upper, pair ^ 1, pair) if self.flip else pair

    def device_pairs(self, pairs, first_level):
        lower = [(2 * a, 2 * b) for a, b in pairs]
        if self.flip and first_level:
            upper = [(2 * b + 1, 2 * a + 1) for a, b in pairs]
        elif self.flip:
            upper = [(2 * (a ^ 1) + 1, 2 * (b ^ 1) + 1) for a, b in pairs]
        else:
            upper = [(2 * a + 1, 2 * b + 1) for a, b in pairs]
        return self.way.actual(lower + upper)

    def pair_gain(self, level, low_pair, pair_span):
        table = min(level + 2, len(self.way.tables) - 1)
        return self.way.gain(table, 2 * low_pair, 2 * pair_span)

    def up_send(self, level):
        span = 1 << level
        pairs = [(a, a + span) for a in range(self.pair_count) if a % (2 * span) == span - 1]
        return self.device_pairs(pairs, level == 0)

    def up_combine(self, level, total, lower):
        span = 1 << level
        if self.flip and level == 0:
            pair = self.way.pair
            kept_upper = self.pair_gain(0, pair ^ 1, 1) * total + lower
            kept_lower = self.pair_gain(0, pair, 1) * lower + total
            return jnp.where(self.way.upper, kept_upper, kept_lower)
        return self.pair_gain(level, self.role - span + 1, span) * lower + total

    def down_send(self, level, prefix, pair_total):
        span = 1 << level
        if self.flip and level == 0:
            pair = self.way.pair
            sent = jnp.where(self.way.upper, self.pair_gain(0, pair, 1) * prefix + pair_total, prefix)
            pairs = [(2 * (a + 1), 2 * a) for a in range(0, self.pair_count, 2)]
            pairs += [(2 * a + 1, 2 * (a + 1) + 1) for a in range(0, self.pair_count, 2)]
            return sent, self.way.actual(pairs)
        pairs = [(a, a - span) for a in range(self.pair_count) if a % (2 * span) == 2 * span - 1]
        return prefix, self.device_pairs(pairs, False)

    def down_combine(self, level, prefix, got, lowers):
        span = 1 << level
        if self.flip and level == 0:
            pair = self.way.pair
            grown = self.pair_gain(self.level_count, pair - 1, 1) * prefix + lowers[0]
            odd = pair % 2 == 1
            return jnp.where(self.way.upper, jnp.where(odd, got, prefix), jnp.where(odd, grown, got))
        if got is not None:
            prefix = prefix + got
        lower_gain = self.pair_gain(self.level_count, self.role - 2 * span + 1, span)
        lower_gain = jnp.where(self.role % (2 * span) == 2 * span - 1, lower_gain, 1.0)
        return lower_gain * prefix + lowers[level]


def pair_scans(ways, pair_totals):
    scans = [PairScan(way) for way in ways]
    level_count = scans[0].level_count
    totals = list(pair_totals)
    lowers = [[] for _ in scans]
    for level in range(level_count):
        got = exchange(totals, [scan.up_send(level) for scan in scans])
        for k, scan in enumerate(scans):
            lowers[k].append(got[k])
            if level < level_count - 1:
                totals[k] = scan.up_combine(level, totals[k], got[k])
    prefixes = [jnp.zeros_like(total) for total in pair_totals]
    for level in reversed(range(level_count)):
        if level < level_count - 1 or (scans[0].flip and level == 0):
            sends = [scan.down_send(level, p, t) for scan, p, t in zip(scans, prefixes, pair_totals)]
            got = exchange([s[0] for s in sends], [s[1] for s in sends])
        else:
            got = [None] * len(scans)
        prefixes = [
            scan.down_combine(level, p, g, low) for scan, p, g, low in zip(scans, prefixes, got, lowers)
        ]
    anchor = lowers[0][0] if level_count else pair_totals[0]
    return prefixes, anchor


def carried_pair(tables, fwd_state, adj_state, position, count, head_width):
    ways = [Direction(tables, position, count, reverse, head_width) for reverse in (False, True)]
    states = [fwd_state, adj_state]
    sent = jnp.concatenate([take_half(s, ~w.upper) for s, w in zip(states, ways)], -1)
    got = lax.ppermute(sent, "ctx", [(i, i ^ 1) for i in range(count)])
    got = [got[..., : got.shape[-1] // 2], got[..., got.shape[-1] // 2 :]]
    lows = []
    totals = []
    extend_totals(tables, count, 0, 1)
    for way, state, other in zip(ways, states, got):
        own = take_half(state, way.upper)
        low_block = jnp.where(way.upper, other, own)
        high_block = jnp.where(way.upper, own, other)
        lows.append(low_block)
        totals.append(way.gain(1, 2 * way.pair + 1, 1) * low_block + high_block)
    tables[-1], _ = lax.optimization_barrier((tables[-1], totals))
    extend_totals(tables, count, 1, count.bit_length())
    pair_prefixes, anchor = pair_scans(ways, totals)
    lifted_parts = []
    keep_parts = []
    for way, pair_prefix, low_block in zip(ways, pair_prefixes, lows):
        lifted = way.gain(1, 2 * way.pair, 1) * pair_prefix + low_block
        lifted_parts.append(jnp.where(way.upper, pair_prefix, lifted))
        keep_parts.append(jnp.where(way.upper, lifted, pair_prefix))
    got = lax.ppermute(jnp.concatenate(lifted_parts, -1), "ctx", [(i, i ^ 1) for i in range(count)])
    unit = jnp.exp(jnp.min(tables[-1]) * 0.0)
    got = got * unit
    half = got.shape[-1] // 2
    others = [got[..., :half], got[..., half:]]
    return (keep_parts, others, [way.upper for way in ways]), anchor, tables[-1]


def block_carried_grads(write_map, value_scale, decayed_vals, decayed_cot, carried, local_grads):
    local_values, local_write, local_read = local_grads
    (state_mine, adjoint_mine), (state_other, adjoint_other), (state_upper, adjoint_upper) = carried

    def rows_times(coeffs, mine, other, upper):
        return jnp.einsum(
            "iq,nq->in", take_half(coeffs, upper), mine.astype(jnp.bfloat16), preferred_element_type=jnp.float32
        ) + jnp.einsum(
            "iq,nq->in", take_half(coeffs, ~upper), other.astype(jnp.bfloat16), preferred_element_type=jnp.float32
        )

    grad_read = local_read + rows_times(decayed_cot, state_mine, state_other, state_upper)
    grad_write = local_write + rows_times(decayed_vals, adjoint_mine, adjoint_other, adjoint_upper)
    term_mine = jnp.einsum(
        "jn,nq->jq", write_map, adjoint_mine.astype(jnp.bfloat16), preferred_element_type=jnp.float32
    )
    term_other = jnp.einsum(
        "jn,nq->jq", write_map, adjoint_other.astype(jnp.bfloat16), preferred_element_type=jnp.float32
    )
    carried_term = join_halves(term_mine, term_other, adjoint_upper)
    grad_values = local_values + value_scale * carried_term
    return (
        grad_values.astype(jnp.bfloat16),
        grad_write.astype(jnp.bfloat16),
        grad_read.astype(jnp.bfloat16),
    )


def local(token_values, cotangent, write_coeffs, read_coeffs, decay_codes, skip_gain):
    seq_len = token_values.shape[1] * lax.axis_size("ctx")
    factor = 0.25 / seq_len
    prepare = jax.vmap(functools.partial(block_states, factor=factor))
    within, totals, value_scale, decayed_vals, decayed_cot, fwd_state, adj_state, skip_parts = prepare(
        token_values, cotangent, write_coeffs, read_coeffs, decay_codes
    )
    position = lax.axis_index("ctx")
    count = lax.axis_size("ctx")
    tables = jax.vmap(gather_totals, (0, 0, None, None))(totals, skip_parts, position, count)
    head_width = token_values.shape[2] // decay_codes.shape[2]
    carried, anchor, final_table = jax.vmap(carried_pair, (0, 0, 0, None, None, None))(
        tables, fwd_state, adj_state, position, count, head_width
    )
    grad_skip = jnp.sum(final_table[:, count], axis=0)
    for bit in range(lax.axis_size("dp").bit_length() - 1):
        grad_skip = grad_skip + lax.ppermute(grad_skip, "dp", xor_pairs(lax.axis_size("dp"), bit))
    local_inputs, _ = lax.optimization_barrier(
        ((token_values, cotangent, write_coeffs, read_coeffs, within), anchor)
    )
    local_grads = jax.vmap(block_local_grads, (0, 0, 0, 0, 0, None))(*local_inputs, skip_gain)
    grad_values, grad_write, grad_read = jax.vmap(block_carried_grads)(
        write_coeffs, value_scale, decayed_vals, decayed_cot, carried, local_grads
    )
    return (grad_values, grad_write, grad_read, grad_skip)


def solution(mesh):
    in_specs = (
        P("dp", "ctx", None),
        P("dp", "ctx", None),
        P("dp", "ctx", None),
        P("dp", "ctx", None),
        P("dp", "ctx", None),
        P(),
    )
    out_specs = (P("dp", "ctx", None), P("dp", "ctx", None), P("dp", "ctx", None), P())
    return jax.shard_map(local, mesh=mesh, in_specs=in_specs, out_specs=out_specs, check_vma=False)
```

```python
import functools

import jax
import jax.numpy as jnp
from jax import lax
from jax.sharding import PartitionSpec as P


def spread_heads(per_head, width):
    return jnp.repeat(per_head, width, axis=-1)


def block_states(values, cotan, write_map, read_map, codes, factor):
    head_count = codes.shape[1]
    head_width = values.shape[1] // head_count
    log_decay = -codes.astype(jnp.float32) * factor
    within = jnp.cumsum(log_decay, axis=0)
    totals = within[-1]
    value_scale = spread_heads(jnp.exp(totals - within), head_width)
    cot_scale = spread_heads(jnp.exp(within), head_width)
    decayed_vals = (values.astype(jnp.float32) * value_scale).astype(jnp.bfloat16)
    decayed_cot = (cotan.astype(jnp.float32) * cot_scale).astype(jnp.bfloat16)
    fwd_state = jnp.einsum("jn,jq->nq", write_map, decayed_vals, preferred_element_type=jnp.float32)
    adj_state = jnp.einsum("in,iq->nq", read_map, decayed_cot, preferred_element_type=jnp.float32)
    skip_part = jnp.sum(
        (values.astype(jnp.float32) * cotan.astype(jnp.float32)).reshape(
            values.shape[0], head_count, head_width
        ),
        axis=(0, 2),
    )
    return within, totals, value_scale, decayed_vals, decayed_cot, fwd_state, adj_state, skip_part


def block_local_grads(values, cotan, write_map, read_map, within, skip_gain):
    token_count = values.shape[0]
    head_count = skip_gain.shape[0]
    head_width = values.shape[1] // head_count
    vals_three = values.reshape(token_count, head_count, head_width)
    cot_three = cotan.reshape(token_count, head_count, head_width)
    rows = jnp.arange(token_count)
    causal = (rows[:, None] >= rows[None, :])[None]
    lead = within.T
    spread = lead[:, :, None] - lead[:, None, :]
    decay_matrix = jnp.where(causal, jnp.exp(jnp.where(causal, spread, 0.0)), 0.0)
    products = jnp.einsum("ihp,jhp->hij", cot_three, vals_three, preferred_element_type=jnp.float32)
    read_weights = (products * decay_matrix).astype(jnp.bfloat16)
    gram = jnp.einsum("in,jn->ij", read_map, write_map, preferred_element_type=jnp.float32)
    value_weights = (gram[None] * decay_matrix).astype(jnp.bfloat16)
    grad_read = jnp.einsum("hij,jn->in", read_weights, write_map, preferred_element_type=jnp.float32)
    grad_write = jnp.einsum("hij,in->jn", read_weights, read_map, preferred_element_type=jnp.float32)
    grad_values = jnp.einsum(
        "hij,ihp->jhp", value_weights, cot_three, preferred_element_type=jnp.float32
    ) + skip_gain[None, :, None] * cot_three.astype(jnp.float32)
    return grad_values.reshape(token_count, head_count * head_width), grad_write, grad_read


def xor_pairs(count, bit):
    return [(i, i ^ (1 << bit)) for i in range(count)]


def gather_totals(totals, skip_part, position, count):
    rows = jnp.arange(count)[:, None]
    table = jnp.concatenate([jnp.where(rows == position, totals[None, :], 0.0), skip_part[None, :]], 0)
    return [table]


def extend_totals(tables, count, start_bit, stop_bit):
    for bit in range(start_bit, min(stop_bit, count.bit_length() - 1)):
        tables.append(tables[-1] + lax.ppermute(tables[-1], "ctx", xor_pairs(count, bit)))


def take_half(array, upper):
    half = array.shape[-1] // 2
    return jnp.where(upper, array[..., half:], array[..., :half])


def join_halves(mine, other, upper):
    return jnp.where(upper, jnp.concatenate([other, mine], -1), jnp.concatenate([mine, other], -1))


class Direction:
    def __init__(self, tables, position, count, reverse, head_width):
        self.tables = tables
        self.count = count
        self.reverse = reverse
        self.head_width = head_width
        self.index = count - 1 - position if reverse else position
        self.upper = self.index % 2 == 1
        self.pair = self.index // 2
        self.pyramids = {}

    def actual(self, pairs):
        if self.reverse:
            return [(self.count - 1 - a, self.count - 1 - b) for a, b in pairs]
        return pairs

    def pair_pairs(self, pairs):
        return self.actual([(2 * a + j, 2 * b + j) for a, b in pairs for j in (0, 1)])

    def gain(self, table_index, low_block, size):
        key = (table_index % len(self.tables), size)
        if key not in self.pyramids:
            rows = self.tables[key[0]][: self.count]
            if self.reverse:
                rows = rows[::-1]
            grouped = rows.reshape(self.count // size, size, rows.shape[-1]).sum(axis=1)
            self.pyramids[key] = jnp.exp(grouped)
        full = lax.dynamic_index_in_dim(self.pyramids[key], low_block // size, keepdims=False)
        return spread_heads(take_half(full, self.upper), self.head_width)[..., None, :]


def exchange(payloads, pair_lists):
    return [
        lax.ppermute(p, "ctx", pairs) if pairs else jnp.zeros_like(p) for p, pairs in zip(payloads, pair_lists)
    ]


class PairScan:
    def __init__(self, way):
        self.way = way
        self.pair_count = way.count // 2
        self.level_count = self.pair_count.bit_length() - 1
        self.flip = self.level_count >= 2
        pair = way.pair
        self.role = jnp.where(way.upper, pair ^ 1, pair) if self.flip else pair

    def device_pairs(self, pairs, first_level):
        lower = [(2 * a, 2 * b) for a, b in pairs]
        if self.flip and first_level:
            upper = [(2 * b + 1, 2 * a + 1) for a, b in pairs]
        elif self.flip:
            upper = [(2 * (a ^ 1) + 1, 2 * (b ^ 1) + 1) for a, b in pairs]
        else:
            upper = [(2 * a + 1, 2 * b + 1) for a, b in pairs]
        return self.way.actual(lower + upper)

    def pair_gain(self, level, low_pair, pair_span):
        table = min(level + 2, len(self.way.tables) - 1)
        return self.way.gain(table, 2 * low_pair, 2 * pair_span)

    def up_send(self, level):
        span = 1 << level
        pairs = [(a, a + span) for a in range(self.pair_count) if a % (2 * span) == span - 1]
        return self.device_pairs(pairs, level == 0)

    def up_combine(self, level, total, lower):
        span = 1 << level
        if self.flip and level == 0:
            pair = self.way.pair
            kept_upper = self.pair_gain(0, pair ^ 1, 1) * total + lower
            kept_lower = self.pair_gain(0, pair, 1) * lower + total
            return jnp.where(self.way.upper, kept_upper, kept_lower)
        return self.pair_gain(level, self.role - span + 1, span) * lower + total

    def down_send(self, level, prefix, pair_total):
        span = 1 << level
        if self.flip and level == 0:
            pair = self.way.pair
            sent = jnp.where(self.way.upper, self.pair_gain(0, pair, 1) * prefix + pair_total, prefix)
            pairs = [(2 * (a + 1), 2 * a) for a in range(2, self.pair_count, 2)]
            pairs += [(2 * a + 1, 2 * (a + 1) + 1) for a in range(0, self.pair_count, 2)]
            return sent, self.way.actual(pairs)
        pairs = [(a, a - span) for a in range(2 * span, self.pair_count) if a % (2 * span) == 2 * span - 1]
        return prefix, self.device_pairs(pairs, False)

    def down_combine(self, level, prefix, got, lowers):
        span = 1 << level
        if self.flip and level == 0:
            pair = self.way.pair
            grown = self.pair_gain(self.level_count, pair - 1, 1) * prefix + lowers[0]
            odd = pair % 2 == 1
            return jnp.where(self.way.upper, jnp.where(odd, got, prefix), jnp.where(odd, grown, got))
        if got is not None:
            prefix = prefix + got
        lower_gain = self.pair_gain(self.level_count, self.role - 2 * span + 1, span)
        lower_gain = jnp.where(self.role % (2 * span) == 2 * span - 1, lower_gain, 1.0)
        return lower_gain * prefix + lowers[level]


def pair_scans(ways, pair_totals):
    scans = [PairScan(way) for way in ways]
    level_count = scans[0].level_count
    totals = list(pair_totals)
    lowers = [[] for _ in scans]
    for level in range(level_count):
        got = exchange(totals, [scan.up_send(level) for scan in scans])
        for k, scan in enumerate(scans):
            lowers[k].append(got[k])
            if level < level_count - 1:
                totals[k] = scan.up_combine(level, totals[k], got[k])
    prefixes = [jnp.zeros_like(total) for total in pair_totals]
    for level in reversed(range(level_count)):
        if level < level_count - 1 or (scans[0].flip and level == 0):
            sends = [scan.down_send(level, p, t) for scan, p, t in zip(scans, prefixes, pair_totals)]
            got = exchange([s[0] for s in sends], [s[1] for s in sends])
        else:
            got = [None] * len(scans)
        prefixes = [
            scan.down_combine(level, p, g, low) for scan, p, g, low in zip(scans, prefixes, got, lowers)
        ]
    anchor = lowers[0][0] if level_count else pair_totals[0]
    return prefixes, anchor


def carried_pair(tables, fwd_state, adj_state, position, count, head_width):
    ways = [Direction(tables, position, count, reverse, head_width) for reverse in (False, True)]
    states = [fwd_state, adj_state]
    sent = jnp.concatenate([take_half(s, ~w.upper) for s, w in zip(states, ways)], -1)
    got = lax.ppermute(sent, "ctx", [(i, i ^ 1) for i in range(count)])
    got = [got[..., : got.shape[-1] // 2], got[..., got.shape[-1] // 2 :]]
    lows = []
    totals = []
    extend_totals(tables, count, 0, 1)
    for way, state, other in zip(ways, states, got):
        own = take_half(state, way.upper)
        low_block = jnp.where(way.upper, other, own)
        high_block = jnp.where(way.upper, own, other)
        lows.append(low_block)
        totals.append(way.gain(1, 2 * way.pair + 1, 1) * low_block + high_block)
    tables[-1], _ = lax.optimization_barrier((tables[-1], totals))
    extend_totals(tables, count, 1, count.bit_length())
    pair_prefixes, anchor = pair_scans(ways, totals)
    lifted_parts = []
    keep_parts = []
    for way, pair_prefix, low_block in zip(ways, pair_prefixes, lows):
        lifted = way.gain(1, 2 * way.pair, 1) * pair_prefix + low_block
        lifted_parts.append(jnp.where(way.upper, pair_prefix, lifted))
        keep_parts.append(jnp.where(way.upper, lifted, pair_prefix))
    got = lax.ppermute(jnp.concatenate(lifted_parts, -1), "ctx", [(i, i ^ 1) for i in range(count)])
    unit = jnp.exp(jnp.min(tables[-1]) * 0.0)
    got = got * unit
    half = got.shape[-1] // 2
    others = [got[..., :half], got[..., half:]]
    return (keep_parts, others, [way.upper for way in ways]), anchor, tables[-1]


def block_carried_grads(write_map, value_scale, decayed_vals, decayed_cot, carried, local_grads):
    local_values, local_write, local_read = local_grads
    (state_mine, adjoint_mine), (state_other, adjoint_other), (state_upper, adjoint_upper) = carried

    def rows_times(coeffs, mine, other, upper):
        return jnp.einsum(
            "iq,nq->in", take_half(coeffs, upper), mine.astype(jnp.bfloat16), preferred_element_type=jnp.float32
        ) + jnp.einsum(
            "iq,nq->in", take_half(coeffs, ~upper), other.astype(jnp.bfloat16), preferred_element_type=jnp.float32
        )

    grad_read = local_read + rows_times(decayed_cot, state_mine, state_other, state_upper)
    grad_write = local_write + rows_times(decayed_vals, adjoint_mine, adjoint_other, adjoint_upper)
    term_mine = jnp.einsum(
        "jn,nq->jq", write_map, adjoint_mine.astype(jnp.bfloat16), preferred_element_type=jnp.float32
    )
    term_other = jnp.einsum(
        "jn,nq->jq", write_map, adjoint_other.astype(jnp.bfloat16), preferred_element_type=jnp.float32
    )
    carried_term = join_halves(term_mine, term_other, adjoint_upper)
    grad_values = local_values + value_scale * carried_term
    return (
        grad_values.astype(jnp.bfloat16),
        grad_write.astype(jnp.bfloat16),
        grad_read.astype(jnp.bfloat16),
    )


def local(token_values, cotangent, write_coeffs, read_coeffs, decay_codes, skip_gain):
    seq_len = token_values.shape[1] * lax.axis_size("ctx")
    factor = 0.25 / seq_len
    prepare = jax.vmap(functools.partial(block_states, factor=factor))
    within, totals, value_scale, decayed_vals, decayed_cot, fwd_state, adj_state, skip_parts = prepare(
        token_values, cotangent, write_coeffs, read_coeffs, decay_codes
    )
    position = lax.axis_index("ctx")
    count = lax.axis_size("ctx")
    tables = jax.vmap(gather_totals, (0, 0, None, None))(totals, skip_parts, position, count)
    head_width = token_values.shape[2] // decay_codes.shape[2]
    carried, anchor, final_table = jax.vmap(carried_pair, (0, 0, 0, None, None, None))(
        tables, fwd_state, adj_state, position, count, head_width
    )
    grad_skip = jnp.sum(final_table[:, count], axis=0)
    for bit in range(lax.axis_size("dp").bit_length() - 1):
        grad_skip = grad_skip + lax.ppermute(grad_skip, "dp", xor_pairs(lax.axis_size("dp"), bit))
    local_inputs, _ = lax.optimization_barrier(
        ((token_values, cotangent, write_coeffs, read_coeffs, within), anchor)
    )
    local_grads = jax.vmap(block_local_grads, (0, 0, 0, 0, 0, None))(*local_inputs, skip_gain)
    grad_values, grad_write, grad_read = jax.vmap(block_carried_grads)(
        write_coeffs, value_scale, decayed_vals, decayed_cot, carried, local_grads
    )
    return (grad_values, grad_write, grad_read, grad_skip)


def solution(mesh):
    in_specs = (
        P("dp", "ctx", None),
        P("dp", "ctx", None),
        P("dp", "ctx", None),
        P("dp", "ctx", None),
        P("dp", "ctx", None),
        P(),
    )
    out_specs = (P("dp", "ctx", None), P("dp", "ctx", None), P("dp", "ctx", None), P())
    return jax.shard_map(local, mesh=mesh, in_specs=in_specs, out_specs=out_specs, check_vma=False)
```

```python
import functools

import jax
import jax.numpy as jnp
from jax import lax
from jax.sharding import PartitionSpec as P


def spread_heads(per_head, width):
    return jnp.repeat(per_head, width, axis=-1)


def block_states(values, cotan, write_map, read_map, codes, factor):
    head_count = codes.shape[1]
    head_width = values.shape[1] // head_count
    log_decay = -codes.astype(jnp.float32) * factor
    within = jnp.cumsum(log_decay, axis=0)
    totals = within[-1]
    value_scale = spread_heads(jnp.exp(totals - within), head_width)
    cot_scale = spread_heads(jnp.exp(within), head_width)
    decayed_vals = (values.astype(jnp.float32) * value_scale).astype(jnp.bfloat16)
    decayed_cot = (cotan.astype(jnp.float32) * cot_scale).astype(jnp.bfloat16)
    fwd_state = jnp.einsum("jn,jq->nq", write_map, decayed_vals, preferred_element_type=jnp.float32)
    adj_state = jnp.einsum("in,iq->nq", read_map, decayed_cot, preferred_element_type=jnp.float32)
    skip_part = jnp.sum(
        (values.astype(jnp.float32) * cotan.astype(jnp.float32)).reshape(
            values.shape[0], head_count, head_width
        ),
        axis=(0, 2),
    )
    return within, totals, value_scale, decayed_vals, decayed_cot, fwd_state, adj_state, skip_part


def block_local_grads(values, cotan, write_map, read_map, within, skip_gain):
    token_count = values.shape[0]
    head_count = skip_gain.shape[0]
    head_width = values.shape[1] // head_count
    vals_three = values.reshape(token_count, head_count, head_width)
    cot_three = cotan.reshape(token_count, head_count, head_width)
    rows = jnp.arange(token_count)
    causal = (rows[:, None] >= rows[None, :])[None]
    lead = within.T
    spread = lead[:, :, None] - lead[:, None, :]
    decay_matrix = jnp.where(causal, jnp.exp(jnp.where(causal, spread, 0.0)), 0.0)
    products = jnp.einsum("ihp,jhp->hij", cot_three, vals_three, preferred_element_type=jnp.float32)
    read_weights = (products * decay_matrix).astype(jnp.bfloat16)
    gram = jnp.einsum("in,jn->ij", read_map, write_map, preferred_element_type=jnp.float32)
    value_weights = (gram[None] * decay_matrix).astype(jnp.bfloat16)
    grad_read = jnp.einsum("hij,jn->in", read_weights, write_map, preferred_element_type=jnp.float32)
    grad_write = jnp.einsum("hij,in->jn", read_weights, read_map, preferred_element_type=jnp.float32)
    grad_values = jnp.einsum(
        "hij,ihp->jhp", value_weights, cot_three, preferred_element_type=jnp.float32
    ) + skip_gain[None, :, None] * cot_three.astype(jnp.float32)
    return grad_values.reshape(token_count, head_count * head_width), grad_write, grad_read


def xor_pairs(count, bit):
    return [(i, i ^ (1 << bit)) for i in range(count)]


def gather_totals(totals, skip_part, position, count):
    rows = jnp.arange(count)[:, None]
    table = jnp.concatenate([jnp.where(rows == position, totals[None, :], 0.0), skip_part[None, :]], 0)
    return [table]


def extend_totals(tables, count, start_bit, stop_bit):
    for bit in range(start_bit, min(stop_bit, count.bit_length() - 1)):
        tables.append(tables[-1] + lax.ppermute(tables[-1], "ctx", xor_pairs(count, bit)))


def take_half(array, upper):
    half = array.shape[-1] // 2
    return jnp.where(upper, array[..., half:], array[..., :half])


def join_halves(mine, other, upper):
    return jnp.where(upper, jnp.concatenate([other, mine], -1), jnp.concatenate([mine, other], -1))


class Direction:
    def __init__(self, tables, position, count, reverse, head_width):
        self.tables = tables
        self.count = count
        self.reverse = reverse
        self.head_width = head_width
        self.index = count - 1 - position if reverse else position
        self.upper = self.index % 2 == 1
        self.pair = self.index // 2
        self.pyramids = {}

    def actual(self, pairs):
        if self.reverse:
            return [(self.count - 1 - a, self.count - 1 - b) for a, b in pairs]
        return pairs

    def pair_pairs(self, pairs):
        return self.actual([(2 * a + j, 2 * b + j) for a, b in pairs for j in (0, 1)])

    def gain(self, table_index, low_block, size):
        key = (table_index % len(self.tables), size)
        if key not in self.pyramids:
            rows = self.tables[key[0]][: self.count]
            if self.reverse:
                rows = rows[::-1]
            grouped = rows.reshape(self.count // size, size, rows.shape[-1]).sum(axis=1)
            self.pyramids[key] = jnp.exp(grouped)
        full = lax.dynamic_index_in_dim(self.pyramids[key], low_block // size, keepdims=False)
        return spread_heads(take_half(full, self.upper), self.head_width)[..., None, :]


def exchange(payloads, pair_lists):
    return [
        lax.ppermute(p, "ctx", pairs) if pairs else jnp.zeros_like(p) for p, pairs in zip(payloads, pair_lists)
    ]


class PairScan:
    def __init__(self, way):
        self.way = way
        self.pair_count = way.count // 2
        self.level_count = self.pair_count.bit_length() - 1
        self.flip = self.level_count >= 2
        pair = way.pair
        self.role = jnp.where(way.upper, pair ^ 1, pair) if self.flip else pair

    def device_pairs(self, pairs, first_level):
        lower = [(2 * a, 2 * b) for a, b in pairs]
        if self.flip and first_level:
            upper = [(2 * b + 1, 2 * a + 1) for a, b in pairs]
        elif self.flip:
            upper = [(2 * (a ^ 1) + 1, 2 * (b ^ 1) + 1) for a, b in pairs]
        else:
            upper = [(2 * a + 1, 2 * b + 1) for a, b in pairs]
        return self.way.actual(lower + upper)

    def pair_gain(self, level, low_pair, pair_span):
        table = min(level + 2, len(self.way.tables) - 1)
        return self.way.gain(table, 2 * low_pair, 2 * pair_span)

    def up_send(self, level):
        span = 1 << level
        pairs = [(a, a + span) for a in range(self.pair_count) if a % (2 * span) == span - 1]
        return self.device_pairs(pairs, level == 0)

    def up_combine(self, level, total, lower):
        span = 1 << level
        if self.flip and level == 0:
            pair = self.way.pair
            kept_upper = self.pair_gain(0, pair ^ 1, 1) * total + lower
            kept_lower = self.pair_gain(0, pair, 1) * lower + total
            return jnp.where(self.way.upper, kept_upper, kept_lower)
        return self.pair_gain(level, self.role - span + 1, span) * lower + total

    def down_send(self, level, prefix, pair_total):
        span = 1 << level
        if self.flip and level == 0:
            pair = self.way.pair
            sent = jnp.where(self.way.upper, self.pair_gain(0, pair, 1) * prefix + pair_total, prefix)
            pairs = [(2 * (a + 1), 2 * a) for a in range(2, self.pair_count, 2)]
            pairs += [(2 * a + 1, 2 * (a + 1) + 1) for a in range(0, self.pair_count, 2)]
            return sent, self.way.actual(pairs)
        pairs = [(a, a - span) for a in range(2 * span, self.pair_count) if a % (2 * span) == 2 * span - 1]
        return prefix, self.device_pairs(pairs, False)

    def down_combine(self, level, prefix, got, lowers):
        span = 1 << level
        if self.flip and level == 0:
            pair = self.way.pair
            grown = self.pair_gain(self.level_count, pair - 1, 1) * prefix + lowers[0]
            odd = pair % 2 == 1
            return jnp.where(self.way.upper, jnp.where(odd, got, prefix), jnp.where(odd, grown, got))
        if got is not None:
            prefix = prefix + got
        lower_gain = self.pair_gain(self.level_count, self.role - 2 * span + 1, span)
        lower_gain = jnp.where(self.role % (2 * span) == 2 * span - 1, lower_gain, 1.0)
        return lower_gain * prefix + lowers[level]


def pair_scans(ways, pair_totals):
    scans = [PairScan(way) for way in ways]
    level_count = scans[0].level_count
    if scans[0].flip:
        return shift_scans(scans, pair_totals)
    totals = list(pair_totals)
    lowers = [[] for _ in scans]
    for level in range(level_count):
        got = exchange(totals, [scan.up_send(level) for scan in scans])
        for k, scan in enumerate(scans):
            lowers[k].append(got[k])
            if level < level_count - 1:
                totals[k] = scan.up_combine(level, totals[k], got[k])
    prefixes = [jnp.zeros_like(total) for total in pair_totals]
    for level in reversed(range(level_count)):
        if level < level_count - 1:
            sends = [scan.down_send(level, p, t) for scan, p, t in zip(scans, prefixes, pair_totals)]
            got = exchange([s[0] for s in sends], [s[1] for s in sends])
        else:
            got = [None] * len(scans)
        prefixes = [
            scan.down_combine(level, p, g, low) for scan, p, g, low in zip(scans, prefixes, got, lowers)
        ]
    anchor = lowers[0][0] if level_count else pair_totals[0]
    return prefixes, anchor


def shift_scans(scans, pair_totals):
    group_count = scans[0].pair_count // 2
    got = exchange(list(pair_totals), [scan.up_send(0) for scan in scans])
    lowers = [[g] for g in got]
    through = [scan.up_combine(0, t, g) for scan, t, g in zip(scans, pair_totals, got)]
    before = [jnp.zeros_like(t) for t in pair_totals]

    def group_gain(scan, group):
        return scan.way.gain(-1, 4 * group, 4)

    span = 1
    while span < group_count:
        pairs = [(2 * g + 1, 2 * (g + span) + 1) for g in range(group_count - span)]
        got = exchange(through, [scan.device_pairs(pairs, False) for scan in scans])
        for k, scan in enumerate(scans):
            group = scan.way.pair // 2
            before_gain = 1.0
            for back in range(1, span):
                before_gain = before_gain * group_gain(scan, group - back)
            if span < group_count // 2:
                through[k] = before_gain * group_gain(scan, group) * got[k] + through[k]
            before[k] = before_gain * got[k] + before[k]
        span *= 2
    sends = [scan.down_send(0, p, t) for scan, p, t in zip(scans, before, pair_totals)]
    got = exchange([s[0] for s in sends], [s[1] for s in sends])
    prefixes = [scan.down_combine(0, p, g, low) for scan, p, g, low in zip(scans, before, got, lowers)]
    return prefixes, lowers[0][0]


def carried_pair(tables, fwd_state, adj_state, position, count, head_width):
    ways = [Direction(tables, position, count, reverse, head_width) for reverse in (False, True)]
    states = [fwd_state, adj_state]
    sent = jnp.concatenate([take_half(s, ~w.upper) for s, w in zip(states, ways)], -1)
    got = lax.ppermute(sent, "ctx", [(i, i ^ 1) for i in range(count)])
    got = [got[..., : got.shape[-1] // 2], got[..., got.shape[-1] // 2 :]]
    lows = []
    totals = []
    extend_totals(tables, count, 0, 1)
    for way, state, other in zip(ways, states, got):
        own = take_half(state, way.upper)
        low_block = jnp.where(way.upper, other, own)
        high_block = jnp.where(way.upper, own, other)
        lows.append(low_block)
        totals.append(way.gain(1, 2 * way.pair + 1, 1) * low_block + high_block)
    tables[-1], _ = lax.optimization_barrier((tables[-1], totals))
    extend_totals(tables, count, 1, count.bit_length())
    pair_prefixes, anchor = pair_scans(ways, totals)
    lifted_parts = []
    keep_parts = []
    for way, pair_prefix, low_block in zip(ways, pair_prefixes, lows):
        lifted = way.gain(1, 2 * way.pair, 1) * pair_prefix + low_block
        lifted_parts.append(jnp.where(way.upper, pair_prefix, lifted))
        keep_parts.append(jnp.where(way.upper, lifted, pair_prefix))
    got = lax.ppermute(jnp.concatenate(lifted_parts, -1), "ctx", [(i, i ^ 1) for i in range(count)])
    unit = jnp.exp(jnp.min(tables[-1]) * 0.0)
    got = got * unit
    half = got.shape[-1] // 2
    others = [got[..., :half], got[..., half:]]
    return (keep_parts, others, [way.upper for way in ways]), anchor, tables[-1]


def block_carried_grads(write_map, value_scale, decayed_vals, decayed_cot, carried, local_grads):
    local_values, local_write, local_read = local_grads
    (state_mine, adjoint_mine), (state_other, adjoint_other), (state_upper, adjoint_upper) = carried

    def rows_times(coeffs, mine, other, upper):
        return jnp.einsum(
            "iq,nq->in", take_half(coeffs, upper), mine.astype(jnp.bfloat16), preferred_element_type=jnp.float32
        ) + jnp.einsum(
            "iq,nq->in", take_half(coeffs, ~upper), other.astype(jnp.bfloat16), preferred_element_type=jnp.float32
        )

    grad_read = local_read + rows_times(decayed_cot, state_mine, state_other, state_upper)
    grad_write = local_write + rows_times(decayed_vals, adjoint_mine, adjoint_other, adjoint_upper)
    term_mine = jnp.einsum(
        "jn,nq->jq", write_map, adjoint_mine.astype(jnp.bfloat16), preferred_element_type=jnp.float32
    )
    term_other = jnp.einsum(
        "jn,nq->jq", write_map, adjoint_other.astype(jnp.bfloat16), preferred_element_type=jnp.float32
    )
    carried_term = join_halves(term_mine, term_other, adjoint_upper)
    grad_values = local_values + value_scale * carried_term
    return (
        grad_values.astype(jnp.bfloat16),
        grad_write.astype(jnp.bfloat16),
        grad_read.astype(jnp.bfloat16),
    )


def local(token_values, cotangent, write_coeffs, read_coeffs, decay_codes, skip_gain):
    seq_len = token_values.shape[1] * lax.axis_size("ctx")
    factor = 0.25 / seq_len
    prepare = jax.vmap(functools.partial(block_states, factor=factor))
    within, totals, value_scale, decayed_vals, decayed_cot, fwd_state, adj_state, skip_parts = prepare(
        token_values, cotangent, write_coeffs, read_coeffs, decay_codes
    )
    position = lax.axis_index("ctx")
    count = lax.axis_size("ctx")
    tables = jax.vmap(gather_totals, (0, 0, None, None))(totals, skip_parts, position, count)
    head_width = token_values.shape[2] // decay_codes.shape[2]
    carried, anchor, final_table = jax.vmap(carried_pair, (0, 0, 0, None, None, None))(
        tables, fwd_state, adj_state, position, count, head_width
    )
    grad_skip = jnp.sum(final_table[:, count], axis=0)
    for bit in range(lax.axis_size("dp").bit_length() - 1):
        grad_skip = grad_skip + lax.ppermute(grad_skip, "dp", xor_pairs(lax.axis_size("dp"), bit))
    local_inputs, _ = lax.optimization_barrier(
        ((token_values, cotangent, write_coeffs, read_coeffs, within), anchor)
    )
    local_grads = jax.vmap(block_local_grads, (0, 0, 0, 0, 0, None))(*local_inputs, skip_gain)
    grad_values, grad_write, grad_read = jax.vmap(block_carried_grads)(
        write_coeffs, value_scale, decayed_vals, decayed_cot, carried, local_grads
    )
    return (grad_values, grad_write, grad_read, grad_skip)


def solution(mesh):
    in_specs = (
        P("dp", "ctx", None),
        P("dp", "ctx", None),
        P("dp", "ctx", None),
        P("dp", "ctx", None),
        P("dp", "ctx", None),
        P(),
    )
    out_specs = (P("dp", "ctx", None), P("dp", "ctx", None), P("dp", "ctx", None), P())
    return jax.shard_map(local, mesh=mesh, in_specs=in_specs, out_specs=out_specs, check_vma=False)
```

```python
import functools

import jax
import jax.numpy as jnp
from jax import lax
from jax.sharding import PartitionSpec as P


def spread_heads(per_head, width):
    return jnp.repeat(per_head, width, axis=-1)


def block_states(values, cotan, write_map, read_map, codes, factor):
    head_count = codes.shape[1]
    head_width = values.shape[1] // head_count
    log_decay = -codes.astype(jnp.float32) * factor
    within = jnp.cumsum(log_decay, axis=0)
    totals = within[-1]
    value_scale = spread_heads(jnp.exp(totals - within), head_width)
    cot_scale = spread_heads(jnp.exp(within), head_width)
    decayed_vals = (values.astype(jnp.float32) * value_scale).astype(jnp.bfloat16)
    decayed_cot = (cotan.astype(jnp.float32) * cot_scale).astype(jnp.bfloat16)
    fwd_state = jnp.einsum("jn,jq->nq", write_map, decayed_vals, preferred_element_type=jnp.float32)
    adj_state = jnp.einsum("in,iq->nq", read_map, decayed_cot, preferred_element_type=jnp.float32)
    skip_part = jnp.sum(
        (values.astype(jnp.float32) * cotan.astype(jnp.float32)).reshape(
            values.shape[0], head_count, head_width
        ),
        axis=(0, 2),
    )
    return within, totals, value_scale, decayed_vals, decayed_cot, fwd_state, adj_state, skip_part


def block_local_grads(values, cotan, write_map, read_map, within, skip_gain):
    token_count = values.shape[0]
    head_count = skip_gain.shape[0]
    head_width = values.shape[1] // head_count
    vals_three = values.reshape(token_count, head_count, head_width)
    cot_three = cotan.reshape(token_count, head_count, head_width)
    rows = jnp.arange(token_count)
    causal = (rows[:, None] >= rows[None, :])[None]
    lead = within.T
    spread = lead[:, :, None] - lead[:, None, :]
    decay_matrix = jnp.where(causal, jnp.exp(jnp.where(causal, spread, 0.0)), 0.0)
    products = jnp.einsum("ihp,jhp->hij", cot_three, vals_three, preferred_element_type=jnp.float32)
    read_weights = (products * decay_matrix).astype(jnp.bfloat16)
    gram = jnp.einsum("in,jn->ij", read_map, write_map, preferred_element_type=jnp.float32)
    value_weights = (gram[None] * decay_matrix).astype(jnp.bfloat16)
    grad_read = jnp.einsum("hij,jn->in", read_weights, write_map, preferred_element_type=jnp.float32)
    grad_write = jnp.einsum("hij,in->jn", read_weights, read_map, preferred_element_type=jnp.float32)
    grad_values = jnp.einsum(
        "hij,ihp->jhp", value_weights, cot_three, preferred_element_type=jnp.float32
    ) + skip_gain[None, :, None] * cot_three.astype(jnp.float32)
    return grad_values.reshape(token_count, head_count * head_width), grad_write, grad_read


def xor_pairs(count, bit):
    return [(i, i ^ (1 << bit)) for i in range(count)]


def gather_totals(totals, skip_part, position, count):
    rows = jnp.arange(count)[:, None]
    table = jnp.concatenate([jnp.where(rows == position, totals[None, :], 0.0), skip_part[None, :]], 0)
    return [table]


def extend_totals(tables, count, start_bit, stop_bit):
    for bit in range(start_bit, min(stop_bit, count.bit_length() - 1)):
        tables.append(tables[-1] + lax.ppermute(tables[-1], "ctx", xor_pairs(count, bit)))


def take_half(array, upper):
    half = array.shape[-1] // 2
    return jnp.where(upper, array[..., half:], array[..., :half])


def join_halves(mine, other, upper):
    return jnp.where(upper, jnp.concatenate([other, mine], -1), jnp.concatenate([mine, other], -1))


class Direction:
    def __init__(self, tables, position, count, reverse, head_width):
        self.tables = tables
        self.count = count
        self.reverse = reverse
        self.head_width = head_width
        self.index = count - 1 - position if reverse else position
        self.upper = self.index % 2 == 1
        self.pair = self.index // 2
        self.pyramids = {}

    def actual(self, pairs):
        if self.reverse:
            return [(self.count - 1 - a, self.count - 1 - b) for a, b in pairs]
        return pairs

    def pair_pairs(self, pairs):
        return self.actual([(2 * a + j, 2 * b + j) for a, b in pairs for j in (0, 1)])

    def gain(self, table_index, low_block, size):
        key = (table_index % len(self.tables), size)
        if key not in self.pyramids:
            rows = self.tables[key[0]][: self.count]
            if self.reverse:
                rows = rows[::-1]
            grouped = rows.reshape(self.count // size, size, rows.shape[-1]).sum(axis=1)
            self.pyramids[key] = jnp.exp(grouped)
        full = lax.dynamic_index_in_dim(self.pyramids[key], low_block // size, keepdims=False)
        return spread_heads(take_half(full, self.upper), self.head_width)[..., None, :]


def exchange(payloads, pair_lists):
    return [
        lax.ppermute(p, "ctx", pairs) if pairs else jnp.zeros_like(p) for p, pairs in zip(payloads, pair_lists)
    ]


class PairScan:
    def __init__(self, way):
        self.way = way
        self.pair_count = way.count // 2
        self.level_count = self.pair_count.bit_length() - 1
        self.flip = self.level_count >= 2
        pair = way.pair
        self.role = jnp.where(way.upper, pair ^ 1, pair) if self.flip else pair

    def device_pairs(self, pairs, first_level):
        lower = [(2 * a, 2 * b) for a, b in pairs]
        if self.flip and first_level:
            upper = [(2 * b + 1, 2 * a + 1) for a, b in pairs]
        elif self.flip:
            upper = [(2 * (a ^ 1) + 1, 2 * (b ^ 1) + 1) for a, b in pairs]
        else:
            upper = [(2 * a + 1, 2 * b + 1) for a, b in pairs]
        return self.way.actual(lower + upper)

    def pair_gain(self, level, low_pair, pair_span):
        table = min(level + 2, len(self.way.tables) - 1)
        return self.way.gain(table, 2 * low_pair, 2 * pair_span)

    def up_send(self, level):
        span = 1 << level
        pairs = [(a, a + span) for a in range(self.pair_count) if a % (2 * span) == span - 1]
        return self.device_pairs(pairs, level == 0)

    def up_combine(self, level, total, lower):
        span = 1 << level
        if self.flip and level == 0:
            pair = self.way.pair
            kept_upper = self.pair_gain(0, pair ^ 1, 1) * total + lower
            kept_lower = self.pair_gain(0, pair, 1) * lower + total
            return jnp.where(self.way.upper, kept_upper, kept_lower)
        return self.pair_gain(level, self.role - span + 1, span) * lower + total

    def down_send(self, level, prefix, pair_total):
        span = 1 << level
        if self.flip and level == 0:
            pair = self.way.pair
            sent = jnp.where(self.way.upper, self.pair_gain(0, pair, 1) * prefix + pair_total, prefix)
            pairs = [(2 * (a + 1), 2 * a) for a in range(2, self.pair_count, 2)]
            pairs += [(2 * a + 1, 2 * (a + 1) + 1) for a in range(0, self.pair_count, 2)]
            return sent, self.way.actual(pairs)
        pairs = [(a, a - span) for a in range(2 * span, self.pair_count) if a % (2 * span) == 2 * span - 1]
        return prefix, self.device_pairs(pairs, False)

    def down_combine(self, level, prefix, got, lowers):
        span = 1 << level
        if self.flip and level == 0:
            pair = self.way.pair
            grown = self.pair_gain(self.level_count, pair - 1, 1) * prefix + lowers[0]
            odd = pair % 2 == 1
            return jnp.where(self.way.upper, jnp.where(odd, got, prefix), jnp.where(odd, grown, got))
        if got is not None:
            prefix = prefix + got
        lower_gain = self.pair_gain(self.level_count, self.role - 2 * span + 1, span)
        lower_gain = jnp.where(self.role % (2 * span) == 2 * span - 1, lower_gain, 1.0)
        return lower_gain * prefix + lowers[level]


def pair_scans(ways, pair_totals, local_terms):
    scans = [PairScan(way) for way in ways]
    level_count = scans[0].level_count
    if scans[0].flip:
        return shift_scans(scans, pair_totals, local_terms)
    totals = list(pair_totals)
    lowers = [[] for _ in scans]
    for level in range(level_count):
        got = exchange(totals, [scan.up_send(level) for scan in scans])
        for k, scan in enumerate(scans):
            lowers[k].append(got[k])
            if level < level_count - 1:
                totals[k] = scan.up_combine(level, totals[k], got[k])
    prefixes = [jnp.zeros_like(total) for total in pair_totals]
    for level in reversed(range(level_count)):
        if level < level_count - 1:
            sends = [scan.down_send(level, p, t) for scan, p, t in zip(scans, prefixes, pair_totals)]
            got = exchange([s[0] for s in sends], [s[1] for s in sends])
        else:
            got = [None] * len(scans)
        prefixes = [
            scan.down_combine(level, p, g, low) for scan, p, g, low in zip(scans, prefixes, got, lowers)
        ]
    anchor = lowers[0][0] if level_count else pair_totals[0]
    return prefixes, local_terms(anchor)


def shift_scans(scans, pair_totals, local_terms):
    group_count = scans[0].pair_count // 2
    got = exchange(list(pair_totals), [scan.up_send(0) for scan in scans])
    lowers = [[g] for g in got]
    through = [scan.up_combine(0, t, g) for scan, t, g in zip(scans, pair_totals, got)]
    before = [jnp.zeros_like(t) for t in pair_totals]

    def group_gain(scan, group):
        return scan.way.gain(-1, 4 * group, 4)

    span = 1
    while span < group_count:
        pairs = [(2 * g + 1, 2 * (g + span) + 1) for g in range(group_count - span)]
        got = exchange(through, [scan.device_pairs(pairs, False) for scan in scans])
        for k, scan in enumerate(scans):
            group = scan.way.pair // 2
            before_gain = 1.0
            for back in range(1, span):
                before_gain = before_gain * group_gain(scan, group - back)
            if span < group_count // 2:
                through[k] = before_gain * group_gain(scan, group) * got[k] + through[k]
            before[k] = before_gain * got[k] + before[k]
        span *= 2
    before, local = lax.optimization_barrier((before, local_terms(lowers[0][0])))
    sends = [scan.down_send(0, p, t) for scan, p, t in zip(scans, before, pair_totals)]
    got = exchange([s[0] for s in sends], [s[1] for s in sends])
    prefixes = [scan.down_combine(0, p, g, low) for scan, p, g, low in zip(scans, before, got, lowers)]
    return prefixes, local


def carried_pair(tables, fwd_state, adj_state, position, count, head_width, local_inputs, skip_gain):
    ways = [Direction(tables, position, count, reverse, head_width) for reverse in (False, True)]
    states = [fwd_state, adj_state]
    sent = jnp.concatenate([take_half(s, ~w.upper) for s, w in zip(states, ways)], -1)
    got = lax.ppermute(sent, "ctx", [(i, i ^ 1) for i in range(count)])
    got = [got[..., : got.shape[-1] // 2], got[..., got.shape[-1] // 2 :]]
    lows = []
    totals = []
    extend_totals(tables, count, 0, 1)
    for way, state, other in zip(ways, states, got):
        own = take_half(state, way.upper)
        low_block = jnp.where(way.upper, other, own)
        high_block = jnp.where(way.upper, own, other)
        lows.append(low_block)
        totals.append(way.gain(1, 2 * way.pair + 1, 1) * low_block + high_block)
    tables[-1], _ = lax.optimization_barrier((tables[-1], totals))
    extend_totals(tables, count, 1, count.bit_length())

    def local_terms(anchor):
        held, _ = lax.optimization_barrier((local_inputs, anchor))
        return block_local_grads(*held, skip_gain)

    pair_prefixes, local_grads = pair_scans(ways, totals, local_terms)
    lifted_parts = []
    keep_parts = []
    for way, pair_prefix, low_block in zip(ways, pair_prefixes, lows):
        lifted = way.gain(1, 2 * way.pair, 1) * pair_prefix + low_block
        lifted_parts.append(jnp.where(way.upper, pair_prefix, lifted))
        keep_parts.append(jnp.where(way.upper, lifted, pair_prefix))
    got = lax.ppermute(jnp.concatenate(lifted_parts, -1), "ctx", [(i, i ^ 1) for i in range(count)])
    unit = jnp.exp(jnp.min(tables[-1]) * 0.0)
    got = got * unit
    half = got.shape[-1] // 2
    others = [got[..., :half], got[..., half:]]
    return (keep_parts, others, [way.upper for way in ways]), local_grads, tables[-1]


def block_carried_grads(write_map, value_scale, decayed_vals, decayed_cot, carried, local_grads):
    local_values, local_write, local_read = local_grads
    (state_mine, adjoint_mine), (state_other, adjoint_other), (state_upper, adjoint_upper) = carried

    def rows_times(coeffs, mine, other, upper):
        return jnp.einsum(
            "iq,nq->in", take_half(coeffs, upper), mine.astype(jnp.bfloat16), preferred_element_type=jnp.float32
        ) + jnp.einsum(
            "iq,nq->in", take_half(coeffs, ~upper), other.astype(jnp.bfloat16), preferred_element_type=jnp.float32
        )

    grad_read = local_read + rows_times(decayed_cot, state_mine, state_other, state_upper)
    grad_write = local_write + rows_times(decayed_vals, adjoint_mine, adjoint_other, adjoint_upper)
    term_mine = jnp.einsum(
        "jn,nq->jq", write_map, adjoint_mine.astype(jnp.bfloat16), preferred_element_type=jnp.float32
    )
    term_other = jnp.einsum(
        "jn,nq->jq", write_map, adjoint_other.astype(jnp.bfloat16), preferred_element_type=jnp.float32
    )
    carried_term = join_halves(term_mine, term_other, adjoint_upper)
    grad_values = local_values + value_scale * carried_term
    return (
        grad_values.astype(jnp.bfloat16),
        grad_write.astype(jnp.bfloat16),
        grad_read.astype(jnp.bfloat16),
    )


def local(token_values, cotangent, write_coeffs, read_coeffs, decay_codes, skip_gain):
    seq_len = token_values.shape[1] * lax.axis_size("ctx")
    factor = 0.25 / seq_len
    prepare = jax.vmap(functools.partial(block_states, factor=factor))
    within, totals, value_scale, decayed_vals, decayed_cot, fwd_state, adj_state, skip_parts = prepare(
        token_values, cotangent, write_coeffs, read_coeffs, decay_codes
    )
    position = lax.axis_index("ctx")
    count = lax.axis_size("ctx")
    tables = jax.vmap(gather_totals, (0, 0, None, None))(totals, skip_parts, position, count)
    head_width = token_values.shape[2] // decay_codes.shape[2]
    local_inputs = (token_values, cotangent, write_coeffs, read_coeffs, within)
    carried, local_grads, final_table = jax.vmap(carried_pair, (0, 0, 0, None, None, None, 0, None))(
        tables, fwd_state, adj_state, position, count, head_width, local_inputs, skip_gain
    )
    grad_skip = jnp.sum(final_table[:, count], axis=0)
    for bit in range(lax.axis_size("dp").bit_length() - 1):
        grad_skip = grad_skip + lax.ppermute(grad_skip, "dp", xor_pairs(lax.axis_size("dp"), bit))
    grad_values, grad_write, grad_read = jax.vmap(block_carried_grads)(
        write_coeffs, value_scale, decayed_vals, decayed_cot, carried, local_grads
    )
    return (grad_values, grad_write, grad_read, grad_skip)


def solution(mesh):
    in_specs = (
        P("dp", "ctx", None),
        P("dp", "ctx", None),
        P("dp", "ctx", None),
        P("dp", "ctx", None),
        P("dp", "ctx", None),
        P(),
    )
    out_specs = (P("dp", "ctx", None), P("dp", "ctx", None), P("dp", "ctx", None), P())
    return jax.shard_map(local, mesh=mesh, in_specs=in_specs, out_specs=out_specs, check_vma=False)
```

```python
import functools

import jax
import jax.numpy as jnp
from jax import lax
from jax.sharding import PartitionSpec as P


def spread_heads(per_head, width):
    return jnp.repeat(per_head, width, axis=-1)


def block_states(values, cotan, write_map, read_map, codes, factor):
    head_count = codes.shape[1]
    head_width = values.shape[1] // head_count
    log_decay = -codes.astype(jnp.float32) * factor
    within = jnp.cumsum(log_decay, axis=0)
    totals = within[-1]
    value_scale = spread_heads(jnp.exp(totals - within), head_width)
    cot_scale = spread_heads(jnp.exp(within), head_width)
    decayed_vals = (values.astype(jnp.float32) * value_scale).astype(jnp.bfloat16)
    decayed_cot = (cotan.astype(jnp.float32) * cot_scale).astype(jnp.bfloat16)
    fwd_state = jnp.einsum("jn,jq->nq", write_map, decayed_vals, preferred_element_type=jnp.float32)
    adj_state = jnp.einsum("in,iq->nq", read_map, decayed_cot, preferred_element_type=jnp.float32)
    skip_part = jnp.sum(
        (values.astype(jnp.float32) * cotan.astype(jnp.float32)).reshape(
            values.shape[0], head_count, head_width
        ),
        axis=(0, 2),
    )
    return within, totals, value_scale, decayed_vals, decayed_cot, fwd_state, adj_state, skip_part


def block_local_grads(values, cotan, write_map, read_map, within, skip_gain):
    token_count = values.shape[0]
    head_count = skip_gain.shape[0]
    head_width = values.shape[1] // head_count
    vals_three = values.reshape(token_count, head_count, head_width)
    cot_three = cotan.reshape(token_count, head_count, head_width)
    rows = jnp.arange(token_count)
    causal = (rows[:, None] >= rows[None, :])[None]
    lead = within.T
    spread = lead[:, :, None] - lead[:, None, :]
    decay_matrix = jnp.where(causal, jnp.exp(jnp.where(causal, spread, 0.0)), 0.0)
    products = jnp.einsum("ihp,jhp->hij", cot_three, vals_three, preferred_element_type=jnp.float32)
    read_weights = (products * decay_matrix).astype(jnp.bfloat16)
    gram = jnp.einsum("in,jn->ij", read_map, write_map, preferred_element_type=jnp.float32)
    value_weights = (gram[None] * decay_matrix).astype(jnp.bfloat16)
    grad_read = jnp.einsum("hij,jn->in", read_weights, write_map, preferred_element_type=jnp.float32)
    grad_write = jnp.einsum("hij,in->jn", read_weights, read_map, preferred_element_type=jnp.float32)
    grad_values = jnp.einsum(
        "hij,ihp->jhp", value_weights, cot_three, preferred_element_type=jnp.float32
    ) + skip_gain[None, :, None] * cot_three.astype(jnp.float32)
    return grad_values.reshape(token_count, head_count * head_width), grad_write, grad_read


def xor_pairs(count, bit):
    return [(i, i ^ (1 << bit)) for i in range(count)]


def gather_totals(totals, skip_part, position, count):
    rows = jnp.arange(count)[:, None]
    table = jnp.concatenate([jnp.where(rows == position, totals[None, :], 0.0), skip_part[None, :]], 0)
    return [table]


def extend_totals(tables, count, start_bit, stop_bit):
    for bit in range(start_bit, min(stop_bit, count.bit_length() - 1)):
        tables.append(tables[-1] + lax.ppermute(tables[-1], "ctx", xor_pairs(count, bit)))


def take_half(array, upper):
    half = array.shape[-1] // 2
    return jnp.where(upper, array[..., half:], array[..., :half])


def join_halves(mine, other, upper):
    return jnp.where(upper, jnp.concatenate([other, mine], -1), jnp.concatenate([mine, other], -1))


class Direction:
    def __init__(self, tables, position, count, reverse, head_width):
        self.tables = tables
        self.count = count
        self.reverse = reverse
        self.head_width = head_width
        self.index = count - 1 - position if reverse else position
        self.upper = self.index % 2 == 1
        self.pair = self.index // 2
        self.pyramids = {}

    def actual(self, pairs):
        if self.reverse:
            return [(self.count - 1 - a, self.count - 1 - b) for a, b in pairs]
        return pairs

    def pair_pairs(self, pairs):
        return self.actual([(2 * a + j, 2 * b + j) for a, b in pairs for j in (0, 1)])

    def gain(self, table_index, low_block, size):
        key = (table_index % len(self.tables), size)
        if key not in self.pyramids:
            rows = self.tables[key[0]][: self.count]
            if self.reverse:
                rows = rows[::-1]
            grouped = rows.reshape(self.count // size, size, rows.shape[-1]).sum(axis=1)
            self.pyramids[key] = jnp.exp(grouped)
        full = lax.dynamic_index_in_dim(self.pyramids[key], low_block // size, keepdims=False)
        return spread_heads(take_half(full, self.upper), self.head_width)[..., None, :]


def exchange(payloads, pair_lists):
    return [
        lax.ppermute(p, "ctx", pairs) if pairs else jnp.zeros_like(p) for p, pairs in zip(payloads, pair_lists)
    ]


class PairScan:
    def __init__(self, way):
        self.way = way
        self.pair_count = way.count // 2
        self.level_count = self.pair_count.bit_length() - 1
        self.flip = self.level_count >= 2
        pair = way.pair
        self.role = jnp.where(way.upper, pair ^ 1, pair) if self.flip else pair

    def device_pairs(self, pairs, first_level):
        lower = [(2 * a, 2 * b) for a, b in pairs]
        if self.flip and first_level:
            upper = [(2 * b + 1, 2 * a + 1) for a, b in pairs]
        elif self.flip:
            upper = [(2 * (a ^ 1) + 1, 2 * (b ^ 1) + 1) for a, b in pairs]
        else:
            upper = [(2 * a + 1, 2 * b + 1) for a, b in pairs]
        return self.way.actual(lower + upper)

    def pair_gain(self, level, low_pair, pair_span):
        table = min(level + 2, len(self.way.tables) - 1)
        return self.way.gain(table, 2 * low_pair, 2 * pair_span)

    def up_send(self, level):
        span = 1 << level
        pairs = [(a, a + span) for a in range(self.pair_count) if a % (2 * span) == span - 1]
        return self.device_pairs(pairs, level == 0)

    def up_combine(self, level, total, lower):
        span = 1 << level
        if self.flip and level == 0:
            pair = self.way.pair
            kept_upper = self.pair_gain(0, pair ^ 1, 1) * total + lower
            kept_lower = self.pair_gain(0, pair, 1) * lower + total
            return jnp.where(self.way.upper, kept_upper, kept_lower)
        return self.pair_gain(level, self.role - span + 1, span) * lower + total

    def down_send(self, level, prefix, pair_total):
        span = 1 << level
        if self.flip and level == 0:
            pair = self.way.pair
            sent = jnp.where(self.way.upper, self.pair_gain(0, pair, 1) * prefix + pair_total, prefix)
            pairs = [(2 * (a + 1), 2 * a) for a in range(2, self.pair_count, 2)]
            pairs += [(2 * a + 1, 2 * (a + 1) + 1) for a in range(0, self.pair_count, 2)]
            return sent, self.way.actual(pairs)
        pairs = [(a, a - span) for a in range(2 * span, self.pair_count) if a % (2 * span) == 2 * span - 1]
        return prefix, self.device_pairs(pairs, False)

    def down_combine(self, level, prefix, got, lowers):
        span = 1 << level
        if self.flip and level == 0:
            pair = self.way.pair
            grown = self.pair_gain(self.level_count, pair - 1, 1) * prefix + lowers[0]
            odd = pair % 2 == 1
            return jnp.where(self.way.upper, jnp.where(odd, got, prefix), jnp.where(odd, grown, got))
        if got is not None:
            prefix = prefix + got
        lower_gain = self.pair_gain(self.level_count, self.role - 2 * span + 1, span)
        lower_gain = jnp.where(self.role % (2 * span) == 2 * span - 1, lower_gain, 1.0)
        return lower_gain * prefix + lowers[level]


def pair_scans(ways, pair_totals):
    scans = [PairScan(way) for way in ways]
    level_count = scans[0].level_count
    if scans[0].flip:
        return shift_scans(scans, pair_totals)
    totals = list(pair_totals)
    lowers = [[] for _ in scans]
    for level in range(level_count):
        got = exchange(totals, [scan.up_send(level) for scan in scans])
        for k, scan in enumerate(scans):
            lowers[k].append(got[k])
            if level < level_count - 1:
                totals[k] = scan.up_combine(level, totals[k], got[k])
    prefixes = [jnp.zeros_like(total) for total in pair_totals]
    for level in reversed(range(level_count)):
        if level < level_count - 1:
            sends = [scan.down_send(level, p, t) for scan, p, t in zip(scans, prefixes, pair_totals)]
            got = exchange([s[0] for s in sends], [s[1] for s in sends])
        else:
            got = [None] * len(scans)
        prefixes = [
            scan.down_combine(level, p, g, low) for scan, p, g, low in zip(scans, prefixes, got, lowers)
        ]
    anchor = lowers[0][0] if level_count else pair_totals[0]
    return prefixes, anchor


def shift_scans(scans, pair_totals):
    group_count = scans[0].pair_count // 2
    got = exchange(list(pair_totals), [scan.up_send(0) for scan in scans])
    lowers = [[g] for g in got]
    through = [scan.up_combine(0, t, g) for scan, t, g in zip(scans, pair_totals, got)]
    before = [jnp.zeros_like(t) for t in pair_totals]

    def group_gain(scan, group):
        return scan.way.gain(-1, 4 * group, 4)

    span = 1
    while span < group_count:
        pairs = [(2 * g + 1, 2 * (g + span) + 1) for g in range(group_count - span)]
        got = exchange(through, [scan.device_pairs(pairs, False) for scan in scans])
        for k, scan in enumerate(scans):
            group = scan.way.pair // 2
            before_gain = 1.0
            for back in range(1, span):
                before_gain = before_gain * group_gain(scan, group - back)
            if span < group_count // 2:
                through[k] = before_gain * group_gain(scan, group) * got[k] + through[k]
            before[k] = before_gain * got[k] + before[k]
        span *= 2
    sends = [scan.down_send(0, p, t) for scan, p, t in zip(scans, before, pair_totals)]
    got = exchange([s[0] for s in sends], [s[1] for s in sends])
    prefixes = [scan.down_combine(0, p, g, low) for scan, p, g, low in zip(scans, before, got, lowers)]
    return prefixes, lowers[0][0]


def carried_pair(tables, fwd_state, adj_state, position, count, head_width):
    ways = [Direction(tables, position, count, reverse, head_width) for reverse in (False, True)]
    states = [fwd_state, adj_state]
    swap = [(i, i ^ 1) for i in range(count)]
    got = [lax.ppermute(take_half(s, ~w.upper), "ctx", swap) for s, w in zip(states, ways)]
    lows = []
    totals = []
    extend_totals(tables, count, 0, 1)
    for way, state, other in zip(ways, states, got):
        own = take_half(state, way.upper)
        low_block = jnp.where(way.upper, other, own)
        high_block = jnp.where(way.upper, own, other)
        lows.append(low_block)
        totals.append(way.gain(1, 2 * way.pair + 1, 1) * low_block + high_block)
    tables[-1], _ = lax.optimization_barrier((tables[-1], totals))
    extend_totals(tables, count, 1, count.bit_length())
    pair_prefixes, anchor = pair_scans(ways, totals)
    lifted_parts = []
    keep_parts = []
    for way, pair_prefix, low_block in zip(ways, pair_prefixes, lows):
        lifted = way.gain(1, 2 * way.pair, 1) * pair_prefix + low_block
        lifted_parts.append(jnp.where(way.upper, pair_prefix, lifted))
        keep_parts.append(jnp.where(way.upper, lifted, pair_prefix))
    unit = jnp.exp(jnp.min(tables[-1]) * 0.0)
    others = [lax.ppermute(part, "ctx", swap) * unit for part in lifted_parts]
    return (keep_parts, others, [way.upper for way in ways]), anchor, tables[-1]


def block_carried_grads(write_map, value_scale, decayed_vals, decayed_cot, carried, local_grads):
    local_values, local_write, local_read = local_grads
    (state_mine, adjoint_mine), (state_other, adjoint_other), (state_upper, adjoint_upper) = carried

    def rows_times(coeffs, mine, other, upper):
        return jnp.einsum(
            "iq,nq->in", take_half(coeffs, upper), mine.astype(jnp.bfloat16), preferred_element_type=jnp.float32
        ) + jnp.einsum(
            "iq,nq->in", take_half(coeffs, ~upper), other.astype(jnp.bfloat16), preferred_element_type=jnp.float32
        )

    grad_read = local_read + rows_times(decayed_cot, state_mine, state_other, state_upper)
    grad_write = local_write + rows_times(decayed_vals, adjoint_mine, adjoint_other, adjoint_upper)
    term_mine = jnp.einsum(
        "jn,nq->jq", write_map, adjoint_mine.astype(jnp.bfloat16), preferred_element_type=jnp.float32
    )
    term_other = jnp.einsum(
        "jn,nq->jq", write_map, adjoint_other.astype(jnp.bfloat16), preferred_element_type=jnp.float32
    )
    carried_term = join_halves(term_mine, term_other, adjoint_upper)
    grad_values = local_values + value_scale * carried_term
    return (
        grad_values.astype(jnp.bfloat16),
        grad_write.astype(jnp.bfloat16),
        grad_read.astype(jnp.bfloat16),
    )


def local(token_values, cotangent, write_coeffs, read_coeffs, decay_codes, skip_gain):
    seq_len = token_values.shape[1] * lax.axis_size("ctx")
    factor = 0.25 / seq_len
    prepare = jax.vmap(functools.partial(block_states, factor=factor))
    within, totals, value_scale, decayed_vals, decayed_cot, fwd_state, adj_state, skip_parts = prepare(
        token_values, cotangent, write_coeffs, read_coeffs, decay_codes
    )
    position = lax.axis_index("ctx")
    count = lax.axis_size("ctx")
    tables = jax.vmap(gather_totals, (0, 0, None, None))(totals, skip_parts, position, count)
    head_width = token_values.shape[2] // decay_codes.shape[2]
    carried, anchor, final_table = jax.vmap(carried_pair, (0, 0, 0, None, None, None))(
        tables, fwd_state, adj_state, position, count, head_width
    )
    grad_skip = jnp.sum(final_table[:, count], axis=0)
    for bit in range(lax.axis_size("dp").bit_length() - 1):
        grad_skip = grad_skip + lax.ppermute(grad_skip, "dp", xor_pairs(lax.axis_size("dp"), bit))
    local_inputs, _ = lax.optimization_barrier(
        ((token_values, cotangent, write_coeffs, read_coeffs, within), anchor)
    )
    local_grads = jax.vmap(block_local_grads, (0, 0, 0, 0, 0, None))(*local_inputs, skip_gain)
    grad_values, grad_write, grad_read = jax.vmap(block_carried_grads)(
        write_coeffs, value_scale, decayed_vals, decayed_cot, carried, local_grads
    )
    return (grad_values, grad_write, grad_read, grad_skip)


def solution(mesh):
    in_specs = (
        P("dp", "ctx", None),
        P("dp", "ctx", None),
        P("dp", "ctx", None),
        P("dp", "ctx", None),
        P("dp", "ctx", None),
        P(),
    )
    out_specs = (P("dp", "ctx", None), P("dp", "ctx", None), P("dp", "ctx", None), P())
    return jax.shard_map(local, mesh=mesh, in_specs=in_specs, out_specs=out_specs, check_vma=False)
```

```python
import functools

import jax
import jax.numpy as jnp
from jax import lax
from jax.sharding import PartitionSpec as P


def spread_heads(per_head, width):
    return jnp.repeat(per_head, width, axis=-1)


def block_states(values, cotan, write_map, read_map, codes, factor):
    head_count = codes.shape[1]
    head_width = values.shape[1] // head_count
    log_decay = -codes.astype(jnp.float32) * factor
    within = jnp.cumsum(log_decay, axis=0)
    totals = within[-1]
    value_scale = spread_heads(jnp.exp(totals - within), head_width)
    cot_scale = spread_heads(jnp.exp(within), head_width)
    decayed_vals = (values.astype(jnp.float32) * value_scale).astype(jnp.bfloat16)
    decayed_cot = (cotan.astype(jnp.float32) * cot_scale).astype(jnp.bfloat16)
    fwd_state = jnp.einsum("jn,jq->nq", write_map, decayed_vals, preferred_element_type=jnp.float32)
    adj_state = jnp.einsum("in,iq->nq", read_map, decayed_cot, preferred_element_type=jnp.float32)
    skip_part = jnp.sum(
        (values.astype(jnp.float32) * cotan.astype(jnp.float32)).reshape(
            values.shape[0], head_count, head_width
        ),
        axis=(0, 2),
    )
    return within, totals, value_scale, decayed_vals, decayed_cot, fwd_state, adj_state, skip_part


def block_local_grads(values, cotan, write_map, read_map, within, skip_gain):
    token_count = values.shape[0]
    head_count = skip_gain.shape[0]
    head_width = values.shape[1] // head_count
    vals_three = values.reshape(token_count, head_count, head_width)
    cot_three = cotan.reshape(token_count, head_count, head_width)
    rows = jnp.arange(token_count)
    causal = (rows[:, None] >= rows[None, :])[None]
    lead = within.T
    spread = lead[:, :, None] - lead[:, None, :]
    decay_matrix = jnp.where(causal, jnp.exp(jnp.where(causal, spread, 0.0)), 0.0)
    products = jnp.einsum("ihp,jhp->hij", cot_three, vals_three, preferred_element_type=jnp.float32)
    read_weights = (products * decay_matrix).astype(jnp.bfloat16)
    gram = jnp.einsum("in,jn->ij", read_map, write_map, preferred_element_type=jnp.float32)
    value_weights = (gram[None] * decay_matrix).astype(jnp.bfloat16)
    grad_read = jnp.einsum("hij,jn->in", read_weights, write_map, preferred_element_type=jnp.float32)
    grad_write = jnp.einsum("hij,in->jn", read_weights, read_map, preferred_element_type=jnp.float32)
    grad_values = jnp.einsum(
        "hij,ihp->jhp", value_weights, cot_three, preferred_element_type=jnp.float32
    ) + skip_gain[None, :, None] * cot_three.astype(jnp.float32)
    return grad_values.reshape(token_count, head_count * head_width), grad_write, grad_read


def xor_pairs(count, bit):
    return [(i, i ^ (1 << bit)) for i in range(count)]


def gather_totals(totals, skip_part, position, count):
    rows = jnp.arange(count)[:, None]
    table = jnp.concatenate([jnp.where(rows == position, totals[None, :], 0.0), skip_part[None, :]], 0)
    return [table]


def extend_totals(tables, count, start_bit, stop_bit):
    for bit in range(start_bit, min(stop_bit, count.bit_length() - 1)):
        tables.append(tables[-1] + lax.ppermute(tables[-1], "ctx", xor_pairs(count, bit)))


def take_half(array, upper):
    half = array.shape[-1] // 2
    return jnp.where(upper, array[..., half:], array[..., :half])


def join_halves(mine, other, upper):
    return jnp.where(upper, jnp.concatenate([other, mine], -1), jnp.concatenate([mine, other], -1))


class Direction:
    def __init__(self, tables, position, count, reverse, head_width):
        self.tables = tables
        self.count = count
        self.reverse = reverse
        self.head_width = head_width
        self.index = count - 1 - position if reverse else position
        self.upper = self.index % 2 == 1
        self.pair = self.index // 2
        self.pyramids = {}

    def actual(self, pairs):
        if self.reverse:
            return [(self.count - 1 - a, self.count - 1 - b) for a, b in pairs]
        return pairs

    def pair_pairs(self, pairs):
        return self.actual([(2 * a + j, 2 * b + j) for a, b in pairs for j in (0, 1)])

    def gain(self, table_index, low_block, size):
        key = (table_index % len(self.tables), size)
        if key not in self.pyramids:
            rows = self.tables[key[0]][: self.count]
            if self.reverse:
                rows = rows[::-1]
            grouped = rows.reshape(self.count // size, size, rows.shape[-1]).sum(axis=1)
            self.pyramids[key] = jnp.exp(grouped)
        full = lax.dynamic_index_in_dim(self.pyramids[key], low_block // size, keepdims=False)
        return spread_heads(take_half(full, self.upper), self.head_width)[..., None, :]


def exchange(payloads, pair_lists):
    results = []
    for p, pairs in zip(payloads, pair_lists):
        got = jnp.zeros_like(p)
        for parity in (0, 1):
            part = [(s, t) for s, t in pairs if s % 2 == parity]
            if part:
                got = got + lax.ppermute(p, "ctx", part)
        results.append(got)
    return results


class PairScan:
    def __init__(self, way):
        self.way = way
        self.pair_count = way.count // 2
        self.level_count = self.pair_count.bit_length() - 1
        self.flip = self.level_count >= 2
        pair = way.pair
        self.role = jnp.where(way.upper, pair ^ 1, pair) if self.flip else pair

    def device_pairs(self, pairs, first_level):
        lower = [(2 * a, 2 * b) for a, b in pairs]
        if self.flip and first_level:
            upper = [(2 * b + 1, 2 * a + 1) for a, b in pairs]
        elif self.flip:
            upper = [(2 * (a ^ 1) + 1, 2 * (b ^ 1) + 1) for a, b in pairs]
        else:
            upper = [(2 * a + 1, 2 * b + 1) for a, b in pairs]
        return self.way.actual(lower + upper)

    def pair_gain(self, level, low_pair, pair_span):
        table = min(level + 2, len(self.way.tables) - 1)
        return self.way.gain(table, 2 * low_pair, 2 * pair_span)

    def up_send(self, level):
        span = 1 << level
        pairs = [(a, a + span) for a in range(self.pair_count) if a % (2 * span) == span - 1]
        return self.device_pairs(pairs, level == 0)

    def up_combine(self, level, total, lower):
        span = 1 << level
        if self.flip and level == 0:
            pair = self.way.pair
            kept_upper = self.pair_gain(0, pair ^ 1, 1) * total + lower
            kept_lower = self.pair_gain(0, pair, 1) * lower + total
            return jnp.where(self.way.upper, kept_upper, kept_lower)
        return self.pair_gain(level, self.role - span + 1, span) * lower + total

    def down_send(self, level, prefix, pair_total):
        span = 1 << level
        if self.flip and level == 0:
            pair = self.way.pair
            sent = jnp.where(self.way.upper, self.pair_gain(0, pair, 1) * prefix + pair_total, prefix)
            pairs = [(2 * (a + 1), 2 * a) for a in range(2, self.pair_count, 2)]
            pairs += [(2 * a + 1, 2 * (a + 1) + 1) for a in range(0, self.pair_count, 2)]
            return sent, self.way.actual(pairs)
        pairs = [(a, a - span) for a in range(2 * span, self.pair_count) if a % (2 * span) == 2 * span - 1]
        return prefix, self.device_pairs(pairs, False)

    def down_combine(self, level, prefix, got, lowers):
        span = 1 << level
        if self.flip and level == 0:
            pair = self.way.pair
            grown = self.pair_gain(self.level_count, pair - 1, 1) * prefix + lowers[0]
            odd = pair % 2 == 1
            return jnp.where(self.way.upper, jnp.where(odd, got, prefix), jnp.where(odd, grown, got))
        if got is not None:
            prefix = prefix + got
        lower_gain = self.pair_gain(self.level_count, self.role - 2 * span + 1, span)
        lower_gain = jnp.where(self.role % (2 * span) == 2 * span - 1, lower_gain, 1.0)
        return lower_gain * prefix + lowers[level]


def pair_scans(ways, pair_totals):
    scans = [PairScan(way) for way in ways]
    level_count = scans[0].level_count
    if scans[0].flip:
        return shift_scans(scans, pair_totals)
    totals = list(pair_totals)
    lowers = [[] for _ in scans]
    for level in range(level_count):
        got = exchange(totals, [scan.up_send(level) for scan in scans])
        for k, scan in enumerate(scans):
            lowers[k].append(got[k])
            if level < level_count - 1:
                totals[k] = scan.up_combine(level, totals[k], got[k])
    prefixes = [jnp.zeros_like(total) for total in pair_totals]
    for level in reversed(range(level_count)):
        if level < level_count - 1:
            sends = [scan.down_send(level, p, t) for scan, p, t in zip(scans, prefixes, pair_totals)]
            got = exchange([s[0] for s in sends], [s[1] for s in sends])
        else:
            got = [None] * len(scans)
        prefixes = [
            scan.down_combine(level, p, g, low) for scan, p, g, low in zip(scans, prefixes, got, lowers)
        ]
    anchor = lowers[0][0] if level_count else pair_totals[0]
    return prefixes, anchor


def shift_scans(scans, pair_totals):
    group_count = scans[0].pair_count // 2
    got = exchange(list(pair_totals), [scan.up_send(0) for scan in scans])
    lowers = [[g] for g in got]
    through = [scan.up_combine(0, t, g) for scan, t, g in zip(scans, pair_totals, got)]
    before = [jnp.zeros_like(t) for t in pair_totals]

    def group_gain(scan, group):
        return scan.way.gain(-1, 4 * group, 4)

    span = 1
    while span < group_count:
        pairs = [(2 * g + 1, 2 * (g + span) + 1) for g in range(group_count - span)]
        got = exchange(through, [scan.device_pairs(pairs, False) for scan in scans])
        for k, scan in enumerate(scans):
            group = scan.way.pair // 2
            before_gain = 1.0
            for back in range(1, span):
                before_gain = before_gain * group_gain(scan, group - back)
            if span < group_count // 2:
                through[k] = before_gain * group_gain(scan, group) * got[k] + through[k]
            before[k] = before_gain * got[k] + before[k]
        span *= 2
    sends = [scan.down_send(0, p, t) for scan, p, t in zip(scans, before, pair_totals)]
    got = exchange([s[0] for s in sends], [s[1] for s in sends])
    prefixes = [scan.down_combine(0, p, g, low) for scan, p, g, low in zip(scans, before, got, lowers)]
    return prefixes, lowers[0][0]


def carried_pair(tables, fwd_state, adj_state, position, count, head_width):
    ways = [Direction(tables, position, count, reverse, head_width) for reverse in (False, True)]
    states = [fwd_state, adj_state]
    sent = jnp.concatenate([take_half(s, ~w.upper) for s, w in zip(states, ways)], -1)
    got = lax.ppermute(sent, "ctx", [(i, i ^ 1) for i in range(count)])
    got = [got[..., : got.shape[-1] // 2], got[..., got.shape[-1] // 2 :]]
    lows = []
    totals = []
    extend_totals(tables, count, 0, 1)
    for way, state, other in zip(ways, states, got):
        own = take_half(state, way.upper)
        low_block = jnp.where(way.upper, other, own)
        high_block = jnp.where(way.upper, own, other)
        lows.append(low_block)
        totals.append(way.gain(1, 2 * way.pair + 1, 1) * low_block + high_block)
    tables[-1], _ = lax.optimization_barrier((tables[-1], totals))
    extend_totals(tables, count, 1, count.bit_length())
    pair_prefixes, anchor = pair_scans(ways, totals)
    lifted_parts = []
    keep_parts = []
    for way, pair_prefix, low_block in zip(ways, pair_prefixes, lows):
        lifted = way.gain(1, 2 * way.pair, 1) * pair_prefix + low_block
        lifted_parts.append(jnp.where(way.upper, pair_prefix, lifted))
        keep_parts.append(jnp.where(way.upper, lifted, pair_prefix))
    got = lax.ppermute(jnp.concatenate(lifted_parts, -1), "ctx", [(i, i ^ 1) for i in range(count)])
    unit = jnp.exp(jnp.min(tables[-1]) * 0.0)
    got = got * unit
    half = got.shape[-1] // 2
    others = [got[..., :half], got[..., half:]]
    return (keep_parts, others, [way.upper for way in ways]), anchor, tables[-1]


def block_carried_grads(write_map, value_scale, decayed_vals, decayed_cot, carried, local_grads):
    local_values, local_write, local_read = local_grads
    (state_mine, adjoint_mine), (state_other, adjoint_other), (state_upper, adjoint_upper) = carried

    def rows_times(coeffs, mine, other, upper):
        return jnp.einsum(
            "iq,nq->in", take_half(coeffs, upper), mine.astype(jnp.bfloat16), preferred_element_type=jnp.float32
        ) + jnp.einsum(
            "iq,nq->in", take_half(coeffs, ~upper), other.astype(jnp.bfloat16), preferred_element_type=jnp.float32
        )

    grad_read = local_read + rows_times(decayed_cot, state_mine, state_other, state_upper)
    grad_write = local_write + rows_times(decayed_vals, adjoint_mine, adjoint_other, adjoint_upper)
    term_mine = jnp.einsum(
        "jn,nq->jq", write_map, adjoint_mine.astype(jnp.bfloat16), preferred_element_type=jnp.float32
    )
    term_other = jnp.einsum(
        "jn,nq->jq", write_map, adjoint_other.astype(jnp.bfloat16), preferred_element_type=jnp.float32
    )
    carried_term = join_halves(term_mine, term_other, adjoint_upper)
    grad_values = local_values + value_scale * carried_term
    return (
        grad_values.astype(jnp.bfloat16),
        grad_write.astype(jnp.bfloat16),
        grad_read.astype(jnp.bfloat16),
    )


def local(token_values, cotangent, write_coeffs, read_coeffs, decay_codes, skip_gain):
    seq_len = token_values.shape[1] * lax.axis_size("ctx")
    factor = 0.25 / seq_len
    prepare = jax.vmap(functools.partial(block_states, factor=factor))
    within, totals, value_scale, decayed_vals, decayed_cot, fwd_state, adj_state, skip_parts = prepare(
        token_values, cotangent, write_coeffs, read_coeffs, decay_codes
    )
    position = lax.axis_index("ctx")
    count = lax.axis_size("ctx")
    tables = jax.vmap(gather_totals, (0, 0, None, None))(totals, skip_parts, position, count)
    head_width = token_values.shape[2] // decay_codes.shape[2]
    carried, anchor, final_table = jax.vmap(carried_pair, (0, 0, 0, None, None, None))(
        tables, fwd_state, adj_state, position, count, head_width
    )
    grad_skip = jnp.sum(final_table[:, count], axis=0)
    for bit in range(lax.axis_size("dp").bit_length() - 1):
        grad_skip = grad_skip + lax.ppermute(grad_skip, "dp", xor_pairs(lax.axis_size("dp"), bit))
    local_inputs, _ = lax.optimization_barrier(
        ((token_values, cotangent, write_coeffs, read_coeffs, within), anchor)
    )
    local_grads = jax.vmap(block_local_grads, (0, 0, 0, 0, 0, None))(*local_inputs, skip_gain)
    grad_values, grad_write, grad_read = jax.vmap(block_carried_grads)(
        write_coeffs, value_scale, decayed_vals, decayed_cot, carried, local_grads
    )
    return (grad_values, grad_write, grad_read, grad_skip)


def solution(mesh):
    in_specs = (
        P("dp", "ctx", None),
        P("dp", "ctx", None),
        P("dp", "ctx", None),
        P("dp", "ctx", None),
        P("dp", "ctx", None),
        P(),
    )
    out_specs = (P("dp", "ctx", None), P("dp", "ctx", None), P("dp", "ctx", None), P())
    return jax.shard_map(local, mesh=mesh, in_specs=in_specs, out_specs=out_specs, check_vma=False)
```

```python
import functools

import jax
import jax.numpy as jnp
from jax import lax
from jax.experimental.layout import Layout, with_layout_constraint
from jax.sharding import PartitionSpec as P


def spread_heads(per_head, width):
    return jnp.repeat(per_head, width, axis=-1)


def block_states(values, cotan, write_map, read_map, codes, factor):
    head_count = codes.shape[1]
    head_width = values.shape[1] // head_count
    log_decay = -codes.astype(jnp.float32) * factor
    within = jnp.cumsum(log_decay, axis=0)
    totals = within[-1]
    value_scale = spread_heads(jnp.exp(totals - within), head_width)
    cot_scale = spread_heads(jnp.exp(within), head_width)
    decayed_vals = (values.astype(jnp.float32) * value_scale).astype(jnp.bfloat16)
    decayed_cot = (cotan.astype(jnp.float32) * cot_scale).astype(jnp.bfloat16)
    fwd_state = jnp.einsum("jn,jq->nq", write_map, decayed_vals, preferred_element_type=jnp.float32)
    adj_state = jnp.einsum("in,iq->nq", read_map, decayed_cot, preferred_element_type=jnp.float32)
    skip_part = jnp.sum(
        (values.astype(jnp.float32) * cotan.astype(jnp.float32)).reshape(
            values.shape[0], head_count, head_width
        ),
        axis=(0, 2),
    )
    return within, totals, value_scale, decayed_vals, decayed_cot, fwd_state, adj_state, skip_part


def block_local_grads(values, cotan, write_map, read_map, within, skip_gain):
    token_count = values.shape[0]
    head_count = skip_gain.shape[0]
    head_width = values.shape[1] // head_count
    vals_three = values.reshape(token_count, head_count, head_width)
    cot_three = cotan.reshape(token_count, head_count, head_width)
    rows = jnp.arange(token_count)
    causal = (rows[:, None] >= rows[None, :])[None]
    lead = within.T
    spread = lead[:, :, None] - lead[:, None, :]
    decay_matrix = jnp.where(causal, jnp.exp(jnp.where(causal, spread, 0.0)), 0.0)
    products = jnp.einsum("ihp,jhp->hij", cot_three, vals_three, preferred_element_type=jnp.float32)
    read_weights = (products * decay_matrix).astype(jnp.bfloat16)
    gram = jnp.einsum("in,jn->ij", read_map, write_map, preferred_element_type=jnp.float32)
    value_weights = (gram[None] * decay_matrix).astype(jnp.bfloat16)
    grad_read = jnp.einsum("hij,jn->in", read_weights, write_map, preferred_element_type=jnp.float32)
    grad_write = jnp.einsum("hij,in->jn", read_weights, read_map, preferred_element_type=jnp.float32)
    grad_values = jnp.einsum(
        "hij,ihp->jhp", value_weights, cot_three, preferred_element_type=jnp.float32
    ) + skip_gain[None, :, None] * cot_three.astype(jnp.float32)
    return grad_values.reshape(token_count, head_count * head_width), grad_write, grad_read


def xor_pairs(count, bit):
    return [(i, i ^ (1 << bit)) for i in range(count)]


def gather_totals(totals, skip_part, position, count):
    rows = jnp.arange(count)[:, None]
    table = jnp.concatenate([jnp.where(rows == position, totals[None, :], 0.0), skip_part[None, :]], 0)
    return [table]


def extend_totals(tables, count, start_bit, stop_bit):
    for bit in range(start_bit, min(stop_bit, count.bit_length() - 1)):
        tables.append(tables[-1] + lax.ppermute(tables[-1], "ctx", xor_pairs(count, bit)))


def take_half(array, upper):
    half = array.shape[-1] // 2
    return jnp.where(upper, array[..., half:], array[..., :half])


def join_halves(mine, other, upper):
    return jnp.where(upper, jnp.concatenate([other, mine], -1), jnp.concatenate([mine, other], -1))


class Direction:
    def __init__(self, tables, position, count, reverse, head_width):
        self.tables = tables
        self.count = count
        self.reverse = reverse
        self.head_width = head_width
        self.index = count - 1 - position if reverse else position
        self.upper = self.index % 2 == 1
        self.pair = self.index // 2
        self.pyramids = {}

    def actual(self, pairs):
        if self.reverse:
            return [(self.count - 1 - a, self.count - 1 - b) for a, b in pairs]
        return pairs

    def pair_pairs(self, pairs):
        return self.actual([(2 * a + j, 2 * b + j) for a, b in pairs for j in (0, 1)])

    def gain(self, table_index, low_block, size):
        key = (table_index % len(self.tables), size)
        if key not in self.pyramids:
            rows = self.tables[key[0]][: self.count]
            if self.reverse:
                rows = rows[::-1]
            grouped = rows.reshape(self.count // size, size, rows.shape[-1]).sum(axis=1)
            self.pyramids[key] = jnp.exp(grouped)
        full = lax.dynamic_index_in_dim(self.pyramids[key], low_block // size, keepdims=False)
        return spread_heads(take_half(full, self.upper), self.head_width)[..., None, :]


def exchange(payloads, pair_lists):
    return [
        lax.ppermute(p, "ctx", pairs) if pairs else jnp.zeros_like(p) for p, pairs in zip(payloads, pair_lists)
    ]


class PairScan:
    def __init__(self, way):
        self.way = way
        self.pair_count = way.count // 2
        self.level_count = self.pair_count.bit_length() - 1
        self.flip = self.level_count >= 2
        pair = way.pair
        self.role = jnp.where(way.upper, pair ^ 1, pair) if self.flip else pair

    def device_pairs(self, pairs, first_level):
        lower = [(2 * a, 2 * b) for a, b in pairs]
        if self.flip and first_level:
            upper = [(2 * b + 1, 2 * a + 1) for a, b in pairs]
        elif self.flip:
            upper = [(2 * (a ^ 1) + 1, 2 * (b ^ 1) + 1) for a, b in pairs]
        else:
            upper = [(2 * a + 1, 2 * b + 1) for a, b in pairs]
        return self.way.actual(lower + upper)

    def pair_gain(self, level, low_pair, pair_span):
        table = min(level + 2, len(self.way.tables) - 1)
        return self.way.gain(table, 2 * low_pair, 2 * pair_span)

    def up_send(self, level):
        span = 1 << level
        pairs = [(a, a + span) for a in range(self.pair_count) if a % (2 * span) == span - 1]
        return self.device_pairs(pairs, level == 0)

    def up_combine(self, level, total, lower):
        span = 1 << level
        if self.flip and level == 0:
            pair = self.way.pair
            kept_upper = self.pair_gain(0, pair ^ 1, 1) * total + lower
            kept_lower = self.pair_gain(0, pair, 1) * lower + total
            return jnp.where(self.way.upper, kept_upper, kept_lower)
        return self.pair_gain(level, self.role - span + 1, span) * lower + total

    def down_send(self, level, prefix, pair_total):
        span = 1 << level
        if self.flip and level == 0:
            pair = self.way.pair
            sent = jnp.where(self.way.upper, self.pair_gain(0, pair, 1) * prefix + pair_total, prefix)
            pairs = [(2 * (a + 1), 2 * a) for a in range(2, self.pair_count, 2)]
            pairs += [(2 * a + 1, 2 * (a + 1) + 1) for a in range(0, self.pair_count, 2)]
            return sent, self.way.actual(pairs)
        pairs = [(a, a - span) for a in range(2 * span, self.pair_count) if a % (2 * span) == 2 * span - 1]
        return prefix, self.device_pairs(pairs, False)

    def down_combine(self, level, prefix, got, lowers):
        span = 1 << level
        if self.flip and level == 0:
            pair = self.way.pair
            grown = self.pair_gain(self.level_count, pair - 1, 1) * prefix + lowers[0]
            odd = pair % 2 == 1
            return jnp.where(self.way.upper, jnp.where(odd, got, prefix), jnp.where(odd, grown, got))
        if got is not None:
            prefix = prefix + got
        lower_gain = self.pair_gain(self.level_count, self.role - 2 * span + 1, span)
        lower_gain = jnp.where(self.role % (2 * span) == 2 * span - 1, lower_gain, 1.0)
        return lower_gain * prefix + lowers[level]


def pair_scans(ways, pair_totals):
    scans = [PairScan(way) for way in ways]
    level_count = scans[0].level_count
    if scans[0].flip:
        return shift_scans(scans, pair_totals)
    totals = list(pair_totals)
    lowers = [[] for _ in scans]
    for level in range(level_count):
        got = exchange(totals, [scan.up_send(level) for scan in scans])
        for k, scan in enumerate(scans):
            lowers[k].append(got[k])
            if level < level_count - 1:
                totals[k] = scan.up_combine(level, totals[k], got[k])
    prefixes = [jnp.zeros_like(total) for total in pair_totals]
    for level in reversed(range(level_count)):
        if level < level_count - 1:
            sends = [scan.down_send(level, p, t) for scan, p, t in zip(scans, prefixes, pair_totals)]
            got = exchange([s[0] for s in sends], [s[1] for s in sends])
        else:
            got = [None] * len(scans)
        prefixes = [
            scan.down_combine(level, p, g, low) for scan, p, g, low in zip(scans, prefixes, got, lowers)
        ]
    anchor = lowers[0][0] if level_count else pair_totals[0]
    return prefixes, anchor


def shift_scans(scans, pair_totals):
    group_count = scans[0].pair_count // 2
    got = exchange(list(pair_totals), [scan.up_send(0) for scan in scans])
    lowers = [[g] for g in got]
    through = [scan.up_combine(0, t, g) for scan, t, g in zip(scans, pair_totals, got)]
    before = [jnp.zeros_like(t) for t in pair_totals]

    def group_gain(scan, group):
        return scan.way.gain(-1, 4 * group, 4)

    span = 1
    while span < group_count:
        pairs = [(2 * g + 1, 2 * (g + span) + 1) for g in range(group_count - span)]
        got = exchange(through, [scan.device_pairs(pairs, False) for scan in scans])
        for k, scan in enumerate(scans):
            group = scan.way.pair // 2
            before_gain = 1.0
            for back in range(1, span):
                before_gain = before_gain * group_gain(scan, group - back)
            if span < group_count // 2:
                through[k] = before_gain * group_gain(scan, group) * got[k] + through[k]
            before[k] = before_gain * got[k] + before[k]
        span *= 2
    sends = [scan.down_send(0, p, t) for scan, p, t in zip(scans, before, pair_totals)]
    got = exchange([s[0] for s in sends], [s[1] for s in sends])
    prefixes = [scan.down_combine(0, p, g, low) for scan, p, g, low in zip(scans, before, got, lowers)]
    return prefixes, lowers[0][0]


def carried_pair(tables, fwd_state, adj_state, position, count, head_width):
    ways = [Direction(tables, position, count, reverse, head_width) for reverse in (False, True)]
    states = [fwd_state, adj_state]
    sent = jnp.concatenate([take_half(s, ~w.upper) for s, w in zip(states, ways)], -1)
    got = lax.ppermute(sent, "ctx", [(i, i ^ 1) for i in range(count)])
    got = [got[..., : got.shape[-1] // 2], got[..., got.shape[-1] // 2 :]]
    lows = []
    totals = []
    extend_totals(tables, count, 0, 1)
    for way, state, other in zip(ways, states, got):
        own = take_half(state, way.upper)
        low_block = jnp.where(way.upper, other, own)
        high_block = jnp.where(way.upper, own, other)
        lows.append(low_block)
        totals.append(way.gain(1, 2 * way.pair + 1, 1) * low_block + high_block)
    tables[-1], _ = lax.optimization_barrier((tables[-1], totals))
    extend_totals(tables, count, 1, count.bit_length())
    pair_prefixes, anchor = pair_scans(ways, totals)
    lifted_parts = []
    keep_parts = []
    for way, pair_prefix, low_block in zip(ways, pair_prefixes, lows):
        lifted = way.gain(1, 2 * way.pair, 1) * pair_prefix + low_block
        lifted_parts.append(jnp.where(way.upper, pair_prefix, lifted))
        keep_parts.append(jnp.where(way.upper, lifted, pair_prefix))
    got = lax.ppermute(jnp.concatenate(lifted_parts, -1), "ctx", [(i, i ^ 1) for i in range(count)])
    unit = jnp.exp(jnp.min(tables[-1]) * 0.0)
    got = got * unit
    half = got.shape[-1] // 2
    others = [got[..., :half], got[..., half:]]
    return (keep_parts, others, [way.upper for way in ways]), anchor, tables[-1]


def block_carried_grads(write_map, value_scale, decayed_vals, decayed_cot, carried, local_grads):
    local_values, local_write, local_read = local_grads
    (state_mine, adjoint_mine), (state_other, adjoint_other), (state_upper, adjoint_upper) = carried

    def rows_times(coeffs, mine, other, upper):
        return jnp.einsum(
            "iq,nq->in", take_half(coeffs, upper), mine.astype(jnp.bfloat16), preferred_element_type=jnp.float32
        ) + jnp.einsum(
            "iq,nq->in", take_half(coeffs, ~upper), other.astype(jnp.bfloat16), preferred_element_type=jnp.float32
        )

    grad_read = local_read + rows_times(decayed_cot, state_mine, state_other, state_upper)
    grad_write = local_write + rows_times(decayed_vals, adjoint_mine, adjoint_other, adjoint_upper)
    term_mine = jnp.einsum(
        "jn,nq->jq", write_map, adjoint_mine.astype(jnp.bfloat16), preferred_element_type=jnp.float32
    )
    term_other = jnp.einsum(
        "jn,nq->jq", write_map, adjoint_other.astype(jnp.bfloat16), preferred_element_type=jnp.float32
    )
    carried_term = join_halves(term_mine, term_other, adjoint_upper)
    grad_values = local_values + value_scale * carried_term
    return (
        grad_values.astype(jnp.bfloat16),
        grad_write.astype(jnp.bfloat16),
        grad_read.astype(jnp.bfloat16),
    )


def local(token_values, cotangent, write_coeffs, read_coeffs, decay_codes, skip_gain):
    seq_len = token_values.shape[1] * lax.axis_size("ctx")
    factor = 0.25 / seq_len
    prepare = jax.vmap(functools.partial(block_states, factor=factor))
    within, totals, value_scale, decayed_vals, decayed_cot, fwd_state, adj_state, skip_parts = prepare(
        token_values, cotangent, write_coeffs, read_coeffs, decay_codes
    )
    position = lax.axis_index("ctx")
    count = lax.axis_size("ctx")
    tables = jax.vmap(gather_totals, (0, 0, None, None))(totals, skip_parts, position, count)
    head_width = token_values.shape[2] // decay_codes.shape[2]
    carried, anchor, final_table = jax.vmap(carried_pair, (0, 0, 0, None, None, None))(
        tables, fwd_state, adj_state, position, count, head_width
    )
    grad_skip = jnp.sum(final_table[:, count], axis=0)
    for bit in range(lax.axis_size("dp").bit_length() - 1):
        grad_skip = grad_skip + lax.ppermute(grad_skip, "dp", xor_pairs(lax.axis_size("dp"), bit))
    local_inputs, _ = lax.optimization_barrier(
        ((token_values, cotangent, write_coeffs, read_coeffs, within), anchor)
    )
    local_grads = jax.vmap(block_local_grads, (0, 0, 0, 0, 0, None))(*local_inputs, skip_gain)
    grad_values, grad_write, grad_read = jax.vmap(block_carried_grads)(
        write_coeffs, value_scale, decayed_vals, decayed_cot, carried, local_grads
    )
    grad_values = with_layout_constraint(grad_values, Layout(major_to_minor=tuple(range(grad_values.ndim))))
    return (grad_values, grad_write, grad_read, grad_skip)


def solution(mesh):
    in_specs = (
        P("dp", "ctx", None),
        P("dp", "ctx", None),
        P("dp", "ctx", None),
        P("dp", "ctx", None),
        P("dp", "ctx", None),
        P(),
    )
    out_specs = (P("dp", "ctx", None), P("dp", "ctx", None), P("dp", "ctx", None), P())
    return jax.shard_map(local, mesh=mesh, in_specs=in_specs, out_specs=out_specs, check_vma=False)
```

```python
import functools

import jax
import jax.numpy as jnp
from jax import lax
from jax.experimental.layout import Layout, with_layout_constraint
from jax.sharding import PartitionSpec as P


def spread_heads(per_head, width):
    return jnp.repeat(per_head, width, axis=-1)


def block_states(values, cotan, write_map, read_map, codes, factor):
    head_count = codes.shape[1]
    head_width = values.shape[1] // head_count
    log_decay = -codes.astype(jnp.float32) * factor
    within = jnp.cumsum(log_decay, axis=0)
    totals = within[-1]
    value_scale = spread_heads(jnp.exp(totals - within), head_width)
    cot_scale = spread_heads(jnp.exp(within), head_width)
    decayed_vals = (values.astype(jnp.float32) * value_scale).astype(jnp.bfloat16)
    decayed_cot = (cotan.astype(jnp.float32) * cot_scale).astype(jnp.bfloat16)
    fwd_state = jnp.einsum("jn,jq->nq", write_map, decayed_vals, preferred_element_type=jnp.float32)
    adj_state = jnp.einsum("in,iq->nq", read_map, decayed_cot, preferred_element_type=jnp.float32)
    skip_part = jnp.sum(
        (values.astype(jnp.float32) * cotan.astype(jnp.float32)).reshape(
            values.shape[0], head_count, head_width
        ),
        axis=(0, 2),
    )
    return within, totals, value_scale, decayed_vals, decayed_cot, fwd_state, adj_state, skip_part


def block_local_grads(values, cotan, write_map, read_map, within, skip_gain):
    token_count = values.shape[0]
    head_count = skip_gain.shape[0]
    head_width = values.shape[1] // head_count
    vals_three = values.reshape(token_count, head_count, head_width)
    cot_three = cotan.reshape(token_count, head_count, head_width)
    rows = jnp.arange(token_count)
    causal = (rows[:, None] >= rows[None, :])[None]
    lead = within.T
    spread = lead[:, :, None] - lead[:, None, :]
    decay_matrix = jnp.where(causal, jnp.exp(jnp.where(causal, spread, 0.0)), 0.0)
    products = jnp.einsum("ihp,jhp->hij", cot_three, vals_three, preferred_element_type=jnp.float32)
    read_weights = (products * decay_matrix).astype(jnp.bfloat16)
    gram = jnp.einsum("in,jn->ij", read_map, write_map, preferred_element_type=jnp.float32)
    value_weights = (gram[None] * decay_matrix).astype(jnp.bfloat16)
    grad_read = jnp.einsum("hij,jn->in", read_weights, write_map, preferred_element_type=jnp.float32)
    grad_write = jnp.einsum("hij,in->jn", read_weights, read_map, preferred_element_type=jnp.float32)
    grad_values = jnp.einsum(
        "hij,ihp->jhp", value_weights, cot_three, preferred_element_type=jnp.float32
    ) + skip_gain[None, :, None] * cot_three.astype(jnp.float32)
    return grad_values.reshape(token_count, head_count * head_width), grad_write, grad_read


def xor_pairs(count, bit):
    return [(i, i ^ (1 << bit)) for i in range(count)]


def gather_totals(totals, skip_part, position, count):
    rows = jnp.arange(count)[:, None]
    table = jnp.concatenate([jnp.where(rows == position, totals[None, :], 0.0), skip_part[None, :]], 0)
    return [table]


def extend_totals(tables, count, start_bit, stop_bit):
    for bit in range(start_bit, min(stop_bit, count.bit_length() - 1)):
        tables.append(tables[-1] + lax.ppermute(tables[-1], "ctx", xor_pairs(count, bit)))


def take_half(array, upper):
    half = array.shape[-1] // 2
    return jnp.where(upper, array[..., half:], array[..., :half])


def join_halves(mine, other, upper):
    return jnp.where(upper, jnp.concatenate([other, mine], -1), jnp.concatenate([mine, other], -1))


class Direction:
    def __init__(self, tables, position, count, reverse, head_width):
        self.tables = tables
        self.count = count
        self.reverse = reverse
        self.head_width = head_width
        self.index = count - 1 - position if reverse else position
        self.upper = self.index % 2 == 1
        self.pair = self.index // 2
        self.pyramids = {}

    def actual(self, pairs):
        if self.reverse:
            return [(self.count - 1 - a, self.count - 1 - b) for a, b in pairs]
        return pairs

    def pair_pairs(self, pairs):
        return self.actual([(2 * a + j, 2 * b + j) for a, b in pairs for j in (0, 1)])

    def gain(self, table_index, low_block, size):
        key = (table_index % len(self.tables), size)
        if key not in self.pyramids:
            rows = self.tables[key[0]][: self.count]
            if self.reverse:
                rows = rows[::-1]
            grouped = rows.reshape(self.count // size, size, rows.shape[-1]).sum(axis=1)
            self.pyramids[key] = jnp.exp(grouped)
        full = lax.dynamic_index_in_dim(self.pyramids[key], low_block // size, keepdims=False)
        return spread_heads(take_half(full, self.upper), self.head_width)[..., None, :]


def exchange(payloads, pair_lists):
    return [
        lax.ppermute(p, "ctx", pairs) if pairs else jnp.zeros_like(p) for p, pairs in zip(payloads, pair_lists)
    ]


class PairScan:
    def __init__(self, way):
        self.way = way
        self.pair_count = way.count // 2
        self.level_count = self.pair_count.bit_length() - 1
        self.flip = self.level_count >= 2
        pair = way.pair
        self.role = jnp.where(way.upper, pair ^ 1, pair) if self.flip else pair

    def device_pairs(self, pairs, first_level):
        lower = [(2 * a, 2 * b) for a, b in pairs]
        if self.flip and first_level:
            upper = [(2 * b + 1, 2 * a + 1) for a, b in pairs]
        elif self.flip:
            upper = [(2 * (a ^ 1) + 1, 2 * (b ^ 1) + 1) for a, b in pairs]
        else:
            upper = [(2 * a + 1, 2 * b + 1) for a, b in pairs]
        return self.way.actual(lower + upper)

    def pair_gain(self, level, low_pair, pair_span):
        table = min(level + 2, len(self.way.tables) - 1)
        return self.way.gain(table, 2 * low_pair, 2 * pair_span)

    def up_send(self, level):
        span = 1 << level
        pairs = [(a, a + span) for a in range(self.pair_count) if a % (2 * span) == span - 1]
        return self.device_pairs(pairs, level == 0)

    def up_combine(self, level, total, lower):
        span = 1 << level
        if self.flip and level == 0:
            pair = self.way.pair
            kept_upper = self.pair_gain(0, pair ^ 1, 1) * total + lower
            kept_lower = self.pair_gain(0, pair, 1) * lower + total
            return jnp.where(self.way.upper, kept_upper, kept_lower)
        return self.pair_gain(level, self.role - span + 1, span) * lower + total

    def down_send(self, level, prefix, pair_total):
        span = 1 << level
        if self.flip and level == 0:
            pair = self.way.pair
            sent = jnp.where(self.way.upper, self.pair_gain(0, pair, 1) * prefix + pair_total, prefix)
            pairs = [(2 * (a + 1), 2 * a) for a in range(2, self.pair_count, 2)]
            pairs += [(2 * a + 1, 2 * (a + 1) + 1) for a in range(0, self.pair_count, 2)]
            return sent, self.way.actual(pairs)
        pairs = [(a, a - span) for a in range(2 * span, self.pair_count) if a % (2 * span) == 2 * span - 1]
        return prefix, self.device_pairs(pairs, False)

    def down_combine(self, level, prefix, got, lowers):
        span = 1 << level
        if self.flip and level == 0:
            pair = self.way.pair
            grown = self.pair_gain(self.level_count, pair - 1, 1) * prefix + lowers[0]
            odd = pair % 2 == 1
            return jnp.where(self.way.upper, jnp.where(odd, got, prefix), jnp.where(odd, grown, got))
        if got is not None:
            prefix = prefix + got
        lower_gain = self.pair_gain(self.level_count, self.role - 2 * span + 1, span)
        lower_gain = jnp.where(self.role % (2 * span) == 2 * span - 1, lower_gain, 1.0)
        return lower_gain * prefix + lowers[level]


def pair_scans(ways, pair_totals):
    scans = [PairScan(way) for way in ways]
    level_count = scans[0].level_count
    if scans[0].flip:
        return shift_scans(scans, pair_totals)
    totals = list(pair_totals)
    lowers = [[] for _ in scans]
    for level in range(level_count):
        got = exchange(totals, [scan.up_send(level) for scan in scans])
        for k, scan in enumerate(scans):
            lowers[k].append(got[k])
            if level < level_count - 1:
                totals[k] = scan.up_combine(level, totals[k], got[k])
    prefixes = [jnp.zeros_like(total) for total in pair_totals]
    for level in reversed(range(level_count)):
        if level < level_count - 1:
            sends = [scan.down_send(level, p, t) for scan, p, t in zip(scans, prefixes, pair_totals)]
            got = exchange([s[0] for s in sends], [s[1] for s in sends])
        else:
            got = [None] * len(scans)
        prefixes = [
            scan.down_combine(level, p, g, low) for scan, p, g, low in zip(scans, prefixes, got, lowers)
        ]
    anchor = lowers[0][0] if level_count else pair_totals[0]
    return prefixes, anchor


def shift_scans(scans, pair_totals):
    group_count = scans[0].pair_count // 2
    got = exchange(list(pair_totals), [scan.up_send(0) for scan in scans])
    lowers = [[g] for g in got]
    through = [scan.up_combine(0, t, g) for scan, t, g in zip(scans, pair_totals, got)]
    before = [jnp.zeros_like(t) for t in pair_totals]

    def group_gain(scan, group):
        return scan.way.gain(-1, 4 * group, 4)

    span = 1
    while span < group_count:
        pairs = [(2 * g + 1, 2 * (g + span) + 1) for g in range(group_count - span)]
        got = exchange(through, [scan.device_pairs(pairs, False) for scan in scans])
        for k, scan in enumerate(scans):
            group = scan.way.pair // 2
            before_gain = 1.0
            for back in range(1, span):
                before_gain = before_gain * group_gain(scan, group - back)
            if span < group_count // 2:
                through[k] = before_gain * group_gain(scan, group) * got[k] + through[k]
            before[k] = before_gain * got[k] + before[k]
        span *= 2
    sends = [scan.down_send(0, p, t) for scan, p, t in zip(scans, before, pair_totals)]
    got = exchange([s[0] for s in sends], [s[1] for s in sends])
    prefixes = [scan.down_combine(0, p, g, low) for scan, p, g, low in zip(scans, before, got, lowers)]
    return prefixes, lowers[0][0]


def carried_pair(tables, fwd_state, adj_state, position, count, head_width):
    ways = [Direction(tables, position, count, reverse, head_width) for reverse in (False, True)]
    states = [fwd_state, adj_state]
    sent = jnp.concatenate([take_half(s, ~w.upper) for s, w in zip(states, ways)], -1)
    got = lax.ppermute(sent, "ctx", [(i, i ^ 1) for i in range(count)])
    got = [got[..., : got.shape[-1] // 2], got[..., got.shape[-1] // 2 :]]
    lows = []
    totals = []
    extend_totals(tables, count, 0, 1)
    for way, state, other in zip(ways, states, got):
        own = take_half(state, way.upper)
        low_block = jnp.where(way.upper, other, own)
        high_block = jnp.where(way.upper, own, other)
        lows.append(low_block)
        totals.append(way.gain(1, 2 * way.pair + 1, 1) * low_block + high_block)
    tables[-1], _ = lax.optimization_barrier((tables[-1], totals))
    extend_totals(tables, count, 1, count.bit_length())
    pair_prefixes, anchor = pair_scans(ways, totals)
    lifted_parts = []
    keep_parts = []
    for way, pair_prefix, low_block in zip(ways, pair_prefixes, lows):
        lifted = way.gain(1, 2 * way.pair, 1) * pair_prefix + low_block
        lifted_parts.append(jnp.where(way.upper, pair_prefix, lifted))
        keep_parts.append(jnp.where(way.upper, lifted, pair_prefix))
    got = lax.ppermute(jnp.concatenate(lifted_parts, -1), "ctx", [(i, i ^ 1) for i in range(count)])
    unit = jnp.exp(jnp.min(tables[-1]) * 0.0)
    got = got * unit
    half = got.shape[-1] // 2
    others = [got[..., :half], got[..., half:]]
    return (keep_parts, others, [way.upper for way in ways]), anchor, tables[-1]


def block_carried_grads(write_map, value_scale, decayed_vals, decayed_cot, carried, local_grads):
    local_values, local_write, local_read = local_grads
    (state_mine, adjoint_mine), (state_other, adjoint_other), (state_upper, adjoint_upper) = carried

    def rows_times(coeffs, mine, other, upper):
        return jnp.einsum(
            "iq,nq->in", take_half(coeffs, upper), mine.astype(jnp.bfloat16), preferred_element_type=jnp.float32
        ) + jnp.einsum(
            "iq,nq->in", take_half(coeffs, ~upper), other.astype(jnp.bfloat16), preferred_element_type=jnp.float32
        )

    grad_read = local_read + rows_times(decayed_cot, state_mine, state_other, state_upper)
    grad_write = local_write + rows_times(decayed_vals, adjoint_mine, adjoint_other, adjoint_upper)
    term_mine = jnp.einsum(
        "jn,nq->jq", write_map, adjoint_mine.astype(jnp.bfloat16), preferred_element_type=jnp.float32
    )
    term_other = jnp.einsum(
        "jn,nq->jq", write_map, adjoint_other.astype(jnp.bfloat16), preferred_element_type=jnp.float32
    )
    carried_term = join_halves(term_mine, term_other, adjoint_upper)
    grad_values = local_values + value_scale * carried_term
    return (
        grad_values.astype(jnp.bfloat16),
        grad_write.astype(jnp.bfloat16),
        grad_read.astype(jnp.bfloat16),
    )


def local(token_values, cotangent, write_coeffs, read_coeffs, decay_codes, skip_gain):
    seq_len = token_values.shape[1] * lax.axis_size("ctx")
    factor = 0.25 / seq_len
    prepare = jax.vmap(functools.partial(block_states, factor=factor))
    within, totals, value_scale, decayed_vals, decayed_cot, fwd_state, adj_state, skip_parts = prepare(
        token_values, cotangent, write_coeffs, read_coeffs, decay_codes
    )
    row_major = Layout(major_to_minor=tuple(range(decayed_vals.ndim)))
    decayed_vals = with_layout_constraint(decayed_vals, row_major)
    decayed_cot = with_layout_constraint(decayed_cot, row_major)
    position = lax.axis_index("ctx")
    count = lax.axis_size("ctx")
    tables = jax.vmap(gather_totals, (0, 0, None, None))(totals, skip_parts, position, count)
    head_width = token_values.shape[2] // decay_codes.shape[2]
    carried, anchor, final_table = jax.vmap(carried_pair, (0, 0, 0, None, None, None))(
        tables, fwd_state, adj_state, position, count, head_width
    )
    grad_skip = jnp.sum(final_table[:, count], axis=0)
    for bit in range(lax.axis_size("dp").bit_length() - 1):
        grad_skip = grad_skip + lax.ppermute(grad_skip, "dp", xor_pairs(lax.axis_size("dp"), bit))
    local_inputs, _ = lax.optimization_barrier(
        ((token_values, cotangent, write_coeffs, read_coeffs, within), anchor)
    )
    local_grads = jax.vmap(block_local_grads, (0, 0, 0, 0, 0, None))(*local_inputs, skip_gain)
    grad_values, grad_write, grad_read = jax.vmap(block_carried_grads)(
        write_coeffs, value_scale, decayed_vals, decayed_cot, carried, local_grads
    )
    grad_values = with_layout_constraint(grad_values, Layout(major_to_minor=tuple(range(grad_values.ndim))))
    return (grad_values, grad_write, grad_read, grad_skip)


def solution(mesh):
    in_specs = (
        P("dp", "ctx", None),
        P("dp", "ctx", None),
        P("dp", "ctx", None),
        P("dp", "ctx", None),
        P("dp", "ctx", None),
        P(),
    )
    out_specs = (P("dp", "ctx", None), P("dp", "ctx", None), P("dp", "ctx", None), P())
    return jax.shard_map(local, mesh=mesh, in_specs=in_specs, out_specs=out_specs, check_vma=False)
```

```python
import functools

import jax
import jax.numpy as jnp
from jax import lax
from jax.sharding import PartitionSpec as P


def spread_heads(per_head, width):
    return jnp.repeat(per_head, width, axis=-1)


def block_states(values, cotan, write_map, read_map, codes, factor):
    head_count = codes.shape[1]
    head_width = values.shape[1] // head_count
    log_decay = -codes.astype(jnp.float32) * factor
    within = jnp.cumsum(log_decay, axis=0)
    totals = within[-1]
    value_scale = spread_heads(jnp.exp(totals - within), head_width)
    cot_scale = spread_heads(jnp.exp(within), head_width)
    decayed_vals = (values.astype(jnp.float32) * value_scale).astype(jnp.bfloat16)
    decayed_cot = (cotan.astype(jnp.float32) * cot_scale).astype(jnp.bfloat16)
    fwd_state = jnp.einsum("jn,jq->nq", write_map, decayed_vals, preferred_element_type=jnp.float32)
    adj_state = jnp.einsum("in,iq->nq", read_map, decayed_cot, preferred_element_type=jnp.float32)
    skip_part = jnp.sum(
        (values.astype(jnp.float32) * cotan.astype(jnp.float32)).reshape(
            values.shape[0], head_count, head_width
        ),
        axis=(0, 2),
    )
    return within, totals, value_scale, decayed_vals, decayed_cot, fwd_state, adj_state, skip_part


def block_local_grads(values, cotan, write_map, read_map, within, skip_gain):
    token_count = values.shape[0]
    head_count = skip_gain.shape[0]
    head_width = values.shape[1] // head_count
    vals_three = values.reshape(token_count, head_count, head_width)
    cot_three = cotan.reshape(token_count, head_count, head_width)
    rows = jnp.arange(token_count)
    causal = (rows[:, None] >= rows[None, :])[None]
    lead = within.T
    spread = lead[:, :, None] - lead[:, None, :]
    decay_matrix = jnp.where(causal, jnp.exp(jnp.where(causal, spread, 0.0)), 0.0)
    products = jnp.einsum("ihp,jhp->hij", cot_three, vals_three, preferred_element_type=jnp.float32)
    read_weights = (products * decay_matrix).astype(jnp.bfloat16)
    gram = jnp.einsum("in,jn->ij", read_map, write_map, preferred_element_type=jnp.float32)
    value_weights = (gram[None] * decay_matrix).astype(jnp.bfloat16)
    grad_read = jnp.einsum("hij,jn->in", read_weights, write_map, preferred_element_type=jnp.float32)
    grad_write = jnp.einsum("hij,in->jn", read_weights, read_map, preferred_element_type=jnp.float32)
    grad_values = jnp.einsum(
        "hij,ihp->jhp", value_weights, cot_three, preferred_element_type=jnp.float32
    ) + skip_gain[None, :, None] * cot_three.astype(jnp.float32)
    return grad_values.reshape(token_count, head_count * head_width), grad_write, grad_read


def xor_pairs(count, bit):
    return [(i, i ^ (1 << bit)) for i in range(count)]


def gather_totals(totals, skip_part, position, count):
    rows = jnp.arange(count)[:, None]
    table = jnp.concatenate([jnp.where(rows == position, totals[None, :], 0.0), skip_part[None, :]], 0)
    return [table]


def extend_totals(tables, count, start_bit, stop_bit):
    for bit in range(start_bit, min(stop_bit, count.bit_length() - 1)):
        tables.append(tables[-1] + lax.ppermute(tables[-1], "ctx", xor_pairs(count, bit)))


def take_half(array, upper):
    half = array.shape[-1] // 2
    return jnp.where(upper, array[..., half:], array[..., :half])


def join_halves(mine, other, upper):
    return jnp.where(upper, jnp.concatenate([other, mine], -1), jnp.concatenate([mine, other], -1))


class Direction:
    def __init__(self, tables, position, count, reverse, head_width):
        self.tables = tables
        self.count = count
        self.reverse = reverse
        self.head_width = head_width
        self.index = count - 1 - position if reverse else position
        self.upper = self.index % 2 == 1
        self.pair = self.index // 2
        self.pyramids = {}

    def actual(self, pairs):
        if self.reverse:
            return [(self.count - 1 - a, self.count - 1 - b) for a, b in pairs]
        return pairs

    def pair_pairs(self, pairs):
        return self.actual([(2 * a + j, 2 * b + j) for a, b in pairs for j in (0, 1)])

    def gain(self, table_index, low_block, size):
        key = (table_index % len(self.tables), size)
        if key not in self.pyramids:
            rows = self.tables[key[0]][: self.count]
            if self.reverse:
                rows = rows[::-1]
            grouped = rows.reshape(self.count // size, size, rows.shape[-1]).sum(axis=1)
            self.pyramids[key] = jnp.exp(grouped)
        full = lax.dynamic_index_in_dim(self.pyramids[key], low_block // size, keepdims=False)
        return spread_heads(take_half(full, self.upper), self.head_width)[..., None, :]


def exchange(payloads, pair_lists):
    return [
        lax.ppermute(p, "ctx", pairs) if pairs else jnp.zeros_like(p) for p, pairs in zip(payloads, pair_lists)
    ]


class PairScan:
    def __init__(self, way):
        self.way = way
        self.pair_count = way.count // 2
        self.level_count = self.pair_count.bit_length() - 1
        self.flip = self.level_count >= 2
        pair = way.pair
        self.role = jnp.where(way.upper, pair ^ 1, pair) if self.flip else pair

    def device_pairs(self, pairs, first_level):
        lower = [(2 * a, 2 * b) for a, b in pairs]
        if self.flip and first_level:
            upper = [(2 * b + 1, 2 * a + 1) for a, b in pairs]
        elif self.flip:
            upper = [(2 * (a ^ 1) + 1, 2 * (b ^ 1) + 1) for a, b in pairs]
        else:
            upper = [(2 * a + 1, 2 * b + 1) for a, b in pairs]
        return self.way.actual(lower + upper)

    def pair_gain(self, level, low_pair, pair_span):
        table = min(level + 2, len(self.way.tables) - 1)
        return self.way.gain(table, 2 * low_pair, 2 * pair_span)

    def up_send(self, level):
        span = 1 << level
        pairs = [(a, a + span) for a in range(self.pair_count) if a % (2 * span) == span - 1]
        return self.device_pairs(pairs, level == 0)

    def up_combine(self, level, total, lower):
        span = 1 << level
        if self.flip and level == 0:
            pair = self.way.pair
            kept_upper = self.pair_gain(0, pair ^ 1, 1) * total + lower
            kept_lower = self.pair_gain(0, pair, 1) * lower + total
            return jnp.where(self.way.upper, kept_upper, kept_lower)
        return self.pair_gain(level, self.role - span + 1, span) * lower + total

    def down_send(self, level, prefix, pair_total):
        span = 1 << level
        if self.flip and level == 0:
            pair = self.way.pair
            sent = jnp.where(self.way.upper, self.pair_gain(0, pair, 1) * prefix + pair_total, prefix)
            pairs = [(2 * (a + 1), 2 * a) for a in range(2, self.pair_count, 2)]
            pairs += [(2 * a + 1, 2 * (a + 1) + 1) for a in range(0, self.pair_count, 2)]
            return sent, self.way.actual(pairs)
        pairs = [(a, a - span) for a in range(2 * span, self.pair_count) if a % (2 * span) == 2 * span - 1]
        return prefix, self.device_pairs(pairs, False)

    def down_combine(self, level, prefix, got, lowers):
        span = 1 << level
        if self.flip and level == 0:
            pair = self.way.pair
            grown = self.pair_gain(self.level_count, pair - 1, 1) * prefix + lowers[0]
            odd = pair % 2 == 1
            return jnp.where(self.way.upper, jnp.where(odd, got, prefix), jnp.where(odd, grown, got))
        if got is not None:
            prefix = prefix + got
        lower_gain = self.pair_gain(self.level_count, self.role - 2 * span + 1, span)
        lower_gain = jnp.where(self.role % (2 * span) == 2 * span - 1, lower_gain, 1.0)
        return lower_gain * prefix + lowers[level]


def pair_scans(ways, pair_totals):
    scans = [PairScan(way) for way in ways]
    level_count = scans[0].level_count
    if scans[0].flip:
        return shift_scans(scans, pair_totals)
    totals = list(pair_totals)
    lowers = [[] for _ in scans]
    for level in range(level_count):
        got = exchange(totals, [scan.up_send(level) for scan in scans])
        for k, scan in enumerate(scans):
            lowers[k].append(got[k])
            if level < level_count - 1:
                totals[k] = scan.up_combine(level, totals[k], got[k])
    prefixes = [jnp.zeros_like(total) for total in pair_totals]
    for level in reversed(range(level_count)):
        if level < level_count - 1:
            sends = [scan.down_send(level, p, t) for scan, p, t in zip(scans, prefixes, pair_totals)]
            got = exchange([s[0] for s in sends], [s[1] for s in sends])
        else:
            got = [None] * len(scans)
        prefixes = [
            scan.down_combine(level, p, g, low) for scan, p, g, low in zip(scans, prefixes, got, lowers)
        ]
    anchor = lowers[0][0] if level_count else pair_totals[0]
    return prefixes, anchor


def shift_scans(scans, pair_totals):
    group_count = scans[0].pair_count // 2
    got = exchange(list(pair_totals), [scan.up_send(0) for scan in scans])
    lowers = [[g] for g in got]
    through = [scan.up_combine(0, t, g) for scan, t, g in zip(scans, pair_totals, got)]
    before = [jnp.zeros_like(t) for t in pair_totals]

    def group_gain(scan, group):
        return scan.way.gain(-1, 4 * group, 4)

    span = 1
    while span < group_count:
        pairs = [(2 * g + 1, 2 * (g + span) + 1) for g in range(group_count - span)]
        got = exchange(through, [scan.device_pairs(pairs, False) for scan in scans])
        for k, scan in enumerate(scans):
            group = scan.way.pair // 2
            before_gain = 1.0
            for back in range(1, span):
                before_gain = before_gain * group_gain(scan, group - back)
            if span < group_count // 2:
                through[k] = before_gain * group_gain(scan, group) * got[k] + through[k]
            before[k] = before_gain * got[k] + before[k]
        span *= 2
    sends = [scan.down_send(0, p, t) for scan, p, t in zip(scans, before, pair_totals)]
    got = exchange([s[0] for s in sends], [s[1] for s in sends])
    prefixes = [scan.down_combine(0, p, g, low) for scan, p, g, low in zip(scans, before, got, lowers)]
    return prefixes, lowers[0][0]


def carried_pair(tables, fwd_state, adj_state, position, count, head_width):
    ways = [Direction(tables, position, count, reverse, head_width) for reverse in (False, True)]
    states = [fwd_state, adj_state]
    sent = jnp.concatenate([take_half(s, ~w.upper) for s, w in zip(states, ways)], -1)
    got = lax.ppermute(sent, "ctx", [(i, i ^ 1) for i in range(count)])
    got = [got[..., : got.shape[-1] // 2], got[..., got.shape[-1] // 2 :]]
    lows = []
    totals = []
    extend_totals(tables, count, 0, 1)
    for way, state, other in zip(ways, states, got):
        own = take_half(state, way.upper)
        low_block = jnp.where(way.upper, other, own)
        high_block = jnp.where(way.upper, own, other)
        lows.append((way.upper, other, state))
        totals.append(way.gain(1, 2 * way.pair + 1, 1) * low_block + high_block)
    tables[-1], _ = lax.optimization_barrier((tables[-1], totals))
    extend_totals(tables, count, 1, count.bit_length())
    pair_prefixes, anchor = pair_scans(ways, totals)
    lifted_parts = []
    keep_parts = []
    for way, pair_prefix, (upper, other, state) in zip(ways, pair_prefixes, lows):
        low_block = jnp.where(upper, other, take_half(state, upper))
        lifted = way.gain(1, 2 * way.pair, 1) * pair_prefix + low_block
        lifted_parts.append(jnp.where(way.upper, pair_prefix, lifted))
        keep_parts.append(jnp.where(way.upper, lifted, pair_prefix))
    got = lax.ppermute(jnp.concatenate(lifted_parts, -1), "ctx", [(i, i ^ 1) for i in range(count)])
    unit = jnp.exp(jnp.min(tables[-1]) * 0.0)
    got = got * unit
    half = got.shape[-1] // 2
    others = [got[..., :half], got[..., half:]]
    return (keep_parts, others, [way.upper for way in ways]), anchor, tables[-1]


def block_carried_grads(write_map, value_scale, decayed_vals, decayed_cot, carried, local_grads):
    local_values, local_write, local_read = local_grads
    (state_mine, adjoint_mine), (state_other, adjoint_other), (state_upper, adjoint_upper) = carried

    def rows_times(coeffs, mine, other, upper):
        return jnp.einsum(
            "iq,nq->in", take_half(coeffs, upper), mine.astype(jnp.bfloat16), preferred_element_type=jnp.float32
        ) + jnp.einsum(
            "iq,nq->in", take_half(coeffs, ~upper), other.astype(jnp.bfloat16), preferred_element_type=jnp.float32
        )

    grad_read = local_read + rows_times(decayed_cot, state_mine, state_other, state_upper)
    grad_write = local_write + rows_times(decayed_vals, adjoint_mine, adjoint_other, adjoint_upper)
    term_mine = jnp.einsum(
        "jn,nq->jq", write_map, adjoint_mine.astype(jnp.bfloat16), preferred_element_type=jnp.float32
    )
    term_other = jnp.einsum(
        "jn,nq->jq", write_map, adjoint_other.astype(jnp.bfloat16), preferred_element_type=jnp.float32
    )
    carried_term = join_halves(term_mine, term_other, adjoint_upper)
    grad_values = local_values + value_scale * carried_term
    return (
        grad_values.astype(jnp.bfloat16),
        grad_write.astype(jnp.bfloat16),
        grad_read.astype(jnp.bfloat16),
    )


def local(token_values, cotangent, write_coeffs, read_coeffs, decay_codes, skip_gain):
    seq_len = token_values.shape[1] * lax.axis_size("ctx")
    factor = 0.25 / seq_len
    prepare = jax.vmap(functools.partial(block_states, factor=factor))
    within, totals, value_scale, decayed_vals, decayed_cot, fwd_state, adj_state, skip_parts = prepare(
        token_values, cotangent, write_coeffs, read_coeffs, decay_codes
    )
    position = lax.axis_index("ctx")
    count = lax.axis_size("ctx")
    tables = jax.vmap(gather_totals, (0, 0, None, None))(totals, skip_parts, position, count)
    head_width = token_values.shape[2] // decay_codes.shape[2]
    carried, anchor, final_table = jax.vmap(carried_pair, (0, 0, 0, None, None, None))(
        tables, fwd_state, adj_state, position, count, head_width
    )
    grad_skip = jnp.sum(final_table[:, count], axis=0)
    for bit in range(lax.axis_size("dp").bit_length() - 1):
        grad_skip = grad_skip + lax.ppermute(grad_skip, "dp", xor_pairs(lax.axis_size("dp"), bit))
    local_inputs, _ = lax.optimization_barrier(
        ((token_values, cotangent, write_coeffs, read_coeffs, within), anchor)
    )
    local_grads = jax.vmap(block_local_grads, (0, 0, 0, 0, 0, None))(*local_inputs, skip_gain)
    grad_values, grad_write, grad_read = jax.vmap(block_carried_grads)(
        write_coeffs, value_scale, decayed_vals, decayed_cot, carried, local_grads
    )
    return (grad_values, grad_write, grad_read, grad_skip)


def solution(mesh):
    in_specs = (
        P("dp", "ctx", None),
        P("dp", "ctx", None),
        P("dp", "ctx", None),
        P("dp", "ctx", None),
        P("dp", "ctx", None),
        P(),
    )
    out_specs = (P("dp", "ctx", None), P("dp", "ctx", None), P("dp", "ctx", None), P())
    return jax.shard_map(local, mesh=mesh, in_specs=in_specs, out_specs=out_specs, check_vma=False)
```

```python
import functools

import jax
import jax.numpy as jnp
from jax import lax
from jax.sharding import PartitionSpec as P


def spread_heads(per_head, width):
    return jnp.repeat(per_head, width, axis=-1)


def block_states(values, cotan, write_map, read_map, codes, factor):
    head_count = codes.shape[1]
    head_width = values.shape[1] // head_count
    log_decay = -codes.astype(jnp.float32) * factor
    within = jnp.cumsum(log_decay, axis=0)
    totals = within[-1]
    value_scale = spread_heads(jnp.exp(totals - within), head_width)
    cot_scale = spread_heads(jnp.exp(within), head_width)
    decayed_vals = (values.astype(jnp.float32) * value_scale).astype(jnp.bfloat16)
    decayed_cot = (cotan.astype(jnp.float32) * cot_scale).astype(jnp.bfloat16)
    fwd_state = jnp.einsum("jn,jq->nq", write_map, decayed_vals, preferred_element_type=jnp.float32)
    adj_state = jnp.einsum("in,iq->nq", read_map, decayed_cot, preferred_element_type=jnp.float32)
    skip_part = jnp.sum(
        (values.astype(jnp.float32) * cotan.astype(jnp.float32)).reshape(
            values.shape[0], head_count, head_width
        ),
        axis=(0, 2),
    )
    return within, totals, value_scale, decayed_vals, decayed_cot, fwd_state, adj_state, skip_part


def block_local_grads(values, cotan, write_map, read_map, within, skip_gain):
    token_count = values.shape[0]
    head_count = skip_gain.shape[0]
    head_width = values.shape[1] // head_count
    vals_three = values.reshape(token_count, head_count, head_width)
    cot_three = cotan.reshape(token_count, head_count, head_width)
    rows = jnp.arange(token_count)
    causal = (rows[:, None] >= rows[None, :])[None]
    lead = within.T
    spread = lead[:, :, None] - lead[:, None, :]
    decay_matrix = jnp.where(causal, jnp.exp(jnp.where(causal, spread, 0.0)), 0.0)
    products = jnp.einsum("ihp,jhp->hij", cot_three, vals_three, preferred_element_type=jnp.float32)
    read_weights = (products * decay_matrix).astype(jnp.bfloat16)
    gram = jnp.einsum("in,jn->ij", read_map, write_map, preferred_element_type=jnp.float32)
    value_weights = (gram[None] * decay_matrix).astype(jnp.bfloat16)
    grad_read = jnp.einsum("hij,jn->in", read_weights, write_map, preferred_element_type=jnp.float32)
    grad_write = jnp.einsum("hij,in->jn", read_weights, read_map, preferred_element_type=jnp.float32)
    grad_values = jnp.einsum(
        "hij,ihp->jhp", value_weights, cot_three, preferred_element_type=jnp.float32
    ) + skip_gain[None, :, None] * cot_three.astype(jnp.float32)
    return grad_values.reshape(token_count, head_count * head_width), grad_write, grad_read


def xor_pairs(count, bit):
    return [(i, i ^ (1 << bit)) for i in range(count)]


def gather_totals(totals, skip_part, position, count):
    rows = jnp.arange(count)[:, None]
    table = jnp.concatenate([jnp.where(rows == position, totals[None, :], 0.0), skip_part[None, :]], 0)
    return [table]


def extend_totals(tables, count, start_bit, stop_bit):
    for bit in range(start_bit, min(stop_bit, count.bit_length() - 1)):
        tables.append(tables[-1] + lax.ppermute(tables[-1], "ctx", xor_pairs(count, bit)))


def take_half(array, upper):
    half = array.shape[-1] // 2
    return lax.dynamic_slice_in_dim(array, upper.astype(jnp.int32) * half, half, axis=array.ndim - 1)


def join_halves(mine, other, upper):
    return jnp.where(upper, jnp.concatenate([other, mine], -1), jnp.concatenate([mine, other], -1))


class Direction:
    def __init__(self, tables, position, count, reverse, head_width):
        self.tables = tables
        self.count = count
        self.reverse = reverse
        self.head_width = head_width
        self.index = count - 1 - position if reverse else position
        self.upper = self.index % 2 == 1
        self.pair = self.index // 2
        self.pyramids = {}

    def actual(self, pairs):
        if self.reverse:
            return [(self.count - 1 - a, self.count - 1 - b) for a, b in pairs]
        return pairs

    def pair_pairs(self, pairs):
        return self.actual([(2 * a + j, 2 * b + j) for a, b in pairs for j in (0, 1)])

    def gain(self, table_index, low_block, size):
        key = (table_index % len(self.tables), size)
        if key not in self.pyramids:
            rows = self.tables[key[0]][: self.count]
            if self.reverse:
                rows = rows[::-1]
            grouped = rows.reshape(self.count // size, size, rows.shape[-1]).sum(axis=1)
            self.pyramids[key] = jnp.exp(grouped)
        full = lax.dynamic_index_in_dim(self.pyramids[key], low_block // size, keepdims=False)
        return spread_heads(take_half(full, self.upper), self.head_width)[..., None, :]


def exchange(payloads, pair_lists):
    return [
        lax.ppermute(p, "ctx", pairs) if pairs else jnp.zeros_like(p) for p, pairs in zip(payloads, pair_lists)
    ]


class PairScan:
    def __init__(self, way):
        self.way = way
        self.pair_count = way.count // 2
        self.level_count = self.pair_count.bit_length() - 1
        self.flip = self.level_count >= 2
        pair = way.pair
        self.role = jnp.where(way.upper, pair ^ 1, pair) if self.flip else pair

    def device_pairs(self, pairs, first_level):
        lower = [(2 * a, 2 * b) for a, b in pairs]
        if self.flip and first_level:
            upper = [(2 * b + 1, 2 * a + 1) for a, b in pairs]
        elif self.flip:
            upper = [(2 * (a ^ 1) + 1, 2 * (b ^ 1) + 1) for a, b in pairs]
        else:
            upper = [(2 * a + 1, 2 * b + 1) for a, b in pairs]
        return self.way.actual(lower + upper)

    def pair_gain(self, level, low_pair, pair_span):
        table = min(level + 2, len(self.way.tables) - 1)
        return self.way.gain(table, 2 * low_pair, 2 * pair_span)

    def up_send(self, level):
        span = 1 << level
        pairs = [(a, a + span) for a in range(self.pair_count) if a % (2 * span) == span - 1]
        return self.device_pairs(pairs, level == 0)

    def up_combine(self, level, total, lower):
        span = 1 << level
        if self.flip and level == 0:
            pair = self.way.pair
            kept_upper = self.pair_gain(0, pair ^ 1, 1) * total + lower
            kept_lower = self.pair_gain(0, pair, 1) * lower + total
            return jnp.where(self.way.upper, kept_upper, kept_lower)
        return self.pair_gain(level, self.role - span + 1, span) * lower + total

    def down_send(self, level, prefix, pair_total):
        span = 1 << level
        if self.flip and level == 0:
            pair = self.way.pair
            sent = jnp.where(self.way.upper, self.pair_gain(0, pair, 1) * prefix + pair_total, prefix)
            pairs = [(2 * (a + 1), 2 * a) for a in range(2, self.pair_count, 2)]
            pairs += [(2 * a + 1, 2 * (a + 1) + 1) for a in range(0, self.pair_count, 2)]
            return sent, self.way.actual(pairs)
        pairs = [(a, a - span) for a in range(2 * span, self.pair_count) if a % (2 * span) == 2 * span - 1]
        return prefix, self.device_pairs(pairs, False)

    def down_combine(self, level, prefix, got, lowers):
        span = 1 << level
        if self.flip and level == 0:
            pair = self.way.pair
            grown = self.pair_gain(self.level_count, pair - 1, 1) * prefix + lowers[0]
            odd = pair % 2 == 1
            return jnp.where(self.way.upper, jnp.where(odd, got, prefix), jnp.where(odd, grown, got))
        if got is not None:
            prefix = prefix + got
        lower_gain = self.pair_gain(self.level_count, self.role - 2 * span + 1, span)
        lower_gain = jnp.where(self.role % (2 * span) == 2 * span - 1, lower_gain, 1.0)
        return lower_gain * prefix + lowers[level]


def pair_scans(ways, pair_totals):
    scans = [PairScan(way) for way in ways]
    level_count = scans[0].level_count
    if scans[0].flip:
        return shift_scans(scans, pair_totals)
    totals = list(pair_totals)
    lowers = [[] for _ in scans]
    for level in range(level_count):
        got = exchange(totals, [scan.up_send(level) for scan in scans])
        for k, scan in enumerate(scans):
            lowers[k].append(got[k])
            if level < level_count - 1:
                totals[k] = scan.up_combine(level, totals[k], got[k])
    prefixes = [jnp.zeros_like(total) for total in pair_totals]
    for level in reversed(range(level_count)):
        if level < level_count - 1:
            sends = [scan.down_send(level, p, t) for scan, p, t in zip(scans, prefixes, pair_totals)]
            got = exchange([s[0] for s in sends], [s[1] for s in sends])
        else:
            got = [None] * len(scans)
        prefixes = [
            scan.down_combine(level, p, g, low) for scan, p, g, low in zip(scans, prefixes, got, lowers)
        ]
    anchor = lowers[0][0] if level_count else pair_totals[0]
    return prefixes, anchor


def shift_scans(scans, pair_totals):
    group_count = scans[0].pair_count // 2
    got = exchange(list(pair_totals), [scan.up_send(0) for scan in scans])
    lowers = [[g] for g in got]
    through = [scan.up_combine(0, t, g) for scan, t, g in zip(scans, pair_totals, got)]
    before = [jnp.zeros_like(t) for t in pair_totals]

    def group_gain(scan, group):
        return scan.way.gain(-1, 4 * group, 4)

    span = 1
    while span < group_count:
        pairs = [(2 * g + 1, 2 * (g + span) + 1) for g in range(group_count - span)]
        got = exchange(through, [scan.device_pairs(pairs, False) for scan in scans])
        for k, scan in enumerate(scans):
            group = scan.way.pair // 2
            before_gain = 1.0
            for back in range(1, span):
                before_gain = before_gain * group_gain(scan, group - back)
            if span < group_count // 2:
                through[k] = before_gain * group_gain(scan, group) * got[k] + through[k]
            before[k] = before_gain * got[k] + before[k]
        span *= 2
    sends = [scan.down_send(0, p, t) for scan, p, t in zip(scans, before, pair_totals)]
    got = exchange([s[0] for s in sends], [s[1] for s in sends])
    prefixes = [scan.down_combine(0, p, g, low) for scan, p, g, low in zip(scans, before, got, lowers)]
    return prefixes, lowers[0][0]


def carried_pair(tables, fwd_state, adj_state, position, count, head_width):
    ways = [Direction(tables, position, count, reverse, head_width) for reverse in (False, True)]
    states = [fwd_state, adj_state]
    sent = jnp.concatenate([take_half(s, ~w.upper) for s, w in zip(states, ways)], -1)
    got = lax.ppermute(sent, "ctx", [(i, i ^ 1) for i in range(count)])
    got = [got[..., : got.shape[-1] // 2], got[..., got.shape[-1] // 2 :]]
    lows = []
    totals = []
    extend_totals(tables, count, 0, 1)
    for way, state, other in zip(ways, states, got):
        own = take_half(state, way.upper)
        low_block = jnp.where(way.upper, other, own)
        high_block = jnp.where(way.upper, own, other)
        lows.append((way.upper, other, state))
        totals.append(way.gain(1, 2 * way.pair + 1, 1) * low_block + high_block)
    tables[-1], _ = lax.optimization_barrier((tables[-1], totals))
    extend_totals(tables, count, 1, count.bit_length())
    pair_prefixes, anchor = pair_scans(ways, totals)
    lifted_parts = []
    keep_parts = []
    for way, pair_prefix, (upper, other, state) in zip(ways, pair_prefixes, lows):
        low_block = jnp.where(upper, other, take_half(state, upper))
        lifted = way.gain(1, 2 * way.pair, 1) * pair_prefix + low_block
        lifted_parts.append(jnp.where(way.upper, pair_prefix, lifted))
        keep_parts.append(jnp.where(way.upper, lifted, pair_prefix))
    got = lax.ppermute(jnp.concatenate(lifted_parts, -1), "ctx", [(i, i ^ 1) for i in range(count)])
    unit = jnp.exp(jnp.min(tables[-1]) * 0.0)
    got = got * unit
    half = got.shape[-1] // 2
    others = [got[..., :half], got[..., half:]]
    return (keep_parts, others, [way.upper for way in ways]), anchor, tables[-1]


def block_carried_grads(write_map, value_scale, decayed_vals, decayed_cot, carried, local_grads):
    local_values, local_write, local_read = local_grads
    (state_mine, adjoint_mine), (state_other, adjoint_other), (state_upper, adjoint_upper) = carried

    def rows_times(coeffs, mine, other, upper):
        return jnp.einsum(
            "iq,nq->in", take_half(coeffs, upper), mine.astype(jnp.bfloat16), preferred_element_type=jnp.float32
        ) + jnp.einsum(
            "iq,nq->in", take_half(coeffs, ~upper), other.astype(jnp.bfloat16), preferred_element_type=jnp.float32
        )

    grad_read = local_read + rows_times(decayed_cot, state_mine, state_other, state_upper)
    grad_write = local_write + rows_times(decayed_vals, adjoint_mine, adjoint_other, adjoint_upper)
    term_mine = jnp.einsum(
        "jn,nq->jq", write_map, adjoint_mine.astype(jnp.bfloat16), preferred_element_type=jnp.float32
    )
    term_other = jnp.einsum(
        "jn,nq->jq", write_map, adjoint_other.astype(jnp.bfloat16), preferred_element_type=jnp.float32
    )
    carried_term = join_halves(term_mine, term_other, adjoint_upper)
    grad_values = local_values + value_scale * carried_term
    return (
        grad_values.astype(jnp.bfloat16),
        grad_write.astype(jnp.bfloat16),
        grad_read.astype(jnp.bfloat16),
    )


def local(token_values, cotangent, write_coeffs, read_coeffs, decay_codes, skip_gain):
    seq_len = token_values.shape[1] * lax.axis_size("ctx")
    factor = 0.25 / seq_len
    prepare = jax.vmap(functools.partial(block_states, factor=factor))
    within, totals, value_scale, decayed_vals, decayed_cot, fwd_state, adj_state, skip_parts = prepare(
        token_values, cotangent, write_coeffs, read_coeffs, decay_codes
    )
    position = lax.axis_index("ctx")
    count = lax.axis_size("ctx")
    tables = jax.vmap(gather_totals, (0, 0, None, None))(totals, skip_parts, position, count)
    head_width = token_values.shape[2] // decay_codes.shape[2]
    carried, anchor, final_table = jax.vmap(carried_pair, (0, 0, 0, None, None, None))(
        tables, fwd_state, adj_state, position, count, head_width
    )
    grad_skip = jnp.sum(final_table[:, count], axis=0)
    for bit in range(lax.axis_size("dp").bit_length() - 1):
        grad_skip = grad_skip + lax.ppermute(grad_skip, "dp", xor_pairs(lax.axis_size("dp"), bit))
    local_inputs, _ = lax.optimization_barrier(
        ((token_values, cotangent, write_coeffs, read_coeffs, within), anchor)
    )
    local_grads = jax.vmap(block_local_grads, (0, 0, 0, 0, 0, None))(*local_inputs, skip_gain)
    grad_values, grad_write, grad_read = jax.vmap(block_carried_grads)(
        write_coeffs, value_scale, decayed_vals, decayed_cot, carried, local_grads
    )
    return (grad_values, grad_write, grad_read, grad_skip)


def solution(mesh):
    in_specs = (
        P("dp", "ctx", None),
        P("dp", "ctx", None),
        P("dp", "ctx", None),
        P("dp", "ctx", None),
        P("dp", "ctx", None),
        P(),
    )
    out_specs = (P("dp", "ctx", None), P("dp", "ctx", None), P("dp", "ctx", None), P())
    return jax.shard_map(local, mesh=mesh, in_specs=in_specs, out_specs=out_specs, check_vma=False)
```

```python
import functools

import jax
import jax.numpy as jnp
from jax import lax
from jax.sharding import PartitionSpec as P


def spread_heads(per_head, width):
    return jnp.repeat(per_head, width, axis=-1)


def block_states(values, cotan, write_map, read_map, codes, factor):
    head_count = codes.shape[1]
    head_width = values.shape[1] // head_count
    log_decay = -codes.astype(jnp.float32) * factor
    within = jnp.cumsum(log_decay, axis=0)
    totals = within[-1]
    value_scale = spread_heads(jnp.exp(totals - within), head_width)
    cot_scale = spread_heads(jnp.exp(within), head_width)
    decayed_vals = (values.astype(jnp.float32) * value_scale).astype(jnp.bfloat16)
    decayed_cot = (cotan.astype(jnp.float32) * cot_scale).astype(jnp.bfloat16)
    fwd_state = jnp.einsum("jn,jq->nq", write_map, decayed_vals, preferred_element_type=jnp.float32)
    adj_state = jnp.einsum("in,iq->nq", read_map, decayed_cot, preferred_element_type=jnp.float32)
    skip_part = jnp.sum(
        (values.astype(jnp.float32) * cotan.astype(jnp.float32)).reshape(
            values.shape[0], head_count, head_width
        ),
        axis=(0, 2),
    )
    return within, totals, value_scale, decayed_vals, decayed_cot, fwd_state, adj_state, skip_part


def block_local_grads(values, cotan, write_map, read_map, within, skip_gain):
    token_count = values.shape[0]
    head_count = skip_gain.shape[0]
    head_width = values.shape[1] // head_count
    vals_three = values.reshape(token_count, head_count, head_width)
    cot_three = cotan.reshape(token_count, head_count, head_width)
    rows = jnp.arange(token_count)
    causal = (rows[:, None] >= rows[None, :])[None]
    lead = within.T
    spread = lead[:, :, None] - lead[:, None, :]
    decay_matrix = jnp.where(causal, jnp.exp(jnp.where(causal, spread, 0.0)), 0.0)
    products = jnp.einsum("ihp,jhp->hij", cot_three, vals_three, preferred_element_type=jnp.float32)
    read_weights = (products * decay_matrix).astype(jnp.bfloat16)
    gram = jnp.einsum("in,jn->ij", read_map, write_map, preferred_element_type=jnp.float32)
    value_weights = (gram[None] * decay_matrix).astype(jnp.bfloat16)
    grad_read = jnp.einsum("hij,jn->in", read_weights, write_map, preferred_element_type=jnp.float32)
    grad_write = jnp.einsum("hij,in->jn", read_weights, read_map, preferred_element_type=jnp.float32)
    grad_values = jnp.einsum(
        "hij,ihp->jhp", value_weights, cot_three, preferred_element_type=jnp.float32
    ) + skip_gain[None, :, None] * cot_three.astype(jnp.float32)
    return grad_values.reshape(token_count, head_count * head_width), grad_write, grad_read


def xor_pairs(count, bit):
    return [(i, i ^ (1 << bit)) for i in range(count)]


def gather_totals(totals, skip_part, position, count):
    rows = jnp.arange(count)[:, None]
    table = jnp.concatenate([jnp.where(rows == position, totals[None, :], 0.0), skip_part[None, :]], 0)
    return [table]


def extend_totals(tables, count, start_bit, stop_bit):
    for bit in range(start_bit, min(stop_bit, count.bit_length() - 1)):
        tables.append(tables[-1] + lax.ppermute(tables[-1], "ctx", xor_pairs(count, bit)))


def take_half(array, upper):
    half = array.shape[-1] // 2
    return jnp.where(upper, array[..., half:], array[..., :half])


def join_halves(mine, other, upper):
    return jnp.where(upper, jnp.concatenate([other, mine], -1), jnp.concatenate([mine, other], -1))


class Direction:
    def __init__(self, tables, position, count, reverse, head_width):
        self.tables = tables
        self.count = count
        self.reverse = reverse
        self.head_width = head_width
        self.index = count - 1 - position if reverse else position
        self.upper = self.index % 2 == 1
        self.pair = self.index // 2
        self.pyramids = {}

    def actual(self, pairs):
        if self.reverse:
            return [(self.count - 1 - a, self.count - 1 - b) for a, b in pairs]
        return pairs

    def pair_pairs(self, pairs):
        return self.actual([(2 * a + j, 2 * b + j) for a, b in pairs for j in (0, 1)])

    def gain(self, table_index, low_block, size):
        key = (table_index % len(self.tables), size)
        if key not in self.pyramids:
            rows = self.tables[key[0]][: self.count]
            if self.reverse:
                rows = rows[::-1]
            grouped = rows.reshape(self.count // size, size, rows.shape[-1]).sum(axis=1)
            self.pyramids[key] = jnp.exp(grouped)
        full = lax.dynamic_index_in_dim(self.pyramids[key], low_block // size, keepdims=False)
        return spread_heads(take_half(full, self.upper), self.head_width)[..., None, :]


def exchange(payloads, pair_lists):
    return [
        lax.ppermute(p, "ctx", pairs) if pairs else jnp.zeros_like(p) for p, pairs in zip(payloads, pair_lists)
    ]


class PairScan:
    def __init__(self, way):
        self.way = way
        self.pair_count = way.count // 2
        self.level_count = self.pair_count.bit_length() - 1
        self.flip = self.level_count >= 2
        pair = way.pair
        self.role = jnp.where(way.upper, pair ^ 1, pair) if self.flip else pair

    def device_pairs(self, pairs, first_level):
        lower = [(2 * a, 2 * b) for a, b in pairs]
        if self.flip and first_level:
            upper = [(2 * b + 1, 2 * a + 1) for a, b in pairs]
        elif self.flip:
            upper = [(2 * (a ^ 1) + 1, 2 * (b ^ 1) + 1) for a, b in pairs]
        else:
            upper = [(2 * a + 1, 2 * b + 1) for a, b in pairs]
        return self.way.actual(lower + upper)

    def pair_gain(self, level, low_pair, pair_span):
        table = min(level + 2, len(self.way.tables) - 1)
        return self.way.gain(table, 2 * low_pair, 2 * pair_span)

    def up_send(self, level):
        span = 1 << level
        pairs = [(a, a + span) for a in range(self.pair_count) if a % (2 * span) == span - 1]
        return self.device_pairs(pairs, level == 0)

    def up_combine(self, level, total, lower):
        span = 1 << level
        if self.flip and level == 0:
            pair = self.way.pair
            kept_upper = self.pair_gain(0, pair ^ 1, 1) * total + lower
            kept_lower = self.pair_gain(0, pair, 1) * lower + total
            return jnp.where(self.way.upper, kept_upper, kept_lower)
        return self.pair_gain(level, self.role - span + 1, span) * lower + total

    def down_send(self, level, prefix, pair_total):
        span = 1 << level
        if self.flip and level == 0:
            pair = self.way.pair
            sent = jnp.where(self.way.upper, self.pair_gain(0, pair, 1) * prefix + pair_total, prefix)
            pairs = [(2 * (a + 1), 2 * a) for a in range(2, self.pair_count, 2)]
            pairs += [(2 * a + 1, 2 * (a + 1) + 1) for a in range(0, self.pair_count, 2)]
            return sent, self.way.actual(pairs)
        pairs = [(a, a - span) for a in range(2 * span, self.pair_count) if a % (2 * span) == 2 * span - 1]
        return prefix, self.device_pairs(pairs, False)

    def down_combine(self, level, prefix, got, lowers):
        span = 1 << level
        if self.flip and level == 0:
            pair = self.way.pair
            grown = self.pair_gain(self.level_count, pair - 1, 1) * prefix + lowers[0]
            odd = pair % 2 == 1
            return jnp.where(self.way.upper, jnp.where(odd, got, prefix), jnp.where(odd, grown, got))
        if got is not None:
            prefix = prefix + got
        lower_gain = self.pair_gain(self.level_count, self.role - 2 * span + 1, span)
        lower_gain = jnp.where(self.role % (2 * span) == 2 * span - 1, lower_gain, 1.0)
        return lower_gain * prefix + lowers[level]


def pair_scans(ways, pair_totals):
    scans = [PairScan(way) for way in ways]
    level_count = scans[0].level_count
    if scans[0].flip:
        return shift_scans(scans, pair_totals)
    totals = list(pair_totals)
    lowers = [[] for _ in scans]
    for level in range(level_count):
        got = exchange(totals, [scan.up_send(level) for scan in scans])
        for k, scan in enumerate(scans):
            lowers[k].append(got[k])
            if level < level_count - 1:
                totals[k] = scan.up_combine(level, totals[k], got[k])
    prefixes = [jnp.zeros_like(total) for total in pair_totals]
    for level in reversed(range(level_count)):
        if level < level_count - 1:
            sends = [scan.down_send(level, p, t) for scan, p, t in zip(scans, prefixes, pair_totals)]
            got = exchange([s[0] for s in sends], [s[1] for s in sends])
        else:
            got = [None] * len(scans)
        prefixes = [
            scan.down_combine(level, p, g, low) for scan, p, g, low in zip(scans, prefixes, got, lowers)
        ]
    anchor = lowers[0][0] if level_count else pair_totals[0]
    return prefixes, anchor


def shift_scans(scans, pair_totals):
    group_count = scans[0].pair_count // 2
    got = exchange(list(pair_totals), [scan.up_send(0) for scan in scans])
    lowers = [[g] for g in got]
    through = [scan.up_combine(0, t, g) for scan, t, g in zip(scans, pair_totals, got)]
    before = [jnp.zeros_like(t) for t in pair_totals]

    def group_gain(scan, group, table=-1):
        return scan.way.gain(table, 4 * group, 4)

    span = 1
    while span < group_count:
        pairs = [(2 * g + 1, 2 * (g + span) + 1) for g in range(group_count - span)]
        got = exchange(through, [scan.device_pairs(pairs, False) for scan in scans])
        for k, scan in enumerate(scans):
            group = scan.way.pair // 2
            before_gain = 1.0
            for back in range(1, span):
                before_gain = before_gain * group_gain(scan, group - back)
            if span < group_count // 2:
                own_table = min(2, len(scan.way.tables) - 1) if span == 1 else -1
                through[k] = before_gain * group_gain(scan, group, own_table) * got[k] + through[k]
            before[k] = before_gain * got[k] + before[k]
        span *= 2
    sends = [scan.down_send(0, p, t) for scan, p, t in zip(scans, before, pair_totals)]
    got = exchange([s[0] for s in sends], [s[1] for s in sends])
    prefixes = [scan.down_combine(0, p, g, low) for scan, p, g, low in zip(scans, before, got, lowers)]
    return prefixes, lowers[0][0]


def carried_pair(tables, fwd_state, adj_state, position, count, head_width):
    ways = [Direction(tables, position, count, reverse, head_width) for reverse in (False, True)]
    states = [fwd_state, adj_state]
    sent = jnp.concatenate([take_half(s, ~w.upper) for s, w in zip(states, ways)], -1)
    got = lax.ppermute(sent, "ctx", [(i, i ^ 1) for i in range(count)])
    got = [got[..., : got.shape[-1] // 2], got[..., got.shape[-1] // 2 :]]
    lows = []
    totals = []
    extend_totals(tables, count, 0, 1)
    for way, state, other in zip(ways, states, got):
        own = take_half(state, way.upper)
        low_block = jnp.where(way.upper, other, own)
        high_block = jnp.where(way.upper, own, other)
        lows.append((way.upper, other, state))
        totals.append(way.gain(1, 2 * way.pair + 1, 1) * low_block + high_block)
    tables[-1], _ = lax.optimization_barrier((tables[-1], totals))
    extend_totals(tables, count, 1, count.bit_length())
    pair_prefixes, anchor = pair_scans(ways, totals)
    lifted_parts = []
    keep_parts = []
    for way, pair_prefix, (upper, other, state) in zip(ways, pair_prefixes, lows):
        low_block = jnp.where(upper, other, take_half(state, upper))
        lifted = way.gain(1, 2 * way.pair, 1) * pair_prefix + low_block
        lifted_parts.append(jnp.where(way.upper, pair_prefix, lifted))
        keep_parts.append(jnp.where(way.upper, lifted, pair_prefix))
    got = lax.ppermute(jnp.concatenate(lifted_parts, -1), "ctx", [(i, i ^ 1) for i in range(count)])
    unit = jnp.exp(jnp.min(tables[-1]) * 0.0)
    got = got * unit
    half = got.shape[-1] // 2
    others = [got[..., :half], got[..., half:]]
    return (keep_parts, others, [way.upper for way in ways]), anchor, tables[-1]


def block_carried_grads(write_map, value_scale, decayed_vals, decayed_cot, carried, local_grads):
    local_values, local_write, local_read = local_grads
    (state_mine, adjoint_mine), (state_other, adjoint_other), (state_upper, adjoint_upper) = carried

    def rows_times(coeffs, mine, other, upper):
        return jnp.einsum(
            "iq,nq->in", take_half(coeffs, upper), mine.astype(jnp.bfloat16), preferred_element_type=jnp.float32
        ) + jnp.einsum(
            "iq,nq->in", take_half(coeffs, ~upper), other.astype(jnp.bfloat16), preferred_element_type=jnp.float32
        )

    grad_read = local_read + rows_times(decayed_cot, state_mine, state_other, state_upper)
    grad_write = local_write + rows_times(decayed_vals, adjoint_mine, adjoint_other, adjoint_upper)
    term_mine = jnp.einsum(
        "jn,nq->jq", write_map, adjoint_mine.astype(jnp.bfloat16), preferred_element_type=jnp.float32
    )
    term_other = jnp.einsum(
        "jn,nq->jq", write_map, adjoint_other.astype(jnp.bfloat16), preferred_element_type=jnp.float32
    )
    carried_term = join_halves(term_mine, term_other, adjoint_upper)
    grad_values = local_values + value_scale * carried_term
    return (
        grad_values.astype(jnp.bfloat16),
        grad_write.astype(jnp.bfloat16),
        grad_read.astype(jnp.bfloat16),
    )


def local(token_values, cotangent, write_coeffs, read_coeffs, decay_codes, skip_gain):
    seq_len = token_values.shape[1] * lax.axis_size("ctx")
    factor = 0.25 / seq_len
    prepare = jax.vmap(functools.partial(block_states, factor=factor))
    within, totals, value_scale, decayed_vals, decayed_cot, fwd_state, adj_state, skip_parts = prepare(
        token_values, cotangent, write_coeffs, read_coeffs, decay_codes
    )
    position = lax.axis_index("ctx")
    count = lax.axis_size("ctx")
    tables = jax.vmap(gather_totals, (0, 0, None, None))(totals, skip_parts, position, count)
    head_width = token_values.shape[2] // decay_codes.shape[2]
    carried, anchor, final_table = jax.vmap(carried_pair, (0, 0, 0, None, None, None))(
        tables, fwd_state, adj_state, position, count, head_width
    )
    grad_skip = jnp.sum(final_table[:, count], axis=0)
    for bit in range(lax.axis_size("dp").bit_length() - 1):
        grad_skip = grad_skip + lax.ppermute(grad_skip, "dp", xor_pairs(lax.axis_size("dp"), bit))
    local_inputs, _ = lax.optimization_barrier(
        ((token_values, cotangent, write_coeffs, read_coeffs, within), anchor)
    )
    local_grads = jax.vmap(block_local_grads, (0, 0, 0, 0, 0, None))(*local_inputs, skip_gain)
    grad_values, grad_write, grad_read = jax.vmap(block_carried_grads)(
        write_coeffs, value_scale, decayed_vals, decayed_cot, carried, local_grads
    )
    return (grad_values, grad_write, grad_read, grad_skip)


def solution(mesh):
    in_specs = (
        P("dp", "ctx", None),
        P("dp", "ctx", None),
        P("dp", "ctx", None),
        P("dp", "ctx", None),
        P("dp", "ctx", None),
        P(),
    )
    out_specs = (P("dp", "ctx", None), P("dp", "ctx", None), P("dp", "ctx", None), P())
    return jax.shard_map(local, mesh=mesh, in_specs=in_specs, out_specs=out_specs, check_vma=False)
```
